32 devices in a mesh: ctx: 8 (over z, x), dp: 4 (over y, core).
Axes of the slice: x: 2, y: 2, z: 4, core: 2. Of those that a mesh axis runs over, the one named last changes fastest.
Arguments:
- queries: bfloat16 [4, 2048, 512], P('dp', 'ctx'), may hold values from -3 to 3
- keys: bfloat16 [4, 2048, 512], P('dp', 'ctx'), may hold values from -6 to 6
- values: bfloat16 [4, 2048, 512], P('dp', 'ctx'), may hold values from -6 to 6
- gates: bfloat16 [4, 2048, 512], P('dp', 'ctx'), may hold values from -6 to 6
- out_grad: bfloat16 [4, 2048, 512], P('dp', 'ctx'), may hold values from -6 to 6
- time_bucket: int32 [4, 2048], P('dp'), may hold values from 0 to 127
- lengths: int32 [4, 6], P('dp'), may hold values from 1 to 1024, 2048 in all within a row
- block_map: int32 [4, 16, 16], P('dp'), may hold values 0 or 1
- bucket_bias_matrix: bfloat16 [4, 128, 128], replicated, may hold values from 1 to 3
- w_out: bfloat16 [512, 512], replicated, may hold values from -0.25 to 0.25
Outputs:
- query_grad: bfloat16 [4, 2048, 512], P('dp', 'ctx')
- key_grad: bfloat16 [4, 2048, 512], P('dp', 'ctx')
- value_grad: bfloat16 [4, 2048, 512], P('dp', 'ctx')
- gate_grad: bfloat16 [4, 2048, 512], P('dp', 'ctx')
- w_out_grad: float32 [512, 512], P('dp')
- table_grad: float32 [4, 128, 128], replicated
The draws below stay inside these ranges and needn't reach their ends.
Inputs may be any that keep to these rules, and one draw needn't show every extreme that they name: Each row of lengths sums to 2048, and its largest entry is 1024. `block_map`: 1 marks a visible pair of blocks.
All inputs are finite; a program needn't handle non-finite values.
Results may differ from the reference program's by a relative error of at most 0.0059.
Values may be sent and summed in bfloat16 or wider, within the bound.
No kernel may reach another device: no remote copies, remote signals or barrier semaphores. Data moves between devices by JAX's collectives and lax.ppermute only.
A program may use at most 64 MiB of HBM per device.

```python
import math
import jax
import jax.numpy as jnp
import numpy as np
from jax import lax

D = 512
HEADS = 4
NB = 128
BLK = 128
NSEQ = 6
TOK_DEV = 256
SEQ = 2048
BATCH = 4
NBLK = 16
N_CTX = 8


def plant(drawn, stream_key, smallest, largest):
    longest = drawn.shape.index(max(drawn.shape))
    spots = []
    for shift in (0, 1):
        where = [jax.random.randint(jax.random.fold_in(stream_key, axis), (), 0, length) for axis, length in enumerate(drawn.shape)]
        where[longest] = (where[longest] + shift) % drawn.shape[longest]
        spots.append(tuple(where))
    return drawn.at[spots[0]].set(smallest).at[spots[1]].set(largest)


def block_scale(own_key, shape, shards, smallest, top_value):
    def one(dim, blocks):
        heights = jax.random.uniform(jax.random.fold_in(jax.random.fold_in(own_key, 6), dim), (blocks,), jnp.float32, smallest / len(shards), top_value / len(shards))
        return jnp.repeat(jnp.exp(heights), shape[dim] // blocks).reshape((-1,) + (1,) * (len(shape) - dim - 1))

    loudness = one(*shards[0])
    for cut in shards[1:]:
        loudness = loudness * one(*cut)
    return loudness


def split_up(amount, total, limit, slope):
    portions = [(1 << 20) // math.isqrt(grade ** slope) + 1 for grade in range(2, amount + 1)]
    surplus, counts = total - limit - (amount - 1), [1] * (amount - 1)
    while surplus > 0:
        movable = [i for i in range(amount - 1) if counts[i] < limit]
        whole, remaining = sum([portions[i] for i in movable]), surplus
        for i in movable:
            more = min(limit - counts[i], max(1, remaining * portions[i] // whole), surplus)
            counts[i] = counts[i] + more
            surplus = surplus - more
    return np.array([limit] + counts)


def ragged(rng, count, total, reach, skew):
    if count == 2:
        one = jax.random.randint(rng, (), max(1, total - reach), min(reach, total - 1) + 1)
        return jnp.stack([one, total - one])
    sizes = jnp.asarray(split_up(count, total, reach, skew), jnp.int32)
    twos = (count - 1) // 2
    donor, sink = sizes[1:1 + 2 * twos:2], sizes[2:2 + 2 * twos:2]
    room = jnp.minimum(donor - 1, reach - sink)
    moved = jax.random.randint(jax.random.fold_in(rng, 1), (twos,), 0, 1 << 20) % (room + 1)
    sizes = sizes.at[1:1 + 2 * twos:2].set(donor - moved).at[2:2 + 2 * twos:2].set(sink + moved)
    return sizes[jax.random.permutation(jax.random.fold_in(rng, 2), count)]


def centred(stream_key, dims, deviation, reach, cuts=(), kind=jnp.bfloat16):
    array = jax.random.normal(stream_key, dims, jnp.float32) * deviation
    if len(cuts) > 0:
        array = block_scale(stream_key, dims, cuts, -0.22, 0.18) * array
    return jnp.clip(array, min=-reach, max=reach).astype(kind)


def setup_inputs(seed: int = 0) -> dict:
    arg_keys = jax.random.split(jax.random.key(seed), 11)
    return {
        "queries": centred(arg_keys[0], (BATCH, SEQ, D), 0.5, 3.0, ((0, 4), (1, 8))),
        "keys": centred(arg_keys[1], (BATCH, SEQ, D), 1.0, 6.0, ((0, 4), (1, 8))),
        "values": centred(arg_keys[2], (BATCH, SEQ, D), 1.0, 6.0, ((0, 4), (1, 8))),
        "gates": centred(arg_keys[3], (BATCH, SEQ, D), 1.0, 6.0, ((0, 4), (1, 8))),
        "out_grad": centred(arg_keys[4], (BATCH, SEQ, D), 1.0, 6.0, ((0, 4), (1, 8))),
        "time_bucket": plant(jax.random.randint(arg_keys[5], (BATCH, SEQ), 0, NB), jax.random.fold_in(arg_keys[5], 1), 0, NB - 1).astype(jnp.int32),
        "lengths": jax.vmap(lambda own: ragged(own, NSEQ, SEQ, SEQ // 2, 2))(jax.random.split(arg_keys[6], BATCH)).reshape((BATCH, NSEQ)).astype(jnp.int32),
        "block_map": plant((jax.random.randint(arg_keys[7], (BATCH, NBLK, NBLK), 0, 4) < 3).astype(jnp.int32), jax.random.fold_in(arg_keys[7], 1), 0, 1),
        "bucket_bias_matrix": jnp.clip(jax.random.uniform(arg_keys[8], (HEADS, NB, NB), jnp.float32, 1.0, 3.0), 1.0, 3.0).astype(jnp.bfloat16),
        "w_out": centred(arg_keys[9], (D, D), D ** -0.5, 0.25),
    }


NORM_EPSILON = 1e-05

def silu_slope(scores):
    sigmoid = jax.nn.sigmoid(scores)
    return sigmoid * (1.0 + scores * (1.0 - sigmoid))

def round_trip(values_in):
    return lax.optimization_barrier(values_in.astype(jnp.bfloat16)).astype(jnp.float32)

def reference(queries, keys, values, gates, out_grad, time_bucket, lengths, block_map, bucket_bias_matrix, w_out):
    head_dim = D // HEADS
    scale = head_dim ** (-0.5)
    margin = 2 * TOK_DEV
    window_len = 3 * TOK_DEV
    bucket_ids = jnp.arange(NB, dtype=jnp.int32)
    table_float = bucket_bias_matrix.astype(jnp.float32)
    highest_precision = lax.Precision.HIGHEST

    def one_row(carry, row_data):
        q_row, k_row, v_row, u_row, dy_row, bucket_row, length_row, map_row = row_data
        offsets = jnp.cumsum(length_row, dtype=jnp.int32) - length_row
        positions = jnp.arange(SEQ, dtype=jnp.int32)
        segment = lax.optimization_barrier(jnp.sum((positions[:, None] >= offsets[None, 1:]).astype(jnp.int32), axis=1, dtype=jnp.int32))
        keys_pad = jnp.pad(k_row, ((margin, 0), (0, 0)))
        values_pad = jnp.pad(v_row, ((margin, 0), (0, 0)))
        bucket_pad = jnp.pad(bucket_row, (margin, 0))
        segment_pad = jnp.pad(segment, (margin, 0), constant_values=-1)
        map_pad = jnp.pad(map_row, ((0, 0), (margin // BLK, 0)))

        def one_block(inner, block_index):
            key_acc, value_acc, proj_acc, table_acc = inner
            first = (block_index * TOK_DEV).astype(jnp.int32)
            query_block = lax.dynamic_slice_in_dim(q_row, first, TOK_DEV, 0).astype(jnp.float32)
            gate_block = lax.dynamic_slice_in_dim(u_row, first, TOK_DEV, 0).astype(jnp.float32)
            grad_block = lax.dynamic_slice_in_dim(dy_row, first, TOK_DEV, 0)
            key_block = lax.dynamic_slice_in_dim(keys_pad, first, window_len, 0).astype(jnp.float32)
            value_block = lax.dynamic_slice_in_dim(values_pad, first, window_len, 0).astype(jnp.float32)
            query_pos = first + jnp.arange(TOK_DEV, dtype=jnp.int32)
            key_pos = first - margin + jnp.arange(window_len, dtype=jnp.int32)
            query_seg = lax.dynamic_slice_in_dim(segment, first, TOK_DEV, 0)
            key_seg = lax.dynamic_slice_in_dim(segment_pad, first, window_len, 0)
            query_bucket = lax.dynamic_slice_in_dim(bucket_row, first, TOK_DEV, 0)
            key_bucket = lax.dynamic_slice_in_dim(bucket_pad, first, window_len, 0)
            map_part = lax.dynamic_slice(map_pad, (first // BLK, first // BLK), (TOK_DEV // BLK, window_len // BLK))
            map_full = jnp.repeat(jnp.repeat(map_part, BLK, axis=0), BLK, axis=1)
            same_block = query_pos[:, None] // BLK == key_pos[None, :] // BLK
            visible = (query_seg[:, None] == key_seg[None, :]) & (key_pos[None, :] <= query_pos[:, None]) & (key_pos[None, :] >= 0) & ((map_full == 1) | same_block)
            bias_terms = table_float[:, query_bucket[:, None], key_bucket[None, :]]
            query_heads = query_block.reshape(TOK_DEV, HEADS, head_dim)
            key_heads = key_block.reshape(window_len, HEADS, head_dim)
            value_heads = value_block.reshape(window_len, HEADS, head_dim)
            scores = jnp.einsum('ihd,jhd->hij', query_heads, key_heads) * scale + bias_terms
            weights = round_trip(jnp.where(visible[None], jax.nn.silu(scores), 0.0))
            attended = jnp.einsum('hij,jhd->ihd', weights, value_heads).reshape(TOK_DEV, D)
            centered = attended - lax.optimization_barrier(jnp.mean(attended, axis=1, keepdims=True))
            inverse = lax.rsqrt(lax.optimization_barrier(jnp.mean(centered * centered, axis=1, keepdims=True)) + NORM_EPSILON)
            normed = centered * inverse
            dz_rows = jnp.dot(grad_block, w_out.T, preferred_element_type=jnp.float32)
            mixed = (normed * gate_block).astype(jnp.bfloat16)
            proj_term = jnp.dot(mixed.T, grad_block, preferred_element_type=jnp.float32)
            gate_grad = (dz_rows * normed).astype(jnp.bfloat16)
            lifted = dz_rows * gate_block
            attended_grad = round_trip((lifted - lax.optimization_barrier(jnp.mean(lifted, axis=1, keepdims=True)) - normed * lax.optimization_barrier(jnp.mean(lifted * normed, axis=1, keepdims=True))) * inverse)
            grad_heads = attended_grad.reshape(TOK_DEV, HEADS, head_dim)
            weight_grad = jnp.einsum('ihd,jhd->hij', grad_heads, value_heads)
            value_part = jnp.einsum('hij,ihd->jhd', weights, grad_heads).reshape(window_len, D)
            score_gradient = round_trip(jnp.where(visible[None], weight_grad * silu_slope(scores), 0.0))
            query_grad = (jnp.einsum('hij,jhd->ihd', score_gradient, key_heads).reshape(TOK_DEV, D) * scale).astype(jnp.bfloat16)
            key_part = jnp.einsum('hij,ihd->jhd', score_gradient, query_heads).reshape(window_len, D) * scale
            indicator_query_rows = (query_bucket[:, None] == bucket_ids[None, :]).astype(jnp.float32)
            indicator_key_rows = (key_bucket[:, None] == bucket_ids[None, :]).astype(jnp.float32)
            bucket_share_piece = jnp.einsum('rmw,wx->rmx', score_gradient, indicator_key_rows, precision=highest_precision)
            bias_matrix_term = jnp.einsum('qp,cqk->cpk', indicator_query_rows, bucket_share_piece, precision=highest_precision)
            key_acc = lax.dynamic_update_slice_in_dim(key_acc, lax.dynamic_slice_in_dim(key_acc, first, window_len, 0) + key_part, first, 0)
            value_acc = lax.dynamic_update_slice_in_dim(value_acc, lax.dynamic_slice_in_dim(value_acc, first, window_len, 0) + value_part, first, 0)
            return ((key_acc, value_acc, proj_acc + proj_term, table_acc + bias_matrix_term), (query_grad, gate_grad))
        proj_acc, table_acc = carry
        zeros_pad = jnp.zeros((SEQ + margin, D), jnp.float32)
        inner_out, block_out = lax.scan(one_block, (zeros_pad, zeros_pad, proj_acc, table_acc), jnp.arange(N_CTX, dtype=jnp.int32))
        key_acc, value_acc, proj_acc, table_acc = inner_out
        query_grads, gate_grads = block_out
        key_grad = key_acc[margin:].astype(jnp.bfloat16)
        value_grad = value_acc[margin:].astype(jnp.bfloat16)
        return ((proj_acc, table_acc), (query_grads.reshape(SEQ, D), key_grad, value_grad, gate_grads.reshape(SEQ, D)))
    start_carry = (jnp.zeros((D, D), jnp.float32), jnp.zeros((HEADS, NB, NB), jnp.float32))
    sums, per_row = lax.scan(one_row, start_carry, (queries, keys, values, gates, out_grad, time_bucket, lengths, block_map))
    w_out_grad, table_grad = sums
    query_grad, key_grad, value_grad, gate_grad = per_row
    return (query_grad, key_grad, value_grad, gate_grad, w_out_grad, table_grad)
```

```python
import jax
import jax.numpy as jnp
from jax import lax
from jax.sharding import PartitionSpec as P

BLK = 128


NORM_EPSILON = 1e-05


def passed_along(value, axis, by):
    length = lax.axis_size(axis)
    pairs = [(i, i + by) for i in range(length) if 0 <= i + by < length]
    return lax.ppermute(value, axis, pairs)


def exchanged(value, axis, mask):
    length = lax.axis_size(axis)
    pairs = [(i, i ^ mask) for i in range(length)]
    return lax.ppermute(value, axis, pairs)


def axis_bits(axis):
    length = lax.axis_size(axis)
    bits = []
    mask = 1
    while mask < length:
        bits.append(mask)
        mask *= 2
    return bits


def scatter_blocks(blocks, axis):
    index = lax.axis_index(axis)
    for mask in axis_bits(axis):
        bit = (index // mask) % 2
        pairs = blocks.reshape(blocks.shape[0] // 2, 2, blocks.shape[1])
        keep = lax.dynamic_index_in_dim(pairs, bit, axis=1, keepdims=False)
        send = lax.dynamic_index_in_dim(pairs, 1 - bit, axis=1, keepdims=False)
        blocks = keep + exchanged(send, axis, mask)
    return blocks[0]


def gather_blocks(chunk, axis):
    index = lax.axis_index(axis)
    held = chunk[None]
    for mask in reversed(axis_bits(axis)):
        bit = (index // mask) % 2
        other = exchanged(held, axis, mask)
        low = jnp.where(bit == 0, held, other)
        high = jnp.where(bit == 0, other, held)
        held = jnp.stack([low, high], axis=1).reshape(held.shape[0] * 2, held.shape[1])
    return held


def summed_over(flat, axis):
    size = lax.axis_size(axis)
    part = scatter_blocks(flat.reshape(size, flat.shape[0] // size), axis)
    return gather_blocks(part, axis).reshape(flat.shape)


def silu_slope(scores):
    sigmoid = jax.nn.sigmoid(scores)
    return sigmoid * (1.0 + scores * (1.0 - sigmoid))


def expand_blocks(block_rows, block_size):
    return jnp.repeat(jnp.repeat(block_rows, block_size, axis=0), block_size, axis=1)


def shards(
    queries,
    keys,
    values,
    gates,
    out_grad,
    time_bucket,
    lengths,
    block_map,
    bucket_bias_matrix,
    w_out,
):
    query_rows = queries[0]
    key_rows = keys[0]
    value_rows = values[0]
    gate_rows = gates[0]
    grad_rows = out_grad[0]
    local_rows, width = query_rows.shape
    head_count = bucket_bias_matrix.shape[0]
    bucket_count = bucket_bias_matrix.shape[1]
    head_dim = width // head_count
    scale = head_dim ** (-0.5)
    blocks_here = local_rows // BLK
    cycle_index = lax.axis_index("ctx")
    row_start = cycle_index * local_rows
    offsets = jnp.cumsum(lengths[0], dtype=jnp.int32) - lengths[0]

    def segment_of(positions):
        return jnp.sum(
            (positions[:, None] >= offsets[None, 1:]).astype(jnp.int32), axis=1, dtype=jnp.int32
        )

    bucket_ids = jnp.arange(bucket_count, dtype=jnp.int32)
    query_pos = row_start + jnp.arange(local_rows, dtype=jnp.int32)
    query_seg = segment_of(query_pos)
    query_bucket = lax.dynamic_slice_in_dim(time_bucket[0], row_start, local_rows, 0)
    query_bucket_indicator = (query_bucket[:, None] == bucket_ids[None, :]).astype(jnp.bfloat16)
    bias_matrix_rows = jnp.einsum(
        "lf,sfq->slq",
        query_bucket_indicator,
        bucket_bias_matrix,
        preferred_element_type=jnp.float32,
    ).astype(jnp.bfloat16)
    map_rows = lax.dynamic_slice_in_dim(block_map[0], cycle_index * blocks_here, blocks_here, 0)
    query_heads = query_rows.reshape(local_rows, head_count, head_dim)
    stacked = jnp.stack([key_rows, value_rows])
    window = [stacked, passed_along(stacked, "ctx", 1), passed_along(stacked, "ctx", 2)]
    tiles = []
    attended = jnp.zeros((local_rows, head_count, head_dim), jnp.float32)
    for distance in range(3):
        key_first = row_start - distance * local_rows
        key_pos = key_first + jnp.arange(local_rows, dtype=jnp.int32)
        safe_first = jnp.maximum(key_first, 0)
        key_bucket = lax.dynamic_slice_in_dim(time_bucket[0], safe_first, local_rows, 0)
        key_bucket_indicator = (key_bucket[:, None] == bucket_ids[None, :]).astype(jnp.bfloat16)
        map_cols = lax.dynamic_slice_in_dim(map_rows, safe_first // BLK, blocks_here, 1)
        same_block = query_pos[:, None] // BLK == key_pos[None, :] // BLK
        key_visible = (
            (query_seg[:, None] == segment_of(key_pos)[None, :])
            & (key_pos[None, :] <= query_pos[:, None])
            & (key_pos[None, :] >= 0)
            & ((expand_blocks(map_cols, BLK) == 1) | same_block)
        )
        key_bias_terms = jnp.einsum(
            "vqx,px->vqp",
            bias_matrix_rows,
            key_bucket_indicator,
            preferred_element_type=jnp.float32,
        )
        visible, bias_terms, key_bucket_indicator = (
            key_visible,
            key_bias_terms,
            key_bucket_indicator,
        )
        forward_pair = window[distance]
        forward_key_heads = forward_pair[0].reshape(local_rows, head_count, head_dim)
        forward_value_heads = forward_pair[1].reshape(local_rows, head_count, head_dim)
        forward_scores = (
            jnp.einsum(
                "ihd,jhd->hij", query_heads, forward_key_heads, preferred_element_type=jnp.float32
            )
            * scale
            + bias_terms
        )
        forward_weights = jnp.where(visible[None], jax.nn.silu(forward_scores), 0.0).astype(
            jnp.bfloat16
        )
        attended_part = jnp.einsum(
            "hij,jhd->ihd", forward_weights, forward_value_heads, preferred_element_type=jnp.float32
        )
        attended = attended + attended_part
        tiles.append((visible, forward_scores, forward_weights, key_bucket_indicator))
    attended = attended.reshape(local_rows, width)
    centered = attended - jnp.mean(attended, axis=1, keepdims=True)
    inverse = lax.rsqrt(jnp.mean(centered * centered, axis=1, keepdims=True) + NORM_EPSILON)
    normed = centered * inverse
    dz_rows = lax.dot_general(
        grad_rows, w_out, (((1,), (1,)), ((), ())), preferred_element_type=jnp.float32
    )
    gate_float = gate_rows.astype(jnp.float32)
    gate_grad = (dz_rows * normed).astype(jnp.bfloat16)
    mixed = (normed * gate_float).astype(jnp.bfloat16)
    lifted = dz_rows * gate_float
    attended_grad = (
        (
            lifted
            - jnp.mean(lifted, axis=1, keepdims=True)
            - normed * jnp.mean(lifted * normed, axis=1, keepdims=True)
        )
        * inverse
    ).astype(jnp.bfloat16)
    grad_heads = attended_grad.reshape(local_rows, head_count, head_dim)
    indicator_float = query_bucket_indicator.astype(jnp.float32)
    query_sum = jnp.zeros((local_rows, width), jnp.float32)
    table_local = jnp.zeros((head_count, bucket_count, bucket_count), jnp.float32)
    key_terms = []
    for distance in range(3):
        visible, scores, weights, key_bucket_indicator = tiles[distance]
        pair = window[distance]
        key_heads = pair[0].reshape(local_rows, head_count, head_dim)
        value_heads = pair[1].reshape(local_rows, head_count, head_dim)
        weight_grad = jnp.einsum(
            "ihd,jhd->hij", grad_heads, value_heads, preferred_element_type=jnp.float32
        )
        value_part = jnp.einsum(
            "hij,ihd->jhd", weights, grad_heads, preferred_element_type=jnp.float32
        ).reshape(local_rows, width)
        score_gradient = jnp.where(visible[None], weight_grad * silu_slope(scores), 0.0).astype(
            jnp.bfloat16
        )
        query_part = jnp.einsum(
            "hij,jhd->ihd", score_gradient, key_heads, preferred_element_type=jnp.float32
        ).reshape(local_rows, width)
        key_part = (
            jnp.einsum(
                "hij,ihd->jhd", score_gradient, query_heads, preferred_element_type=jnp.float32
            ).reshape(local_rows, width)
            * scale
        )
        bucket_share_piece = jnp.einsum(
            "rmw,wx->rmx", score_gradient, key_bucket_indicator, preferred_element_type=jnp.float32
        )
        table_part = jnp.einsum(
            "qp,cqk->cpk", indicator_float, bucket_share_piece, precision=lax.Precision.HIGHEST
        )
        query_sum = query_sum + query_part
        table_local = table_local + table_part
        key_terms.append(jnp.stack([key_part, value_part]))
    gathered = (
        key_terms[0] + passed_along(key_terms[1], "ctx", -1) + passed_along(key_terms[2], "ctx", -2)
    )
    query_grad = (query_sum * scale).astype(jnp.bfloat16)
    key_grad = gathered[0].astype(jnp.bfloat16)
    value_grad = gathered[1].astype(jnp.bfloat16)
    dp_size = lax.axis_size("dp")
    weight_term = lax.dot_general(
        mixed, grad_rows, (((0,), (0,)), ((), ())), preferred_element_type=jnp.float32
    )
    weight_rows = scatter_blocks(weight_term.reshape(dp_size, -1), "dp")
    projection_grad = summed_over(weight_rows, "ctx").reshape(width // dp_size, width)
    table_rows = scatter_blocks(table_local.reshape(dp_size, -1), "dp")
    table_rows = summed_over(table_rows, "ctx")
    table_grad = gather_blocks(table_rows, "dp").reshape(table_local.shape)
    return (
        query_grad[None],
        key_grad[None],
        value_grad[None],
        gate_grad[None],
        projection_grad,
        table_grad,
    )


def solution(mesh):
    return jax.shard_map(
        shards,
        mesh=mesh,
        in_specs=(
            P("dp", "ctx", None),
            P("dp", "ctx", None),
            P("dp", "ctx", None),
            P("dp", "ctx", None),
            P("dp", "ctx", None),
            P("dp", None),
            P("dp", None),
            P("dp", None, None),
            P(),
            P(),
        ),
        out_specs=(
            P("dp", "ctx", None),
            P("dp", "ctx", None),
            P("dp", "ctx", None),
            P("dp", "ctx", None),
            P("dp", None),
            P(),
        ),
        check_vma=False,
    )
```

```python
import jax
import jax.numpy as jnp
from jax import lax
from jax.sharding import PartitionSpec as P

BLK = 128


NORM_EPSILON = 1e-05


def passed_along(value, axis, by):
    length = lax.axis_size(axis)
    pairs = [(i, i + by) for i in range(length) if 0 <= i + by < length]
    return lax.ppermute(value, axis, pairs)


def exchanged(value, axis, mask):
    length = lax.axis_size(axis)
    pairs = [(i, i ^ mask) for i in range(length)]
    return lax.ppermute(value, axis, pairs)


def axis_bits(axis):
    length = lax.axis_size(axis)
    bits = []
    mask = 1
    while mask < length:
        bits.append(mask)
        mask *= 2
    return bits


def scatter_blocks(blocks, axis):
    index = lax.axis_index(axis)
    for mask in axis_bits(axis):
        bit = (index // mask) % 2
        pairs = blocks.reshape(blocks.shape[0] // 2, 2, blocks.shape[1])
        keep = lax.dynamic_index_in_dim(pairs, bit, axis=1, keepdims=False)
        send = lax.dynamic_index_in_dim(pairs, 1 - bit, axis=1, keepdims=False)
        blocks = keep + exchanged(send, axis, mask)
    return blocks[0]


def gather_blocks(chunk, axis):
    index = lax.axis_index(axis)
    held = chunk[None]
    for mask in reversed(axis_bits(axis)):
        bit = (index // mask) % 2
        other = exchanged(held, axis, mask)
        low = jnp.where(bit == 0, held, other)
        high = jnp.where(bit == 0, other, held)
        held = jnp.stack([low, high], axis=1).reshape(held.shape[0] * 2, held.shape[1])
    return held


def summed_over(flat, axis):
    size = lax.axis_size(axis)
    part = scatter_blocks(flat.reshape(size, flat.shape[0] // size), axis)
    return gather_blocks(part, axis).reshape(flat.shape)


def summed_by_exchange(flat, axes):
    size = 1
    for axis in axes:
        size *= lax.axis_size(axis)
    pieces = lax.all_to_all(flat.reshape(size, -1), axes, 0, 0, tiled=True)
    total = jnp.sum(pieces, axis=0, keepdims=True)
    spread = jnp.broadcast_to(total, pieces.shape)
    return lax.all_to_all(spread, axes, 0, 0, tiled=True).reshape(flat.shape)


def silu_slope(scores):
    sigmoid = jax.nn.sigmoid(scores)
    return sigmoid * (1.0 + scores * (1.0 - sigmoid))


def expand_blocks(block_rows, block_size):
    return jnp.repeat(jnp.repeat(block_rows, block_size, axis=0), block_size, axis=1)


def shards(
    queries,
    keys,
    values,
    gates,
    out_grad,
    time_bucket,
    lengths,
    block_map,
    bucket_bias_matrix,
    w_out,
):
    query_rows = queries[0]
    key_rows = keys[0]
    value_rows = values[0]
    gate_rows = gates[0]
    grad_rows = out_grad[0]
    local_rows, width = query_rows.shape
    head_count = bucket_bias_matrix.shape[0]
    bucket_count = bucket_bias_matrix.shape[1]
    head_dim = width // head_count
    scale = head_dim ** (-0.5)
    blocks_here = local_rows // BLK
    cycle_index = lax.axis_index("ctx")
    row_start = cycle_index * local_rows
    offsets = jnp.cumsum(lengths[0], dtype=jnp.int32) - lengths[0]

    def segment_of(positions):
        return jnp.sum(
            (positions[:, None] >= offsets[None, 1:]).astype(jnp.int32), axis=1, dtype=jnp.int32
        )

    bucket_ids = jnp.arange(bucket_count, dtype=jnp.int32)
    query_pos = row_start + jnp.arange(local_rows, dtype=jnp.int32)
    query_seg = segment_of(query_pos)
    query_bucket = lax.dynamic_slice_in_dim(time_bucket[0], row_start, local_rows, 0)
    query_bucket_indicator = (query_bucket[:, None] == bucket_ids[None, :]).astype(jnp.bfloat16)
    bias_matrix_rows = jnp.einsum(
        "lf,sfq->slq",
        query_bucket_indicator,
        bucket_bias_matrix,
        preferred_element_type=jnp.float32,
    ).astype(jnp.bfloat16)
    map_rows = lax.dynamic_slice_in_dim(block_map[0], cycle_index * blocks_here, blocks_here, 0)
    query_heads = query_rows.reshape(local_rows, head_count, head_dim)
    stacked = jnp.stack([key_rows, value_rows])
    window = [stacked, passed_along(stacked, "ctx", 1), passed_along(stacked, "ctx", 2)]
    tiles = []
    attended = jnp.zeros((local_rows, head_count, head_dim), jnp.float32)
    for distance in range(3):
        key_first = row_start - distance * local_rows
        key_pos = key_first + jnp.arange(local_rows, dtype=jnp.int32)
        safe_first = jnp.maximum(key_first, 0)
        key_bucket = lax.dynamic_slice_in_dim(time_bucket[0], safe_first, local_rows, 0)
        key_bucket_indicator = (key_bucket[:, None] == bucket_ids[None, :]).astype(jnp.bfloat16)
        map_cols = lax.dynamic_slice_in_dim(map_rows, safe_first // BLK, blocks_here, 1)
        same_block = query_pos[:, None] // BLK == key_pos[None, :] // BLK
        key_visible = (
            (query_seg[:, None] == segment_of(key_pos)[None, :])
            & (key_pos[None, :] <= query_pos[:, None])
            & (key_pos[None, :] >= 0)
            & ((expand_blocks(map_cols, BLK) == 1) | same_block)
        )
        key_bias_terms = jnp.einsum(
            "vqx,px->vqp",
            bias_matrix_rows,
            key_bucket_indicator,
            preferred_element_type=jnp.float32,
        )
        visible, bias_terms, key_bucket_indicator = (
            key_visible,
            key_bias_terms,
            key_bucket_indicator,
        )
        forward_pair = window[distance]
        forward_key_heads = forward_pair[0].reshape(local_rows, head_count, head_dim)
        forward_value_heads = forward_pair[1].reshape(local_rows, head_count, head_dim)
        forward_scores = (
            jnp.einsum(
                "ihd,jhd->hij", query_heads, forward_key_heads, preferred_element_type=jnp.float32
            )
            * scale
            + bias_terms
        )
        forward_weights = jnp.where(visible[None], jax.nn.silu(forward_scores), 0.0).astype(
            jnp.bfloat16
        )
        attended_part = jnp.einsum(
            "hij,jhd->ihd", forward_weights, forward_value_heads, preferred_element_type=jnp.float32
        )
        attended = attended + attended_part
        tiles.append((visible, forward_scores, forward_weights, key_bucket_indicator))
    attended = attended.reshape(local_rows, width)
    centered = attended - jnp.mean(attended, axis=1, keepdims=True)
    inverse = lax.rsqrt(jnp.mean(centered * centered, axis=1, keepdims=True) + NORM_EPSILON)
    normed = centered * inverse
    dz_rows = lax.dot_general(
        grad_rows, w_out, (((1,), (1,)), ((), ())), preferred_element_type=jnp.float32
    )
    gate_float = gate_rows.astype(jnp.float32)
    gate_grad = (dz_rows * normed).astype(jnp.bfloat16)
    mixed = (normed * gate_float).astype(jnp.bfloat16)
    lifted = dz_rows * gate_float
    attended_grad = (
        (
            lifted
            - jnp.mean(lifted, axis=1, keepdims=True)
            - normed * jnp.mean(lifted * normed, axis=1, keepdims=True)
        )
        * inverse
    ).astype(jnp.bfloat16)
    grad_heads = attended_grad.reshape(local_rows, head_count, head_dim)
    indicator_float = query_bucket_indicator.astype(jnp.float32)
    query_sum = jnp.zeros((local_rows, width), jnp.float32)
    table_local = jnp.zeros((head_count, bucket_count, bucket_count), jnp.float32)
    key_terms = [None, None, None]
    for distance in (2, 1, 0):
        visible, scores, weights, key_bucket_indicator = tiles[distance]
        pair = window[distance]
        key_heads = pair[0].reshape(local_rows, head_count, head_dim)
        value_heads = pair[1].reshape(local_rows, head_count, head_dim)
        weight_grad = jnp.einsum(
            "ihd,jhd->hij", grad_heads, value_heads, preferred_element_type=jnp.float32
        )
        value_part = jnp.einsum(
            "hij,ihd->jhd", weights, grad_heads, preferred_element_type=jnp.float32
        ).reshape(local_rows, width)
        score_gradient = jnp.where(visible[None], weight_grad * silu_slope(scores), 0.0).astype(
            jnp.bfloat16
        )
        query_part = jnp.einsum(
            "hij,jhd->ihd", score_gradient, key_heads, preferred_element_type=jnp.float32
        ).reshape(local_rows, width)
        key_part = (
            jnp.einsum(
                "hij,ihd->jhd", score_gradient, query_heads, preferred_element_type=jnp.float32
            ).reshape(local_rows, width)
            * scale
        )
        bucket_share_piece = jnp.einsum(
            "rmw,wx->rmx", score_gradient, key_bucket_indicator, preferred_element_type=jnp.float32
        )
        table_part = jnp.einsum(
            "qp,cqk->cpk", indicator_float, bucket_share_piece, precision=lax.Precision.HIGHEST
        )
        query_sum = query_sum + query_part
        table_local = table_local + table_part
        key_terms[distance] = jnp.stack([key_part, value_part])
    gathered = (
        key_terms[0] + passed_along(key_terms[1], "ctx", -1) + passed_along(key_terms[2], "ctx", -2)
    )
    query_grad = (query_sum * scale).astype(jnp.bfloat16)
    key_grad = gathered[0].astype(jnp.bfloat16)
    value_grad = gathered[1].astype(jnp.bfloat16)
    dp_size = lax.axis_size("dp")
    weight_term = lax.dot_general(
        mixed, grad_rows, (((0,), (0,)), ((), ())), preferred_element_type=jnp.float32
    )
    weight_rows = scatter_blocks(weight_term.reshape(dp_size, -1), "dp")
    projection_grad = summed_over(weight_rows, "ctx").reshape(width // dp_size, width)
    table_grad = summed_by_exchange(table_local.reshape(-1), ("ctx", "dp")).reshape(
        table_local.shape
    )
    return (
        query_grad[None],
        key_grad[None],
        value_grad[None],
        gate_grad[None],
        projection_grad,
        table_grad,
    )


def solution(mesh):
    return jax.shard_map(
        shards,
        mesh=mesh,
        in_specs=(
            P("dp", "ctx", None),
            P("dp", "ctx", None),
            P("dp", "ctx", None),
            P("dp", "ctx", None),
            P("dp", "ctx", None),
            P("dp", None),
            P("dp", None),
            P("dp", None, None),
            P(),
            P(),
        ),
        out_specs=(
            P("dp", "ctx", None),
            P("dp", "ctx", None),
            P("dp", "ctx", None),
            P("dp", "ctx", None),
            P("dp", None),
            P(),
        ),
        check_vma=False,
    )
```

```python
import jax
import jax.numpy as jnp
from jax import lax
from jax.sharding import PartitionSpec as P

BLK = 128


NORM_EPSILON = 1e-05


def passed_along(value, axis, by):
    length = lax.axis_size(axis)
    pairs = [(i, i + by) for i in range(length) if 0 <= i + by < length]
    return lax.ppermute(value, axis, pairs)


def exchanged(value, axis, mask):
    length = lax.axis_size(axis)
    pairs = [(i, i ^ mask) for i in range(length)]
    return lax.ppermute(value, axis, pairs)


def axis_bits(axis):
    length = lax.axis_size(axis)
    bits = []
    mask = 1
    while mask < length:
        bits.append(mask)
        mask *= 2
    return bits


def scatter_blocks(blocks, axis):
    index = lax.axis_index(axis)
    for mask in axis_bits(axis):
        bit = (index // mask) % 2
        pairs = blocks.reshape(blocks.shape[0] // 2, 2, blocks.shape[1])
        keep = lax.dynamic_index_in_dim(pairs, bit, axis=1, keepdims=False)
        send = lax.dynamic_index_in_dim(pairs, 1 - bit, axis=1, keepdims=False)
        blocks = keep + exchanged(send, axis, mask)
    return blocks[0]


def gather_blocks(chunk, axis):
    index = lax.axis_index(axis)
    held = chunk[None]
    for mask in reversed(axis_bits(axis)):
        bit = (index // mask) % 2
        other = exchanged(held, axis, mask)
        low = jnp.where(bit == 0, held, other)
        high = jnp.where(bit == 0, other, held)
        held = jnp.stack([low, high], axis=1).reshape(held.shape[0] * 2, held.shape[1])
    return held


def summed_over(flat, axis):
    size = lax.axis_size(axis)
    part = scatter_blocks(flat.reshape(size, flat.shape[0] // size), axis)
    return gather_blocks(part, axis).reshape(flat.shape)


def plan_step(blocks, kind, axis, mask):
    bit = (lax.axis_index(axis) // mask) % 2
    if kind == "split":
        if blocks.shape[0] == 1:
            blocks = blocks.reshape(2, -1)
        pairs = blocks.reshape(blocks.shape[0] // 2, 2, blocks.shape[1])
        keep = lax.dynamic_index_in_dim(pairs, bit, axis=1, keepdims=False)
        send = lax.dynamic_index_in_dim(pairs, 1 - bit, axis=1, keepdims=False)
        return keep + exchanged(send, axis, mask)
    other = exchanged(blocks, axis, mask)
    low = jnp.where(bit == 0, blocks, other)
    high = jnp.where(bit == 0, other, blocks)
    return jnp.concatenate([low, high], axis=1)


def summed_by_exchange(flat, axes):
    size = 1
    for axis in axes:
        size *= lax.axis_size(axis)
    pieces = lax.all_to_all(flat.reshape(size, -1), axes, 0, 0, tiled=True)
    total = jnp.sum(pieces, axis=0, keepdims=True)
    spread = jnp.broadcast_to(total, pieces.shape)
    return lax.all_to_all(spread, axes, 0, 0, tiled=True).reshape(flat.shape)


def silu_slope(scores):
    sigmoid = jax.nn.sigmoid(scores)
    return sigmoid * (1.0 + scores * (1.0 - sigmoid))


def expand_blocks(block_rows, block_size):
    return jnp.repeat(jnp.repeat(block_rows, block_size, axis=0), block_size, axis=1)


def shards(
    queries,
    keys,
    values,
    gates,
    out_grad,
    time_bucket,
    lengths,
    block_map,
    bucket_bias_matrix,
    w_out,
):
    query_rows = queries[0]
    key_rows = keys[0]
    value_rows = values[0]
    gate_rows = gates[0]
    grad_rows = out_grad[0]
    local_rows, width = query_rows.shape
    head_count = bucket_bias_matrix.shape[0]
    bucket_count = bucket_bias_matrix.shape[1]
    head_dim = width // head_count
    scale = head_dim ** (-0.5)
    blocks_here = local_rows // BLK
    cycle_index = lax.axis_index("ctx")
    row_start = cycle_index * local_rows
    offsets = jnp.cumsum(lengths[0], dtype=jnp.int32) - lengths[0]

    def segment_of(positions):
        return jnp.sum(
            (positions[:, None] >= offsets[None, 1:]).astype(jnp.int32), axis=1, dtype=jnp.int32
        )

    bucket_ids = jnp.arange(bucket_count, dtype=jnp.int32)
    query_pos = row_start + jnp.arange(local_rows, dtype=jnp.int32)
    query_seg = segment_of(query_pos)
    query_bucket = lax.dynamic_slice_in_dim(time_bucket[0], row_start, local_rows, 0)
    query_bucket_indicator = (query_bucket[:, None] == bucket_ids[None, :]).astype(jnp.bfloat16)
    bias_matrix_rows = jnp.einsum(
        "lf,sfq->slq",
        query_bucket_indicator,
        bucket_bias_matrix,
        preferred_element_type=jnp.float32,
    ).astype(jnp.bfloat16)
    map_rows = lax.dynamic_slice_in_dim(block_map[0], cycle_index * blocks_here, blocks_here, 0)
    query_heads = query_rows.reshape(local_rows, head_count, head_dim)
    stacked = jnp.stack([key_rows, value_rows])
    window = [stacked, passed_along(stacked, "ctx", 1), passed_along(stacked, "ctx", 2)]
    tiles = []
    attended = jnp.zeros((local_rows, head_count, head_dim), jnp.float32)
    for distance in range(3):
        key_first = row_start - distance * local_rows
        key_pos = key_first + jnp.arange(local_rows, dtype=jnp.int32)
        safe_first = jnp.maximum(key_first, 0)
        key_bucket = lax.dynamic_slice_in_dim(time_bucket[0], safe_first, local_rows, 0)
        key_bucket_indicator = (key_bucket[:, None] == bucket_ids[None, :]).astype(jnp.bfloat16)
        map_cols = lax.dynamic_slice_in_dim(map_rows, safe_first // BLK, blocks_here, 1)
        same_block = query_pos[:, None] // BLK == key_pos[None, :] // BLK
        key_visible = (
            (query_seg[:, None] == segment_of(key_pos)[None, :])
            & (key_pos[None, :] <= query_pos[:, None])
            & (key_pos[None, :] >= 0)
            & ((expand_blocks(map_cols, BLK) == 1) | same_block)
        )
        key_bias_terms = jnp.einsum(
            "vqx,px->vqp",
            bias_matrix_rows,
            key_bucket_indicator,
            preferred_element_type=jnp.float32,
        )
        visible, bias_terms, key_bucket_indicator = (
            key_visible,
            key_bias_terms,
            key_bucket_indicator,
        )
        forward_pair = window[distance]
        forward_key_heads = forward_pair[0].reshape(local_rows, head_count, head_dim)
        forward_value_heads = forward_pair[1].reshape(local_rows, head_count, head_dim)
        forward_scores = (
            jnp.einsum(
                "ihd,jhd->hij", query_heads, forward_key_heads, preferred_element_type=jnp.float32
            )
            * scale
            + bias_terms
        )
        forward_weights = jnp.where(visible[None], jax.nn.silu(forward_scores), 0.0).astype(
            jnp.bfloat16
        )
        attended_part = jnp.einsum(
            "hij,jhd->ihd", forward_weights, forward_value_heads, preferred_element_type=jnp.float32
        )
        attended = attended + attended_part
        tiles.append((visible, forward_scores, forward_weights, key_bucket_indicator))
    attended = attended.reshape(local_rows, width)
    centered = attended - jnp.mean(attended, axis=1, keepdims=True)
    inverse = lax.rsqrt(jnp.mean(centered * centered, axis=1, keepdims=True) + NORM_EPSILON)
    normed = centered * inverse
    dz_rows = lax.dot_general(
        grad_rows, w_out, (((1,), (1,)), ((), ())), preferred_element_type=jnp.float32
    )
    gate_float = gate_rows.astype(jnp.float32)
    gate_grad = (dz_rows * normed).astype(jnp.bfloat16)
    mixed = (normed * gate_float).astype(jnp.bfloat16)
    lifted = dz_rows * gate_float
    attended_grad = (
        (
            lifted
            - jnp.mean(lifted, axis=1, keepdims=True)
            - normed * jnp.mean(lifted * normed, axis=1, keepdims=True)
        )
        * inverse
    ).astype(jnp.bfloat16)
    grad_heads = attended_grad.reshape(local_rows, head_count, head_dim)
    indicator_float = query_bucket_indicator.astype(jnp.float32)
    dp_size = lax.axis_size("dp")
    weight_term = lax.dot_general(
        mixed, grad_rows, (((0,), (0,)), ((), ())), preferred_element_type=jnp.float32
    )
    weight_plan = [("split", "dp", mask) for mask in axis_bits("dp")]
    weight_plan += [("split", "ctx", mask) for mask in axis_bits("ctx")]
    weight_plan += [("join", "ctx", mask) for mask in reversed(axis_bits("ctx"))]
    weight_state = [weight_term.reshape(dp_size, -1), 0]

    def slot(anchor):
        blocks, done = weight_state
        if done < len(weight_plan):
            blocks, anchor = lax.optimization_barrier((blocks, anchor))
            weight_state[0] = plan_step(blocks, *weight_plan[done])
            weight_state[1] = done + 1
        return anchor

    query_sum = jnp.zeros((local_rows, width), jnp.float32)
    share_sum = None
    key_terms = [None, None, None]
    sent = [None, None, None]
    for distance in (2, 1, 0):
        visible, scores, weights, key_bucket_indicator = tiles[distance]
        pair = slot(window[distance])
        if distance == 0:
            sent[2], pair = lax.optimization_barrier((sent[2], pair))
        key_heads = pair[0].reshape(local_rows, head_count, head_dim)
        value_heads = pair[1].reshape(local_rows, head_count, head_dim)
        weight_grad = jnp.einsum(
            "ihd,jhd->hij", grad_heads, value_heads, preferred_element_type=jnp.float32
        )
        value_part = jnp.einsum(
            "hij,ihd->jhd", weights, grad_heads, preferred_element_type=jnp.float32
        ).reshape(local_rows, width)
        score_gradient = jnp.where(visible[None], weight_grad * silu_slope(scores), 0.0).astype(
            jnp.bfloat16
        )
        score_gradient = slot(score_gradient)
        query_part = jnp.einsum(
            "hij,jhd->ihd", score_gradient, key_heads, preferred_element_type=jnp.float32
        ).reshape(local_rows, width)
        key_part = (
            jnp.einsum(
                "hij,ihd->jhd", score_gradient, query_heads, preferred_element_type=jnp.float32
            ).reshape(local_rows, width)
            * scale
        )
        bucket_share_piece = jnp.einsum(
            "rmw,wx->rmx", score_gradient, key_bucket_indicator, preferred_element_type=jnp.float32
        )
        share_sum = bucket_share_piece if share_sum is None else share_sum + bucket_share_piece
        query_sum = query_sum + query_part
        key_terms[distance] = jnp.stack([key_part, value_part])
        if distance > 0:
            sent[distance] = passed_along(key_terms[distance], "ctx", -distance)
    table_local = jnp.einsum(
        "qp,cqk->cpk", indicator_float, share_sum, precision=lax.Precision.HIGHEST
    )
    table_local = slot(table_local)
    while weight_state[1] < len(weight_plan):
        table_local = slot(table_local)
    gathered = key_terms[0] + sent[1] + sent[2]
    query_grad = (query_sum * scale).astype(jnp.bfloat16)
    key_grad = gathered[0].astype(jnp.bfloat16)
    value_grad = gathered[1].astype(jnp.bfloat16)
    projection_grad = weight_state[0].reshape(width // dp_size, width)
    table_grad = summed_by_exchange(table_local.reshape(-1), ("ctx", "dp")).reshape(
        table_local.shape
    )
    return (
        query_grad[None],
        key_grad[None],
        value_grad[None],
        gate_grad[None],
        projection_grad,
        table_grad,
    )


def solution(mesh):
    return jax.shard_map(
        shards,
        mesh=mesh,
        in_specs=(
            P("dp", "ctx", None),
            P("dp", "ctx", None),
            P("dp", "ctx", None),
            P("dp", "ctx", None),
            P("dp", "ctx", None),
            P("dp", None),
            P("dp", None),
            P("dp", None, None),
            P(),
            P(),
        ),
        out_specs=(
            P("dp", "ctx", None),
            P("dp", "ctx", None),
            P("dp", "ctx", None),
            P("dp", "ctx", None),
            P("dp", None),
            P(),
        ),
        check_vma=False,
    )
```

```python
import jax
import jax.numpy as jnp
from jax import lax
from jax.sharding import PartitionSpec as P

BLK = 128


NORM_EPSILON = 1e-05


def passed_along(value, axis, by):
    length = lax.axis_size(axis)
    pairs = [(i, i + by) for i in range(length) if 0 <= i + by < length]
    return lax.ppermute(value, axis, pairs)


def exchanged(value, axis, mask):
    length = lax.axis_size(axis)
    pairs = [(i, i ^ mask) for i in range(length)]
    return lax.ppermute(value, axis, pairs)


def axis_bits(axis):
    length = lax.axis_size(axis)
    bits = []
    mask = 1
    while mask < length:
        bits.append(mask)
        mask *= 2
    return bits


def scatter_blocks(blocks, axis):
    index = lax.axis_index(axis)
    for mask in axis_bits(axis):
        bit = (index // mask) % 2
        pairs = blocks.reshape(blocks.shape[0] // 2, 2, blocks.shape[1])
        keep = lax.dynamic_index_in_dim(pairs, bit, axis=1, keepdims=False)
        send = lax.dynamic_index_in_dim(pairs, 1 - bit, axis=1, keepdims=False)
        blocks = keep + exchanged(send, axis, mask)
    return blocks[0]


def gather_blocks(chunk, axis):
    index = lax.axis_index(axis)
    held = chunk[None]
    for mask in reversed(axis_bits(axis)):
        bit = (index // mask) % 2
        other = exchanged(held, axis, mask)
        low = jnp.where(bit == 0, held, other)
        high = jnp.where(bit == 0, other, held)
        held = jnp.stack([low, high], axis=1).reshape(held.shape[0] * 2, held.shape[1])
    return held


def summed_over(flat, axis):
    size = lax.axis_size(axis)
    part = scatter_blocks(flat.reshape(size, flat.shape[0] // size), axis)
    return gather_blocks(part, axis).reshape(flat.shape)


def plan_step(blocks, kind, axis, mask):
    bit = (lax.axis_index(axis) // mask) % 2
    if kind == "split":
        if blocks.shape[0] == 1:
            blocks = blocks.reshape(2, -1)
        pairs = blocks.reshape(blocks.shape[0] // 2, 2, blocks.shape[1])
        keep = lax.dynamic_index_in_dim(pairs, bit, axis=1, keepdims=False)
        send = lax.dynamic_index_in_dim(pairs, 1 - bit, axis=1, keepdims=False)
        return keep + exchanged(send, axis, mask)
    other = exchanged(blocks, axis, mask)
    low = jnp.where(bit == 0, blocks, other)
    high = jnp.where(bit == 0, other, blocks)
    return jnp.concatenate([low, high], axis=1)


def summed_by_exchange(flat, axes):
    size = 1
    for axis in axes:
        size *= lax.axis_size(axis)
    pieces = lax.all_to_all(flat.reshape(size, -1), axes, 0, 0, tiled=True)
    total = jnp.sum(pieces, axis=0, keepdims=True)
    spread = jnp.broadcast_to(total, pieces.shape)
    return lax.all_to_all(spread, axes, 0, 0, tiled=True).reshape(flat.shape)


def silu_slope(scores):
    sigmoid = jax.nn.sigmoid(scores)
    return sigmoid * (1.0 + scores * (1.0 - sigmoid))


def expand_blocks(block_rows, block_size):
    return jnp.repeat(jnp.repeat(block_rows, block_size, axis=0), block_size, axis=1)


def shards(
    queries,
    keys,
    values,
    gates,
    out_grad,
    time_bucket,
    lengths,
    block_map,
    bucket_bias_matrix,
    w_out,
):
    query_rows = queries[0]
    key_rows = keys[0]
    value_rows = values[0]
    gate_rows = gates[0]
    grad_rows = out_grad[0]
    local_rows, width = query_rows.shape
    head_count = bucket_bias_matrix.shape[0]
    bucket_count = bucket_bias_matrix.shape[1]
    head_dim = width // head_count
    scale = head_dim ** (-0.5)
    blocks_here = local_rows // BLK
    cycle_index = lax.axis_index("ctx")
    row_start = cycle_index * local_rows
    offsets = jnp.cumsum(lengths[0], dtype=jnp.int32) - lengths[0]

    def segment_of(positions):
        return jnp.sum(
            (positions[:, None] >= offsets[None, 1:]).astype(jnp.int32), axis=1, dtype=jnp.int32
        )

    bucket_ids = jnp.arange(bucket_count, dtype=jnp.int32)
    query_pos = row_start + jnp.arange(local_rows, dtype=jnp.int32)
    query_seg = segment_of(query_pos)
    query_bucket = lax.dynamic_slice_in_dim(time_bucket[0], row_start, local_rows, 0)
    query_bucket_indicator = (query_bucket[:, None] == bucket_ids[None, :]).astype(jnp.bfloat16)
    bias_matrix_rows = jnp.einsum(
        "lf,sfq->slq",
        query_bucket_indicator,
        bucket_bias_matrix,
        preferred_element_type=jnp.float32,
    ).astype(jnp.bfloat16)
    map_rows = lax.dynamic_slice_in_dim(block_map[0], cycle_index * blocks_here, blocks_here, 0)
    query_heads = query_rows.reshape(local_rows, head_count, head_dim)
    stacked = jnp.stack([key_rows, value_rows])
    window = [stacked, passed_along(stacked, "ctx", 1), passed_along(stacked, "ctx", 2)]
    tiles = []
    attended = jnp.zeros((local_rows, head_count, head_dim), jnp.float32)
    for distance in range(3):
        key_first = row_start - distance * local_rows
        key_pos = key_first + jnp.arange(local_rows, dtype=jnp.int32)
        safe_first = jnp.maximum(key_first, 0)
        key_bucket = lax.dynamic_slice_in_dim(time_bucket[0], safe_first, local_rows, 0)
        key_bucket_indicator = (key_bucket[:, None] == bucket_ids[None, :]).astype(jnp.bfloat16)
        map_cols = lax.dynamic_slice_in_dim(map_rows, safe_first // BLK, blocks_here, 1)
        same_block = query_pos[:, None] // BLK == key_pos[None, :] // BLK
        key_visible = (
            (query_seg[:, None] == segment_of(key_pos)[None, :])
            & (key_pos[None, :] <= query_pos[:, None])
            & (key_pos[None, :] >= 0)
            & ((expand_blocks(map_cols, BLK) == 1) | same_block)
        )
        key_bias_terms = jnp.einsum(
            "vqx,px->vqp",
            bias_matrix_rows,
            key_bucket_indicator,
            preferred_element_type=jnp.float32,
        )
        visible, bias_terms, key_bucket_indicator = (
            key_visible,
            key_bias_terms,
            key_bucket_indicator,
        )
        forward_pair = window[distance]
        forward_key_heads = forward_pair[0].reshape(local_rows, head_count, head_dim)
        forward_value_heads = forward_pair[1].reshape(local_rows, head_count, head_dim)
        forward_scores = (
            jnp.einsum(
                "ihd,jhd->hij", query_heads, forward_key_heads, preferred_element_type=jnp.float32
            )
            * scale
            + bias_terms
        )
        forward_weights = jnp.where(visible[None], jax.nn.silu(forward_scores), 0.0).astype(
            jnp.bfloat16
        )
        attended_part = jnp.einsum(
            "hij,jhd->ihd", forward_weights, forward_value_heads, preferred_element_type=jnp.float32
        )
        attended = attended + attended_part
        tiles.append((visible, forward_scores, forward_weights, key_bucket_indicator))
    attended = attended.reshape(local_rows, width)
    centered = attended - jnp.mean(attended, axis=1, keepdims=True)
    inverse = lax.rsqrt(jnp.mean(centered * centered, axis=1, keepdims=True) + NORM_EPSILON)
    normed = centered * inverse
    dz_rows = lax.dot_general(
        grad_rows, w_out, (((1,), (1,)), ((), ())), preferred_element_type=jnp.float32
    )
    gate_float = gate_rows.astype(jnp.float32)
    gate_grad = (dz_rows * normed).astype(jnp.bfloat16)
    mixed = (normed * gate_float).astype(jnp.bfloat16)
    lifted = dz_rows * gate_float
    attended_grad = (
        (
            lifted
            - jnp.mean(lifted, axis=1, keepdims=True)
            - normed * jnp.mean(lifted * normed, axis=1, keepdims=True)
        )
        * inverse
    ).astype(jnp.bfloat16)
    grad_heads = attended_grad.reshape(local_rows, head_count, head_dim)
    indicator_float = query_bucket_indicator.astype(jnp.float32)
    dp_size = lax.axis_size("dp")
    weight_term = lax.dot_general(
        mixed, grad_rows, (((0,), (0,)), ((), ())), preferred_element_type=jnp.float32
    )
    weight_plan = [("split", "dp", mask) for mask in axis_bits("dp")]
    weight_plan.append(("exchange", "ctx", 0))
    weight_state = [weight_term.reshape(dp_size, -1), 0]

    def slot(anchor):
        blocks, done = weight_state
        if done < len(weight_plan):
            blocks, anchor = lax.optimization_barrier((blocks, anchor))
            kind, axis, mask = weight_plan[done]
            if kind == "exchange":
                weight_state[0] = summed_by_exchange(blocks.reshape(-1), (axis,))
            else:
                weight_state[0] = plan_step(blocks, kind, axis, mask)
            weight_state[1] = done + 1
        return anchor

    query_sum = jnp.zeros((local_rows, width), jnp.float32)
    share_sum = None
    key_terms = [None, None, None]
    sent = [None, None, None]
    for distance in (2, 1, 0):
        visible, scores, weights, key_bucket_indicator = tiles[distance]
        pair = slot(window[distance])
        if distance == 0:
            sent[2], pair = lax.optimization_barrier((sent[2], pair))
        key_heads = pair[0].reshape(local_rows, head_count, head_dim)
        value_heads = pair[1].reshape(local_rows, head_count, head_dim)
        weight_grad = jnp.einsum(
            "ihd,jhd->hij", grad_heads, value_heads, preferred_element_type=jnp.float32
        )
        value_part = jnp.einsum(
            "hij,ihd->jhd", weights, grad_heads, preferred_element_type=jnp.float32
        ).reshape(local_rows, width)
        score_gradient = jnp.where(visible[None], weight_grad * silu_slope(scores), 0.0).astype(
            jnp.bfloat16
        )
        score_gradient = slot(score_gradient)
        query_part = jnp.einsum(
            "hij,jhd->ihd", score_gradient, key_heads, preferred_element_type=jnp.float32
        ).reshape(local_rows, width)
        key_part = (
            jnp.einsum(
                "hij,ihd->jhd", score_gradient, query_heads, preferred_element_type=jnp.float32
            ).reshape(local_rows, width)
            * scale
        )
        bucket_share_piece = jnp.einsum(
            "rmw,wx->rmx", score_gradient, key_bucket_indicator, preferred_element_type=jnp.float32
        )
        share_sum = bucket_share_piece if share_sum is None else share_sum + bucket_share_piece
        query_sum = query_sum + query_part
        key_terms[distance] = jnp.stack([key_part, value_part])
        if distance > 0:
            sent[distance] = passed_along(key_terms[distance], "ctx", -distance)
    table_local = jnp.einsum(
        "qp,cqk->cpk", indicator_float, share_sum, precision=lax.Precision.HIGHEST
    )
    gathered = key_terms[0] + sent[1] + sent[2]
    query_grad = (query_sum * scale).astype(jnp.bfloat16)
    key_grad = gathered[0].astype(jnp.bfloat16)
    value_grad = gathered[1].astype(jnp.bfloat16)
    projection_grad = weight_state[0].reshape(width // dp_size, width)
    table_grad = summed_by_exchange(table_local.reshape(-1), ("ctx", "dp")).reshape(
        table_local.shape
    )
    return (
        query_grad[None],
        key_grad[None],
        value_grad[None],
        gate_grad[None],
        projection_grad,
        table_grad,
    )


def solution(mesh):
    return jax.shard_map(
        shards,
        mesh=mesh,
        in_specs=(
            P("dp", "ctx", None),
            P("dp", "ctx", None),
            P("dp", "ctx", None),
            P("dp", "ctx", None),
            P("dp", "ctx", None),
            P("dp", None),
            P("dp", None),
            P("dp", None, None),
            P(),
            P(),
        ),
        out_specs=(
            P("dp", "ctx", None),
            P("dp", "ctx", None),
            P("dp", "ctx", None),
            P("dp", "ctx", None),
            P("dp", None),
            P(),
        ),
        check_vma=False,
    )
```

```python
import jax
import jax.numpy as jnp
from jax import lax
from jax.sharding import PartitionSpec as P

BLK = 128


NORM_EPSILON = 1e-05


def passed_along(value, axis, by):
    length = lax.axis_size(axis)
    pairs = [(i, i + by) for i in range(length) if 0 <= i + by < length]
    return lax.ppermute(value, axis, pairs)


def exchanged(value, axis, mask):
    length = lax.axis_size(axis)
    pairs = [(i, i ^ mask) for i in range(length)]
    return lax.ppermute(value, axis, pairs)


def axis_bits(axis):
    length = lax.axis_size(axis)
    bits = []
    mask = 1
    while mask < length:
        bits.append(mask)
        mask *= 2
    return bits


def scatter_blocks(blocks, axis):
    index = lax.axis_index(axis)
    for mask in axis_bits(axis):
        bit = (index // mask) % 2
        pairs = blocks.reshape(blocks.shape[0] // 2, 2, blocks.shape[1])
        keep = lax.dynamic_index_in_dim(pairs, bit, axis=1, keepdims=False)
        send = lax.dynamic_index_in_dim(pairs, 1 - bit, axis=1, keepdims=False)
        blocks = keep + exchanged(send, axis, mask)
    return blocks[0]


def gather_blocks(chunk, axis):
    index = lax.axis_index(axis)
    held = chunk[None]
    for mask in reversed(axis_bits(axis)):
        bit = (index // mask) % 2
        other = exchanged(held, axis, mask)
        low = jnp.where(bit == 0, held, other)
        high = jnp.where(bit == 0, other, held)
        held = jnp.stack([low, high], axis=1).reshape(held.shape[0] * 2, held.shape[1])
    return held


def summed_over(flat, axis):
    size = lax.axis_size(axis)
    part = scatter_blocks(flat.reshape(size, flat.shape[0] // size), axis)
    return gather_blocks(part, axis).reshape(flat.shape)


def plan_step(blocks, kind, axis, mask):
    bit = (lax.axis_index(axis) // mask) % 2
    if kind == "split":
        if blocks.shape[0] == 1:
            blocks = blocks.reshape(2, -1)
        pairs = blocks.reshape(blocks.shape[0] // 2, 2, blocks.shape[1])
        keep = lax.dynamic_index_in_dim(pairs, bit, axis=1, keepdims=False)
        send = lax.dynamic_index_in_dim(pairs, 1 - bit, axis=1, keepdims=False)
        return keep + exchanged(send, axis, mask)
    other = exchanged(blocks, axis, mask)
    low = jnp.where(bit == 0, blocks, other)
    high = jnp.where(bit == 0, other, blocks)
    return jnp.concatenate([low, high], axis=1)


def summed_by_exchange(flat, axes):
    size = 1
    for axis in axes:
        size *= lax.axis_size(axis)
    pieces = lax.all_to_all(flat.reshape(size, -1), axes, 0, 0, tiled=True)
    total = jnp.sum(pieces, axis=0, keepdims=True)
    spread = jnp.broadcast_to(total, pieces.shape)
    return lax.all_to_all(spread, axes, 0, 0, tiled=True).reshape(flat.shape)


def silu_slope(scores):
    sigmoid = jax.nn.sigmoid(scores)
    return sigmoid * (1.0 + scores * (1.0 - sigmoid))


def expand_blocks(block_rows, block_size):
    return jnp.repeat(jnp.repeat(block_rows, block_size, axis=0), block_size, axis=1)


def shards(
    queries,
    keys,
    values,
    gates,
    out_grad,
    time_bucket,
    lengths,
    block_map,
    bucket_bias_matrix,
    w_out,
):
    query_rows = queries[0]
    key_rows = keys[0]
    value_rows = values[0]
    gate_rows = gates[0]
    grad_rows = out_grad[0]
    local_rows, width = query_rows.shape
    head_count = bucket_bias_matrix.shape[0]
    bucket_count = bucket_bias_matrix.shape[1]
    head_dim = width // head_count
    scale = head_dim ** (-0.5)
    blocks_here = local_rows // BLK
    cycle_index = lax.axis_index("ctx")
    row_start = cycle_index * local_rows
    offsets = jnp.cumsum(lengths[0], dtype=jnp.int32) - lengths[0]

    def segment_of(positions):
        return jnp.sum(
            (positions[:, None] >= offsets[None, 1:]).astype(jnp.int32), axis=1, dtype=jnp.int32
        )

    bucket_ids = jnp.arange(bucket_count, dtype=jnp.int32)
    query_pos = row_start + jnp.arange(local_rows, dtype=jnp.int32)
    query_seg = segment_of(query_pos)
    query_bucket = lax.dynamic_slice_in_dim(time_bucket[0], row_start, local_rows, 0)
    query_bucket_indicator = (query_bucket[:, None] == bucket_ids[None, :]).astype(jnp.bfloat16)
    bias_matrix_rows = jnp.einsum(
        "lf,sfq->slq",
        query_bucket_indicator,
        bucket_bias_matrix,
        preferred_element_type=jnp.float32,
    ).astype(jnp.bfloat16)
    map_rows = lax.dynamic_slice_in_dim(block_map[0], cycle_index * blocks_here, blocks_here, 0)
    query_heads = query_rows.reshape(local_rows, head_count, head_dim)
    stacked = jnp.stack([key_rows, value_rows])
    window = [stacked, passed_along(stacked, "ctx", 1), passed_along(stacked, "ctx", 2)]
    tiles = []
    attended = jnp.zeros((local_rows, head_count, head_dim), jnp.float32)
    for distance in range(3):
        key_first = row_start - distance * local_rows
        key_pos = key_first + jnp.arange(local_rows, dtype=jnp.int32)
        safe_first = jnp.maximum(key_first, 0)
        key_bucket = lax.dynamic_slice_in_dim(time_bucket[0], safe_first, local_rows, 0)
        key_bucket_indicator = (key_bucket[:, None] == bucket_ids[None, :]).astype(jnp.bfloat16)
        map_cols = lax.dynamic_slice_in_dim(map_rows, safe_first // BLK, blocks_here, 1)
        same_block = query_pos[:, None] // BLK == key_pos[None, :] // BLK
        key_visible = (
            (query_seg[:, None] == segment_of(key_pos)[None, :])
            & (key_pos[None, :] <= query_pos[:, None])
            & (key_pos[None, :] >= 0)
            & ((expand_blocks(map_cols, BLK) == 1) | same_block)
        )
        key_bias_terms = jnp.einsum(
            "vqx,px->vqp",
            bias_matrix_rows,
            key_bucket_indicator,
            preferred_element_type=jnp.float32,
        )
        visible, bias_terms, key_bucket_indicator = (
            key_visible,
            key_bias_terms,
            key_bucket_indicator,
        )
        forward_pair = window[distance]
        forward_key_heads = forward_pair[0].reshape(local_rows, head_count, head_dim)
        forward_value_heads = forward_pair[1].reshape(local_rows, head_count, head_dim)
        forward_scores = (
            jnp.einsum(
                "ihd,jhd->hij", query_heads, forward_key_heads, preferred_element_type=jnp.float32
            )
            * scale
            + bias_terms
        )
        forward_weights = jnp.where(visible[None], jax.nn.silu(forward_scores), 0.0).astype(
            jnp.bfloat16
        )
        attended_part = jnp.einsum(
            "hij,jhd->ihd", forward_weights, forward_value_heads, preferred_element_type=jnp.float32
        )
        attended = attended + attended_part
        tiles.append((visible, forward_scores, forward_weights, key_bucket_indicator))
    attended = attended.reshape(local_rows, width)
    centered = attended - jnp.mean(attended, axis=1, keepdims=True)
    inverse = lax.rsqrt(jnp.mean(centered * centered, axis=1, keepdims=True) + NORM_EPSILON)
    normed = centered * inverse
    dz_rows = lax.dot_general(
        grad_rows, w_out, (((1,), (1,)), ((), ())), preferred_element_type=jnp.float32
    )
    gate_float = gate_rows.astype(jnp.float32)
    gate_grad = (dz_rows * normed).astype(jnp.bfloat16)
    mixed = (normed * gate_float).astype(jnp.bfloat16)
    lifted = dz_rows * gate_float
    attended_grad = (
        (
            lifted
            - jnp.mean(lifted, axis=1, keepdims=True)
            - normed * jnp.mean(lifted * normed, axis=1, keepdims=True)
        )
        * inverse
    ).astype(jnp.bfloat16)
    grad_heads = attended_grad.reshape(local_rows, head_count, head_dim)
    indicator_float = query_bucket_indicator.astype(jnp.float32)
    dp_size = lax.axis_size("dp")
    weight_term = lax.dot_general(
        mixed, grad_rows, (((0,), (0,)), ((), ())), preferred_element_type=jnp.float32
    )
    weight_plan = [("split", "dp", mask) for mask in axis_bits("dp")]
    weight_plan.append(("exchange", "ctx", 0))
    weight_state = [weight_term.reshape(dp_size, -1), 0]

    def slot(anchor):
        blocks, done = weight_state
        if done < len(weight_plan):
            blocks, anchor = lax.optimization_barrier((blocks, anchor))
            kind, axis, mask = weight_plan[done]
            if kind == "exchange":
                weight_state[0] = summed_by_exchange(blocks.reshape(-1), (axis,))
            else:
                weight_state[0] = plan_step(blocks, kind, axis, mask)
            weight_state[1] = done + 1
        return anchor

    query_sum = jnp.zeros((local_rows, width), jnp.float32)
    share_sum = None
    key_terms = [None, None, None]
    sent = [None, None, None]
    for distance in (2, 1, 0):
        visible, scores, weights, key_bucket_indicator = tiles[distance]
        pair = slot(window[distance])
        if distance == 0:
            sent[2], pair = lax.optimization_barrier((sent[2], pair))
        key_heads = pair[0].reshape(local_rows, head_count, head_dim)
        value_heads = pair[1].reshape(local_rows, head_count, head_dim)
        weight_grad = jnp.einsum(
            "ihd,jhd->hij", grad_heads, value_heads, preferred_element_type=jnp.float32
        )
        value_part = jnp.einsum(
            "hij,ihd->jhd", weights, grad_heads, preferred_element_type=jnp.float32
        ).reshape(local_rows, width)
        score_gradient = jnp.where(visible[None], weight_grad * silu_slope(scores), 0.0).astype(
            jnp.bfloat16
        )
        score_gradient = slot(score_gradient)
        query_part = jnp.einsum(
            "hij,jhd->ihd", score_gradient, key_heads, preferred_element_type=jnp.float32
        ).reshape(local_rows, width)
        key_part = (
            jnp.einsum(
                "hij,ihd->jhd", score_gradient, query_heads, preferred_element_type=jnp.float32
            ).reshape(local_rows, width)
            * scale
        )
        bucket_share_piece = jnp.einsum(
            "rmw,wx->rmx", score_gradient, key_bucket_indicator, preferred_element_type=jnp.float32
        )
        share_sum = bucket_share_piece if share_sum is None else share_sum + bucket_share_piece
        query_sum = query_sum + query_part
        key_terms[distance] = jnp.stack([key_part, value_part])
        if distance > 0:
            sent[distance] = passed_along(
                key_terms[distance].astype(jnp.bfloat16), "ctx", -distance
            )
    table_local = jnp.einsum(
        "qp,cqk->cpk", indicator_float, share_sum, precision=lax.Precision.HIGHEST
    )
    gathered = key_terms[0] + sent[1].astype(jnp.float32) + sent[2].astype(jnp.float32)
    query_grad = (query_sum * scale).astype(jnp.bfloat16)
    key_grad = gathered[0].astype(jnp.bfloat16)
    value_grad = gathered[1].astype(jnp.bfloat16)
    projection_grad = weight_state[0].reshape(width // dp_size, width)
    table_grad = summed_by_exchange(table_local.reshape(-1), ("ctx", "dp")).reshape(
        table_local.shape
    )
    return (
        query_grad[None],
        key_grad[None],
        value_grad[None],
        gate_grad[None],
        projection_grad,
        table_grad,
    )


def solution(mesh):
    return jax.shard_map(
        shards,
        mesh=mesh,
        in_specs=(
            P("dp", "ctx", None),
            P("dp", "ctx", None),
            P("dp", "ctx", None),
            P("dp", "ctx", None),
            P("dp", "ctx", None),
            P("dp", None),
            P("dp", None),
            P("dp", None, None),
            P(),
            P(),
        ),
        out_specs=(
            P("dp", "ctx", None),
            P("dp", "ctx", None),
            P("dp", "ctx", None),
            P("dp", "ctx", None),
            P("dp", None),
            P(),
        ),
        check_vma=False,
    )
```

```python
import jax
import jax.numpy as jnp
from jax import lax
from jax.sharding import PartitionSpec as P

BLK = 128


NORM_EPSILON = 1e-05


def passed_along(value, axis, by):
    length = lax.axis_size(axis)
    pairs = [(i, i + by) for i in range(length) if 0 <= i + by < length]
    return lax.ppermute(value, axis, pairs)


def exchanged(value, axis, mask):
    length = lax.axis_size(axis)
    pairs = [(i, i ^ mask) for i in range(length)]
    return lax.ppermute(value, axis, pairs)


def axis_bits(axis):
    length = lax.axis_size(axis)
    bits = []
    mask = 1
    while mask < length:
        bits.append(mask)
        mask *= 2
    return bits


def scatter_blocks(blocks, axis):
    index = lax.axis_index(axis)
    for mask in axis_bits(axis):
        bit = (index // mask) % 2
        pairs = blocks.reshape(blocks.shape[0] // 2, 2, blocks.shape[1])
        keep = lax.dynamic_index_in_dim(pairs, bit, axis=1, keepdims=False)
        send = lax.dynamic_index_in_dim(pairs, 1 - bit, axis=1, keepdims=False)
        blocks = keep + exchanged(send, axis, mask)
    return blocks[0]


def gather_blocks(chunk, axis):
    index = lax.axis_index(axis)
    held = chunk[None]
    for mask in reversed(axis_bits(axis)):
        bit = (index // mask) % 2
        other = exchanged(held, axis, mask)
        low = jnp.where(bit == 0, held, other)
        high = jnp.where(bit == 0, other, held)
        held = jnp.stack([low, high], axis=1).reshape(held.shape[0] * 2, held.shape[1])
    return held


def summed_over(flat, axis):
    size = lax.axis_size(axis)
    part = scatter_blocks(flat.reshape(size, flat.shape[0] // size), axis)
    return gather_blocks(part, axis).reshape(flat.shape)


def plan_step(blocks, kind, axis, mask):
    bit = (lax.axis_index(axis) // mask) % 2
    if kind == "split":
        if blocks.shape[0] == 1:
            blocks = blocks.reshape(2, -1)
        pairs = blocks.reshape(blocks.shape[0] // 2, 2, blocks.shape[1])
        keep = lax.dynamic_index_in_dim(pairs, bit, axis=1, keepdims=False)
        send = lax.dynamic_index_in_dim(pairs, 1 - bit, axis=1, keepdims=False)
        return keep + exchanged(send, axis, mask)
    other = exchanged(blocks, axis, mask)
    low = jnp.where(bit == 0, blocks, other)
    high = jnp.where(bit == 0, other, blocks)
    return jnp.concatenate([low, high], axis=1)


def summed_by_exchange(flat, axes):
    size = 1
    for axis in axes:
        size *= lax.axis_size(axis)
    pieces = lax.all_to_all(flat.reshape(size, -1), axes, 0, 0, tiled=True)
    total = jnp.sum(pieces, axis=0, keepdims=True)
    spread = jnp.broadcast_to(total, pieces.shape)
    return lax.all_to_all(spread, axes, 0, 0, tiled=True).reshape(flat.shape)


def silu_slope(scores):
    sigmoid = jax.nn.sigmoid(scores)
    return sigmoid * (1.0 + scores * (1.0 - sigmoid))


def expand_blocks(block_rows, block_size):
    return jnp.repeat(jnp.repeat(block_rows, block_size, axis=0), block_size, axis=1)


def shards(
    queries,
    keys,
    values,
    gates,
    out_grad,
    time_bucket,
    lengths,
    block_map,
    bucket_bias_matrix,
    w_out,
):
    query_rows = queries[0]
    key_rows = keys[0]
    value_rows = values[0]
    gate_rows = gates[0]
    grad_rows = out_grad[0]
    local_rows, width = query_rows.shape
    head_count = bucket_bias_matrix.shape[0]
    bucket_count = bucket_bias_matrix.shape[1]
    head_dim = width // head_count
    scale = head_dim ** (-0.5)
    blocks_here = local_rows // BLK
    cycle_index = lax.axis_index("ctx")
    row_start = cycle_index * local_rows
    offsets = jnp.cumsum(lengths[0], dtype=jnp.int32) - lengths[0]

    def segment_of(positions):
        return jnp.sum(
            (positions[:, None] >= offsets[None, 1:]).astype(jnp.int32), axis=1, dtype=jnp.int32
        )

    bucket_ids = jnp.arange(bucket_count, dtype=jnp.int32)
    query_pos = row_start + jnp.arange(local_rows, dtype=jnp.int32)
    query_seg = segment_of(query_pos)
    query_bucket = lax.dynamic_slice_in_dim(time_bucket[0], row_start, local_rows, 0)
    query_bucket_indicator = (query_bucket[:, None] == bucket_ids[None, :]).astype(jnp.bfloat16)
    bias_matrix_rows = jnp.einsum(
        "lf,sfq->slq",
        query_bucket_indicator,
        bucket_bias_matrix,
        preferred_element_type=jnp.float32,
    ).astype(jnp.bfloat16)
    map_rows = lax.dynamic_slice_in_dim(block_map[0], cycle_index * blocks_here, blocks_here, 0)
    query_heads = query_rows.reshape(local_rows, head_count, head_dim)
    stacked = jnp.stack([key_rows, value_rows])
    window = [stacked, passed_along(stacked, "ctx", 1), passed_along(stacked, "ctx", 2)]
    tiles = []
    attended = jnp.zeros((local_rows, head_count, head_dim), jnp.float32)
    for distance in range(3):
        key_first = row_start - distance * local_rows
        key_pos = key_first + jnp.arange(local_rows, dtype=jnp.int32)
        safe_first = jnp.maximum(key_first, 0)
        key_bucket = lax.dynamic_slice_in_dim(time_bucket[0], safe_first, local_rows, 0)
        key_bucket_indicator = (key_bucket[:, None] == bucket_ids[None, :]).astype(jnp.bfloat16)
        map_cols = lax.dynamic_slice_in_dim(map_rows, safe_first // BLK, blocks_here, 1)
        same_block = query_pos[:, None] // BLK == key_pos[None, :] // BLK
        key_visible = (
            (query_seg[:, None] == segment_of(key_pos)[None, :])
            & (key_pos[None, :] <= query_pos[:, None])
            & (key_pos[None, :] >= 0)
            & ((expand_blocks(map_cols, BLK) == 1) | same_block)
        )
        key_bias_terms = jnp.einsum(
            "vqx,px->vqp",
            bias_matrix_rows,
            key_bucket_indicator,
            preferred_element_type=jnp.float32,
        )
        visible, bias_terms, key_bucket_indicator = (
            key_visible,
            key_bias_terms,
            key_bucket_indicator,
        )
        forward_pair = window[distance]
        forward_key_heads = forward_pair[0].reshape(local_rows, head_count, head_dim)
        forward_value_heads = forward_pair[1].reshape(local_rows, head_count, head_dim)
        forward_scores = (
            jnp.einsum(
                "ihd,jhd->hij", query_heads, forward_key_heads, preferred_element_type=jnp.float32
            )
            * scale
            + bias_terms
        )
        forward_weights = jnp.where(visible[None], jax.nn.silu(forward_scores), 0.0).astype(
            jnp.bfloat16
        )
        attended_part = jnp.einsum(
            "hij,jhd->ihd", forward_weights, forward_value_heads, preferred_element_type=jnp.float32
        )
        attended = attended + attended_part
        tiles.append((visible, forward_scores, forward_weights, key_bucket_indicator))
    attended = attended.reshape(local_rows, width)
    centered = attended - jnp.mean(attended, axis=1, keepdims=True)
    inverse = lax.rsqrt(jnp.mean(centered * centered, axis=1, keepdims=True) + NORM_EPSILON)
    normed = centered * inverse
    dz_rows = lax.dot_general(
        grad_rows, w_out, (((1,), (1,)), ((), ())), preferred_element_type=jnp.float32
    )
    gate_float = gate_rows.astype(jnp.float32)
    gate_grad = (dz_rows * normed).astype(jnp.bfloat16)
    mixed = (normed * gate_float).astype(jnp.bfloat16)
    lifted = dz_rows * gate_float
    attended_grad = (
        (
            lifted
            - jnp.mean(lifted, axis=1, keepdims=True)
            - normed * jnp.mean(lifted * normed, axis=1, keepdims=True)
        )
        * inverse
    ).astype(jnp.bfloat16)
    grad_heads = attended_grad.reshape(local_rows, head_count, head_dim)
    indicator_float = query_bucket_indicator.astype(jnp.float32)
    dp_size = lax.axis_size("dp")
    weight_term = lax.dot_general(
        mixed, grad_rows, (((0,), (0,)), ((), ())), preferred_element_type=jnp.float32
    )
    weight_plan = [("split", "dp", mask) for mask in axis_bits("dp")]
    weight_plan.append(("exchange", "ctx", 0))
    weight_state = [weight_term.reshape(dp_size, -1), 0]

    def slot(anchor):
        blocks, done = weight_state
        if done < len(weight_plan):
            blocks, anchor = lax.optimization_barrier((blocks, anchor))
            kind, axis, mask = weight_plan[done]
            if kind == "exchange":
                weight_state[0] = summed_by_exchange(blocks.reshape(-1), (axis,))
            else:
                weight_state[0] = plan_step(blocks, kind, axis, mask)
            weight_state[1] = done + 1
        return anchor

    query_sum = jnp.zeros((local_rows, width), jnp.float32)
    share_sum = None
    key_terms = [None, None, None]
    sent = [None, None, None]
    held = [None, None, None]
    for distance in (2, 1, 0):
        visible, scores, weights, key_bucket_indicator = tiles[distance]
        pair = slot(window[distance])
        value_heads = pair[1].reshape(local_rows, head_count, head_dim)
        weight_grad = jnp.einsum(
            "ihd,jhd->hij", grad_heads, value_heads, preferred_element_type=jnp.float32
        )
        score_gradient = jnp.where(visible[None], weight_grad * silu_slope(scores), 0.0).astype(
            jnp.bfloat16
        )
        score_gradient = slot(score_gradient)
        bucket_share_piece = jnp.einsum(
            "rmw,wx->rmx", score_gradient, key_bucket_indicator, preferred_element_type=jnp.float32
        )
        share_sum = bucket_share_piece if share_sum is None else share_sum + bucket_share_piece
        held[distance] = (score_gradient, pair)
    table_local = jnp.einsum(
        "qp,cqk->cpk", indicator_float, share_sum, precision=lax.Precision.HIGHEST
    )
    table_grad = summed_by_exchange(table_local.reshape(-1), ("ctx", "dp")).reshape(
        table_local.shape
    )
    for distance in (2, 1, 0):
        weights = tiles[distance][2]
        score_gradient, pair = held[distance]
        key_heads = pair[0].reshape(local_rows, head_count, head_dim)
        value_part = jnp.einsum(
            "hij,ihd->jhd", weights, grad_heads, preferred_element_type=jnp.float32
        ).reshape(local_rows, width)
        query_part = jnp.einsum(
            "hij,jhd->ihd", score_gradient, key_heads, preferred_element_type=jnp.float32
        ).reshape(local_rows, width)
        key_part = (
            jnp.einsum(
                "hij,ihd->jhd", score_gradient, query_heads, preferred_element_type=jnp.float32
            ).reshape(local_rows, width)
            * scale
        )
        query_sum = query_sum + query_part
        key_terms[distance] = jnp.stack([key_part, value_part])
        if distance > 0:
            sent[distance] = passed_along(
                key_terms[distance].astype(jnp.bfloat16), "ctx", -distance
            )
    gathered = key_terms[0] + sent[1].astype(jnp.float32) + sent[2].astype(jnp.float32)
    query_grad = (query_sum * scale).astype(jnp.bfloat16)
    key_grad = gathered[0].astype(jnp.bfloat16)
    value_grad = gathered[1].astype(jnp.bfloat16)
    projection_grad = weight_state[0].reshape(width // dp_size, width)
    return (
        query_grad[None],
        key_grad[None],
        value_grad[None],
        gate_grad[None],
        projection_grad,
        table_grad,
    )


def solution(mesh):
    return jax.shard_map(
        shards,
        mesh=mesh,
        in_specs=(
            P("dp", "ctx", None),
            P("dp", "ctx", None),
            P("dp", "ctx", None),
            P("dp", "ctx", None),
            P("dp", "ctx", None),
            P("dp", None),
            P("dp", None),
            P("dp", None, None),
            P(),
            P(),
        ),
        out_specs=(
            P("dp", "ctx", None),
            P("dp", "ctx", None),
            P("dp", "ctx", None),
            P("dp", "ctx", None),
            P("dp", None),
            P(),
        ),
        check_vma=False,
    )
```

```python
import jax
import jax.numpy as jnp
from jax import lax
from jax.sharding import PartitionSpec as P

BLK = 128


NORM_EPSILON = 1e-05


def passed_along(value, axis, by):
    length = lax.axis_size(axis)
    pairs = [(i, i + by) for i in range(length) if 0 <= i + by < length]
    return lax.ppermute(value, axis, pairs)


def exchanged(value, axis, mask):
    length = lax.axis_size(axis)
    pairs = [(i, i ^ mask) for i in range(length)]
    return lax.ppermute(value, axis, pairs)


def axis_bits(axis):
    length = lax.axis_size(axis)
    bits = []
    mask = 1
    while mask < length:
        bits.append(mask)
        mask *= 2
    return bits


def scatter_blocks(blocks, axis):
    index = lax.axis_index(axis)
    for mask in axis_bits(axis):
        bit = (index // mask) % 2
        pairs = blocks.reshape(blocks.shape[0] // 2, 2, blocks.shape[1])
        keep = lax.dynamic_index_in_dim(pairs, bit, axis=1, keepdims=False)
        send = lax.dynamic_index_in_dim(pairs, 1 - bit, axis=1, keepdims=False)
        blocks = keep + exchanged(send, axis, mask)
    return blocks[0]


def gather_blocks(chunk, axis):
    index = lax.axis_index(axis)
    held = chunk[None]
    for mask in reversed(axis_bits(axis)):
        bit = (index // mask) % 2
        other = exchanged(held, axis, mask)
        low = jnp.where(bit == 0, held, other)
        high = jnp.where(bit == 0, other, held)
        held = jnp.stack([low, high], axis=1).reshape(held.shape[0] * 2, held.shape[1])
    return held


def summed_over(flat, axis):
    size = lax.axis_size(axis)
    part = scatter_blocks(flat.reshape(size, flat.shape[0] // size), axis)
    return gather_blocks(part, axis).reshape(flat.shape)


def plan_step(blocks, kind, axis, mask):
    bit = (lax.axis_index(axis) // mask) % 2
    if kind == "split":
        if blocks.shape[0] == 1:
            blocks = blocks.reshape(2, -1)
        pairs = blocks.reshape(blocks.shape[0] // 2, 2, blocks.shape[1])
        keep = lax.dynamic_index_in_dim(pairs, bit, axis=1, keepdims=False)
        send = lax.dynamic_index_in_dim(pairs, 1 - bit, axis=1, keepdims=False)
        return keep + exchanged(send, axis, mask)
    other = exchanged(blocks, axis, mask)
    low = jnp.where(bit == 0, blocks, other)
    high = jnp.where(bit == 0, other, blocks)
    return jnp.concatenate([low, high], axis=1)


def summed_by_exchange(flat, axes):
    size = 1
    for axis in axes:
        size *= lax.axis_size(axis)
    pieces = lax.all_to_all(flat.reshape(size, -1), axes, 0, 0, tiled=True)
    total = jnp.sum(pieces, axis=0, keepdims=True)
    spread = jnp.broadcast_to(total, pieces.shape)
    return lax.all_to_all(spread, axes, 0, 0, tiled=True).reshape(flat.shape)


def silu_slope(scores):
    sigmoid = jax.nn.sigmoid(scores)
    return sigmoid * (1.0 + scores * (1.0 - sigmoid))


def expand_blocks(block_rows, block_size):
    return jnp.repeat(jnp.repeat(block_rows, block_size, axis=0), block_size, axis=1)


def shards(
    queries,
    keys,
    values,
    gates,
    out_grad,
    time_bucket,
    lengths,
    block_map,
    bucket_bias_matrix,
    w_out,
):
    query_rows = queries[0]
    key_rows = keys[0]
    value_rows = values[0]
    gate_rows = gates[0]
    grad_rows = out_grad[0]
    local_rows, width = query_rows.shape
    head_count = bucket_bias_matrix.shape[0]
    bucket_count = bucket_bias_matrix.shape[1]
    head_dim = width // head_count
    scale = head_dim ** (-0.5)
    blocks_here = local_rows // BLK
    cycle_index = lax.axis_index("ctx")
    row_start = cycle_index * local_rows
    offsets = jnp.cumsum(lengths[0], dtype=jnp.int32) - lengths[0]

    def segment_of(positions):
        return jnp.sum(
            (positions[:, None] >= offsets[None, 1:]).astype(jnp.int32), axis=1, dtype=jnp.int32
        )

    bucket_ids = jnp.arange(bucket_count, dtype=jnp.int32)
    query_pos = row_start + jnp.arange(local_rows, dtype=jnp.int32)
    query_seg = segment_of(query_pos)
    query_bucket = lax.dynamic_slice_in_dim(time_bucket[0], row_start, local_rows, 0)
    query_bucket_indicator = (query_bucket[:, None] == bucket_ids[None, :]).astype(jnp.bfloat16)
    bias_matrix_rows = jnp.einsum(
        "lf,sfq->slq",
        query_bucket_indicator,
        bucket_bias_matrix,
        preferred_element_type=jnp.float32,
    ).astype(jnp.bfloat16)
    map_rows = lax.dynamic_slice_in_dim(block_map[0], cycle_index * blocks_here, blocks_here, 0)
    query_heads = query_rows.reshape(local_rows, head_count, head_dim)
    stacked = jnp.stack([key_rows, value_rows])
    window = [stacked, passed_along(stacked, "ctx", 1), passed_along(stacked, "ctx", 2)]
    tiles = []
    attended = jnp.zeros((local_rows, head_count, head_dim), jnp.float32)
    for distance in range(3):
        key_first = row_start - distance * local_rows
        key_pos = key_first + jnp.arange(local_rows, dtype=jnp.int32)
        safe_first = jnp.maximum(key_first, 0)
        key_bucket = lax.dynamic_slice_in_dim(time_bucket[0], safe_first, local_rows, 0)
        key_bucket_indicator = (key_bucket[:, None] == bucket_ids[None, :]).astype(jnp.bfloat16)
        map_cols = lax.dynamic_slice_in_dim(map_rows, safe_first // BLK, blocks_here, 1)
        same_block = query_pos[:, None] // BLK == key_pos[None, :] // BLK
        key_visible = (
            (query_seg[:, None] == segment_of(key_pos)[None, :])
            & (key_pos[None, :] <= query_pos[:, None])
            & (key_pos[None, :] >= 0)
            & ((expand_blocks(map_cols, BLK) == 1) | same_block)
        )
        key_bias_terms = jnp.einsum(
            "vqx,px->vqp",
            bias_matrix_rows,
            key_bucket_indicator,
            preferred_element_type=jnp.float32,
        )
        visible, bias_terms, key_bucket_indicator = (
            key_visible,
            key_bias_terms,
            key_bucket_indicator,
        )
        forward_pair = window[distance]
        forward_key_heads = forward_pair[0].reshape(local_rows, head_count, head_dim)
        forward_value_heads = forward_pair[1].reshape(local_rows, head_count, head_dim)
        forward_scores = (
            jnp.einsum(
                "ihd,jhd->hij", query_heads, forward_key_heads, preferred_element_type=jnp.float32
            )
            * scale
            + bias_terms
        )
        forward_weights = jnp.where(visible[None], jax.nn.silu(forward_scores), 0.0).astype(
            jnp.bfloat16
        )
        attended_part = jnp.einsum(
            "hij,jhd->ihd", forward_weights, forward_value_heads, preferred_element_type=jnp.float32
        )
        attended = attended + attended_part
        tiles.append((visible, forward_scores, forward_weights, key_bucket_indicator))
    attended = attended.reshape(local_rows, width)
    centered = attended - jnp.mean(attended, axis=1, keepdims=True)
    inverse = lax.rsqrt(jnp.mean(centered * centered, axis=1, keepdims=True) + NORM_EPSILON)
    normed = centered * inverse
    dz_rows = lax.dot_general(
        grad_rows, w_out, (((1,), (1,)), ((), ())), preferred_element_type=jnp.float32
    )
    gate_float = gate_rows.astype(jnp.float32)
    gate_grad = (dz_rows * normed).astype(jnp.bfloat16)
    mixed = (normed * gate_float).astype(jnp.bfloat16)
    lifted = dz_rows * gate_float
    attended_grad = (
        (
            lifted
            - jnp.mean(lifted, axis=1, keepdims=True)
            - normed * jnp.mean(lifted * normed, axis=1, keepdims=True)
        )
        * inverse
    ).astype(jnp.bfloat16)
    grad_heads = attended_grad.reshape(local_rows, head_count, head_dim)
    indicator_float = query_bucket_indicator.astype(jnp.float32)
    dp_size = lax.axis_size("dp")
    weight_term = lax.dot_general(
        mixed, grad_rows, (((0,), (0,)), ((), ())), preferred_element_type=jnp.float32
    )
    weight_plan = [("split", "dp", mask) for mask in axis_bits("dp")]
    weight_plan += [("split", "ctx", mask) for mask in axis_bits("ctx")]
    weight_plan += [("join", "ctx", mask) for mask in reversed(axis_bits("ctx"))]
    weight_state = [weight_term.reshape(dp_size, -1), 0]

    def slot(anchor, tied=True):
        blocks, done = weight_state
        if done < len(weight_plan):
            if tied:
                blocks, anchor = lax.optimization_barrier((blocks, anchor))
            kind, axis, mask = weight_plan[done]
            if kind == "exchange":
                weight_state[0] = summed_by_exchange(blocks.reshape(-1), (axis,))
            else:
                weight_state[0] = plan_step(blocks, kind, axis, mask)
            weight_state[1] = done + 1
        return anchor

    query_sum = jnp.zeros((local_rows, width), jnp.float32)
    share_sum = None
    key_terms = [None, None, None]
    sent = [None, None, None]
    for distance in (2, 1, 0):
        visible, scores, weights, key_bucket_indicator = tiles[distance]
        pair = slot(window[distance])
        if distance == 0:
            sent[2], pair = lax.optimization_barrier((sent[2], pair))
        key_heads = pair[0].reshape(local_rows, head_count, head_dim)
        value_heads = pair[1].reshape(local_rows, head_count, head_dim)
        weight_grad = jnp.einsum(
            "ihd,jhd->hij", grad_heads, value_heads, preferred_element_type=jnp.float32
        )
        value_part = jnp.einsum(
            "hij,ihd->jhd", weights, grad_heads, preferred_element_type=jnp.float32
        ).reshape(local_rows, width)
        score_gradient = jnp.where(visible[None], weight_grad * silu_slope(scores), 0.0).astype(
            jnp.bfloat16
        )
        score_gradient = slot(score_gradient)
        query_part = jnp.einsum(
            "hij,jhd->ihd", score_gradient, key_heads, preferred_element_type=jnp.float32
        ).reshape(local_rows, width)
        key_part = (
            jnp.einsum(
                "hij,ihd->jhd", score_gradient, query_heads, preferred_element_type=jnp.float32
            ).reshape(local_rows, width)
            * scale
        )
        bucket_share_piece = jnp.einsum(
            "rmw,wx->rmx", score_gradient, key_bucket_indicator, preferred_element_type=jnp.float32
        )
        share_sum = bucket_share_piece if share_sum is None else share_sum + bucket_share_piece
        query_sum = query_sum + query_part
        key_terms[distance] = jnp.stack([key_part, value_part])
        if distance > 0:
            sent[distance] = passed_along(
                key_terms[distance].astype(jnp.bfloat16), "ctx", -distance
            )
    table_local = jnp.einsum(
        "qp,cqk->cpk", indicator_float, share_sum, precision=lax.Precision.HIGHEST
    )
    while weight_state[1] < len(weight_plan):
        slot(None, tied=False)
    gathered = key_terms[0] + sent[1].astype(jnp.float32) + sent[2].astype(jnp.float32)
    query_grad = (query_sum * scale).astype(jnp.bfloat16)
    key_grad = gathered[0].astype(jnp.bfloat16)
    value_grad = gathered[1].astype(jnp.bfloat16)
    projection_grad = weight_state[0].reshape(width // dp_size, width)
    table_grad = summed_by_exchange(table_local.reshape(-1), ("ctx", "dp")).reshape(
        table_local.shape
    )
    return (
        query_grad[None],
        key_grad[None],
        value_grad[None],
        gate_grad[None],
        projection_grad,
        table_grad,
    )


def solution(mesh):
    return jax.shard_map(
        shards,
        mesh=mesh,
        in_specs=(
            P("dp", "ctx", None),
            P("dp", "ctx", None),
            P("dp", "ctx", None),
            P("dp", "ctx", None),
            P("dp", "ctx", None),
            P("dp", None),
            P("dp", None),
            P("dp", None, None),
            P(),
            P(),
        ),
        out_specs=(
            P("dp", "ctx", None),
            P("dp", "ctx", None),
            P("dp", "ctx", None),
            P("dp", "ctx", None),
            P("dp", None),
            P(),
        ),
        check_vma=False,
    )
```

```python
import jax
import jax.numpy as jnp
from jax import lax
from jax.sharding import PartitionSpec as P

BLK = 128


NORM_EPSILON = 1e-05


def passed_along(value, axis, by):
    length = lax.axis_size(axis)
    pairs = [(i, i + by) for i in range(length) if 0 <= i + by < length]
    return lax.ppermute(value, axis, pairs)


def exchanged(value, axis, mask):
    length = lax.axis_size(axis)
    pairs = [(i, i ^ mask) for i in range(length)]
    return lax.ppermute(value, axis, pairs)


def axis_bits(axis):
    length = lax.axis_size(axis)
    bits = []
    mask = 1
    while mask < length:
        bits.append(mask)
        mask *= 2
    return bits


def scatter_blocks(blocks, axis):
    index = lax.axis_index(axis)
    for mask in axis_bits(axis):
        bit = (index // mask) % 2
        pairs = blocks.reshape(blocks.shape[0] // 2, 2, blocks.shape[1])
        keep = lax.dynamic_index_in_dim(pairs, bit, axis=1, keepdims=False)
        send = lax.dynamic_index_in_dim(pairs, 1 - bit, axis=1, keepdims=False)
        blocks = keep + exchanged(send, axis, mask)
    return blocks[0]


def gather_blocks(chunk, axis):
    index = lax.axis_index(axis)
    held = chunk[None]
    for mask in reversed(axis_bits(axis)):
        bit = (index // mask) % 2
        other = exchanged(held, axis, mask)
        low = jnp.where(bit == 0, held, other)
        high = jnp.where(bit == 0, other, held)
        held = jnp.stack([low, high], axis=1).reshape(held.shape[0] * 2, held.shape[1])
    return held


def summed_over(flat, axis):
    size = lax.axis_size(axis)
    part = scatter_blocks(flat.reshape(size, flat.shape[0] // size), axis)
    return gather_blocks(part, axis).reshape(flat.shape)


def plan_step(blocks, kind, axis, mask):
    bit = (lax.axis_index(axis) // mask) % 2
    if kind == "split":
        if blocks.shape[0] == 1:
            blocks = blocks.reshape(2, -1)
        pairs = blocks.reshape(blocks.shape[0] // 2, 2, blocks.shape[1])
        keep = lax.dynamic_index_in_dim(pairs, bit, axis=1, keepdims=False)
        send = lax.dynamic_index_in_dim(pairs, 1 - bit, axis=1, keepdims=False)
        return keep + exchanged(send, axis, mask)
    other = exchanged(blocks, axis, mask)
    low = jnp.where(bit == 0, blocks, other)
    high = jnp.where(bit == 0, other, blocks)
    return jnp.concatenate([low, high], axis=1)


def summed_by_exchange(flat, axes):
    size = 1
    for axis in axes:
        size *= lax.axis_size(axis)
    pieces = lax.all_to_all(flat.reshape(size, -1), axes, 0, 0, tiled=True)
    total = jnp.sum(pieces, axis=0, keepdims=True)
    spread = jnp.broadcast_to(total, pieces.shape)
    return lax.all_to_all(spread, axes, 0, 0, tiled=True).reshape(flat.shape)


def silu_slope(scores):
    sigmoid = jax.nn.sigmoid(scores)
    return sigmoid * (1.0 + scores * (1.0 - sigmoid))


def expand_blocks(block_rows, block_size):
    return jnp.repeat(jnp.repeat(block_rows, block_size, axis=0), block_size, axis=1)


def shards(
    queries,
    keys,
    values,
    gates,
    out_grad,
    time_bucket,
    lengths,
    block_map,
    bucket_bias_matrix,
    w_out,
):
    query_rows = queries[0]
    key_rows = keys[0]
    value_rows = values[0]
    gate_rows = gates[0]
    grad_rows = out_grad[0]
    local_rows, width = query_rows.shape
    head_count = bucket_bias_matrix.shape[0]
    bucket_count = bucket_bias_matrix.shape[1]
    head_dim = width // head_count
    scale = head_dim ** (-0.5)
    blocks_here = local_rows // BLK
    cycle_index = lax.axis_index("ctx")
    row_start = cycle_index * local_rows
    offsets = jnp.cumsum(lengths[0], dtype=jnp.int32) - lengths[0]

    def segment_of(positions):
        return jnp.sum(
            (positions[:, None] >= offsets[None, 1:]).astype(jnp.int32), axis=1, dtype=jnp.int32
        )

    bucket_ids = jnp.arange(bucket_count, dtype=jnp.int32)
    query_pos = row_start + jnp.arange(local_rows, dtype=jnp.int32)
    query_seg = segment_of(query_pos)
    query_bucket = lax.dynamic_slice_in_dim(time_bucket[0], row_start, local_rows, 0)
    query_bucket_indicator = (query_bucket[:, None] == bucket_ids[None, :]).astype(jnp.bfloat16)
    bias_matrix_rows = jnp.einsum(
        "lf,sfq->slq",
        query_bucket_indicator,
        bucket_bias_matrix,
        preferred_element_type=jnp.float32,
    ).astype(jnp.bfloat16)
    map_rows = lax.dynamic_slice_in_dim(block_map[0], cycle_index * blocks_here, blocks_here, 0)
    query_heads = query_rows.reshape(local_rows, head_count, head_dim)
    stacked = jnp.stack([key_rows, value_rows])
    window = [stacked, passed_along(stacked, "ctx", 1), passed_along(stacked, "ctx", 2)]
    tiles = []
    attended = jnp.zeros((local_rows, head_count, head_dim), jnp.float32)
    for distance in range(3):
        key_first = row_start - distance * local_rows
        key_pos = key_first + jnp.arange(local_rows, dtype=jnp.int32)
        safe_first = jnp.maximum(key_first, 0)
        key_bucket = lax.dynamic_slice_in_dim(time_bucket[0], safe_first, local_rows, 0)
        key_bucket_indicator = (key_bucket[:, None] == bucket_ids[None, :]).astype(jnp.bfloat16)
        map_cols = lax.dynamic_slice_in_dim(map_rows, safe_first // BLK, blocks_here, 1)
        same_block = query_pos[:, None] // BLK == key_pos[None, :] // BLK
        key_visible = (
            (query_seg[:, None] == segment_of(key_pos)[None, :])
            & (key_pos[None, :] <= query_pos[:, None])
            & (key_pos[None, :] >= 0)
            & ((expand_blocks(map_cols, BLK) == 1) | same_block)
        )
        key_bias_terms = jnp.einsum(
            "vqx,px->vqp",
            bias_matrix_rows,
            key_bucket_indicator,
            preferred_element_type=jnp.float32,
        )
        visible, bias_terms, key_bucket_indicator = (
            key_visible,
            key_bias_terms,
            key_bucket_indicator,
        )
        forward_pair = window[distance]
        forward_key_heads = forward_pair[0].reshape(local_rows, head_count, head_dim)
        forward_value_heads = forward_pair[1].reshape(local_rows, head_count, head_dim)
        forward_scores = (
            jnp.einsum(
                "ihd,jhd->hij", query_heads, forward_key_heads, preferred_element_type=jnp.float32
            )
            * scale
            + bias_terms
        )
        forward_weights = jnp.where(visible[None], jax.nn.silu(forward_scores), 0.0).astype(
            jnp.bfloat16
        )
        attended_part = jnp.einsum(
            "hij,jhd->ihd", forward_weights, forward_value_heads, preferred_element_type=jnp.float32
        )
        attended = attended + attended_part
        tiles.append((visible, forward_scores, forward_weights, key_bucket_indicator))
    attended = attended.reshape(local_rows, width)
    centered = attended - jnp.mean(attended, axis=1, keepdims=True)
    inverse = lax.rsqrt(jnp.mean(centered * centered, axis=1, keepdims=True) + NORM_EPSILON)
    normed = centered * inverse
    dz_rows = lax.dot_general(
        grad_rows, w_out, (((1,), (1,)), ((), ())), preferred_element_type=jnp.float32
    )
    gate_float = gate_rows.astype(jnp.float32)
    gate_grad = (dz_rows * normed).astype(jnp.bfloat16)
    mixed = (normed * gate_float).astype(jnp.bfloat16)
    lifted = dz_rows * gate_float
    attended_grad = (
        (
            lifted
            - jnp.mean(lifted, axis=1, keepdims=True)
            - normed * jnp.mean(lifted * normed, axis=1, keepdims=True)
        )
        * inverse
    ).astype(jnp.bfloat16)
    grad_heads = attended_grad.reshape(local_rows, head_count, head_dim)
    indicator_float = query_bucket_indicator.astype(jnp.float32)
    dp_size = lax.axis_size("dp")
    weight_term = lax.dot_general(
        mixed, grad_rows, (((0,), (0,)), ((), ())), preferred_element_type=jnp.float32
    )
    weight_plan = [("split", "dp", mask) for mask in axis_bits("dp")]
    weight_state = [weight_term.reshape(dp_size, -1), 0]

    def slot(anchor):
        blocks, done = weight_state
        if done < len(weight_plan):
            blocks, anchor = lax.optimization_barrier((blocks, anchor))
            kind, axis, mask = weight_plan[done]
            if kind == "exchange":
                weight_state[0] = summed_by_exchange(blocks.reshape(-1), (axis,))
            else:
                weight_state[0] = plan_step(blocks, kind, axis, mask)
            weight_state[1] = done + 1
        return anchor

    query_sum = jnp.zeros((local_rows, width), jnp.float32)
    share_sum = None
    key_terms = [None, None, None]
    sent = [None, None, None]
    for distance in (2, 1, 0):
        visible, scores, weights, key_bucket_indicator = tiles[distance]
        pair = slot(window[distance])
        if distance == 0:
            sent[2], pair = lax.optimization_barrier((sent[2], pair))
        key_heads = pair[0].reshape(local_rows, head_count, head_dim)
        value_heads = pair[1].reshape(local_rows, head_count, head_dim)
        weight_grad = jnp.einsum(
            "ihd,jhd->hij", grad_heads, value_heads, preferred_element_type=jnp.float32
        )
        value_part = jnp.einsum(
            "hij,ihd->jhd", weights, grad_heads, preferred_element_type=jnp.float32
        ).reshape(local_rows, width)
        score_gradient = jnp.where(visible[None], weight_grad * silu_slope(scores), 0.0).astype(
            jnp.bfloat16
        )
        score_gradient = slot(score_gradient)
        query_part = jnp.einsum(
            "hij,jhd->ihd", score_gradient, key_heads, preferred_element_type=jnp.float32
        ).reshape(local_rows, width)
        key_part = (
            jnp.einsum(
                "hij,ihd->jhd", score_gradient, query_heads, preferred_element_type=jnp.float32
            ).reshape(local_rows, width)
            * scale
        )
        bucket_share_piece = jnp.einsum(
            "rmw,wx->rmx", score_gradient, key_bucket_indicator, preferred_element_type=jnp.float32
        )
        share_sum = bucket_share_piece if share_sum is None else share_sum + bucket_share_piece
        query_sum = query_sum + query_part
        key_terms[distance] = jnp.stack([key_part, value_part])
        if distance > 0:
            sent[distance] = passed_along(
                key_terms[distance].astype(jnp.bfloat16), "ctx", -distance
            )
    table_local = jnp.einsum(
        "qp,cqk->cpk", indicator_float, share_sum, precision=lax.Precision.HIGHEST
    )
    table_part = scatter_blocks(table_local.reshape(dp_size, -1), "dp")
    weight_rows = weight_state[0].reshape(-1)
    combined = summed_by_exchange(jnp.concatenate([weight_rows, table_part]), ("ctx",))
    projection_grad = combined[: weight_rows.shape[0]].reshape(width // dp_size, width)
    table_grad = gather_blocks(combined[weight_rows.shape[0] :], "dp").reshape(table_local.shape)
    gathered = key_terms[0] + sent[1].astype(jnp.float32) + sent[2].astype(jnp.float32)
    query_grad = (query_sum * scale).astype(jnp.bfloat16)
    key_grad = gathered[0].astype(jnp.bfloat16)
    value_grad = gathered[1].astype(jnp.bfloat16)
    return (
        query_grad[None],
        key_grad[None],
        value_grad[None],
        gate_grad[None],
        projection_grad,
        table_grad,
    )


def solution(mesh):
    return jax.shard_map(
        shards,
        mesh=mesh,
        in_specs=(
            P("dp", "ctx", None),
            P("dp", "ctx", None),
            P("dp", "ctx", None),
            P("dp", "ctx", None),
            P("dp", "ctx", None),
            P("dp", None),
            P("dp", None),
            P("dp", None, None),
            P(),
            P(),
        ),
        out_specs=(
            P("dp", "ctx", None),
            P("dp", "ctx", None),
            P("dp", "ctx", None),
            P("dp", "ctx", None),
            P("dp", None),
            P(),
        ),
        check_vma=False,
    )
```

```python
import jax
import jax.numpy as jnp
from jax import lax
from jax.sharding import PartitionSpec as P

BLK = 128


NORM_EPSILON = 1e-05


def passed_along(value, axis, by):
    length = lax.axis_size(axis)
    pairs = [(i, i + by) for i in range(length) if 0 <= i + by < length]
    return lax.ppermute(value, axis, pairs)


def exchanged(value, axis, mask):
    length = lax.axis_size(axis)
    pairs = [(i, i ^ mask) for i in range(length)]
    return lax.ppermute(value, axis, pairs)


def axis_bits(axis):
    length = lax.axis_size(axis)
    bits = []
    mask = 1
    while mask < length:
        bits.append(mask)
        mask *= 2
    return bits


def scatter_blocks(blocks, axis):
    index = lax.axis_index(axis)
    for mask in axis_bits(axis):
        bit = (index // mask) % 2
        pairs = blocks.reshape(blocks.shape[0] // 2, 2, blocks.shape[1])
        keep = lax.dynamic_index_in_dim(pairs, bit, axis=1, keepdims=False)
        send = lax.dynamic_index_in_dim(pairs, 1 - bit, axis=1, keepdims=False)
        blocks = keep + exchanged(send, axis, mask)
    return blocks[0]


def gather_blocks(chunk, axis):
    index = lax.axis_index(axis)
    held = chunk[None]
    for mask in reversed(axis_bits(axis)):
        bit = (index // mask) % 2
        other = exchanged(held, axis, mask)
        low = jnp.where(bit == 0, held, other)
        high = jnp.where(bit == 0, other, held)
        held = jnp.stack([low, high], axis=1).reshape(held.shape[0] * 2, held.shape[1])
    return held


def summed_over(flat, axis):
    size = lax.axis_size(axis)
    part = scatter_blocks(flat.reshape(size, flat.shape[0] // size), axis)
    return gather_blocks(part, axis).reshape(flat.shape)


def plan_step(blocks, kind, axis, mask):
    bit = (lax.axis_index(axis) // mask) % 2
    if kind == "split":
        if blocks.shape[0] == 1:
            blocks = blocks.reshape(2, -1)
        pairs = blocks.reshape(blocks.shape[0] // 2, 2, blocks.shape[1])
        keep = lax.dynamic_index_in_dim(pairs, bit, axis=1, keepdims=False)
        send = lax.dynamic_index_in_dim(pairs, 1 - bit, axis=1, keepdims=False)
        return keep + exchanged(send, axis, mask)
    other = exchanged(blocks, axis, mask)
    low = jnp.where(bit == 0, blocks, other)
    high = jnp.where(bit == 0, other, blocks)
    return jnp.concatenate([low, high], axis=1)


def summed_by_exchange(flat, axes):
    size = 1
    for axis in axes:
        size *= lax.axis_size(axis)
    pieces = lax.all_to_all(flat.reshape(size, -1), axes, 0, 0, tiled=True)
    total = jnp.sum(pieces, axis=0, keepdims=True)
    spread = jnp.broadcast_to(total, pieces.shape)
    return lax.all_to_all(spread, axes, 0, 0, tiled=True).reshape(flat.shape)


def silu_slope(scores):
    sigmoid = jax.nn.sigmoid(scores)
    return sigmoid * (1.0 + scores * (1.0 - sigmoid))


def expand_blocks(block_rows, block_size):
    return jnp.repeat(jnp.repeat(block_rows, block_size, axis=0), block_size, axis=1)


def shards(
    queries,
    keys,
    values,
    gates,
    out_grad,
    time_bucket,
    lengths,
    block_map,
    bucket_bias_matrix,
    w_out,
):
    query_rows = queries[0]
    key_rows = keys[0]
    value_rows = values[0]
    gate_rows = gates[0]
    grad_rows = out_grad[0]
    local_rows, width = query_rows.shape
    head_count = bucket_bias_matrix.shape[0]
    bucket_count = bucket_bias_matrix.shape[1]
    head_dim = width // head_count
    scale = head_dim ** (-0.5)
    blocks_here = local_rows // BLK
    cycle_index = lax.axis_index("ctx")
    row_start = cycle_index * local_rows
    offsets = jnp.cumsum(lengths[0], dtype=jnp.int32) - lengths[0]

    def segment_of(positions):
        return jnp.sum(
            (positions[:, None] >= offsets[None, 1:]).astype(jnp.int32), axis=1, dtype=jnp.int32
        )

    bucket_ids = jnp.arange(bucket_count, dtype=jnp.int32)
    query_pos = row_start + jnp.arange(local_rows, dtype=jnp.int32)
    query_seg = segment_of(query_pos)
    query_bucket = lax.dynamic_slice_in_dim(time_bucket[0], row_start, local_rows, 0)
    query_bucket_indicator = (query_bucket[:, None] == bucket_ids[None, :]).astype(jnp.bfloat16)
    bias_matrix_rows = jnp.einsum(
        "lf,sfq->slq",
        query_bucket_indicator,
        bucket_bias_matrix,
        preferred_element_type=jnp.float32,
    ).astype(jnp.bfloat16)
    map_rows = lax.dynamic_slice_in_dim(block_map[0], cycle_index * blocks_here, blocks_here, 0)
    query_heads = query_rows.reshape(local_rows, head_count, head_dim)
    stacked = jnp.stack([key_rows, value_rows])
    window = [stacked, passed_along(stacked, "ctx", 1), passed_along(stacked, "ctx", 2)]
    tiles = []
    attended = jnp.zeros((local_rows, head_count, head_dim), jnp.float32)
    for distance in range(3):
        key_first = row_start - distance * local_rows
        key_pos = key_first + jnp.arange(local_rows, dtype=jnp.int32)
        safe_first = jnp.maximum(key_first, 0)
        key_bucket = lax.dynamic_slice_in_dim(time_bucket[0], safe_first, local_rows, 0)
        key_bucket_indicator = (key_bucket[:, None] == bucket_ids[None, :]).astype(jnp.bfloat16)
        map_cols = lax.dynamic_slice_in_dim(map_rows, safe_first // BLK, blocks_here, 1)
        same_block = query_pos[:, None] // BLK == key_pos[None, :] // BLK
        key_visible = (
            (query_seg[:, None] == segment_of(key_pos)[None, :])
            & (key_pos[None, :] <= query_pos[:, None])
            & (key_pos[None, :] >= 0)
            & ((expand_blocks(map_cols, BLK) == 1) | same_block)
        )
        key_bias_terms = jnp.einsum(
            "vqx,px->vqp",
            bias_matrix_rows,
            key_bucket_indicator,
            preferred_element_type=jnp.float32,
        )
        visible, bias_terms, key_bucket_indicator = (
            key_visible,
            key_bias_terms,
            key_bucket_indicator,
        )
        forward_pair = window[distance]
        forward_key_heads = forward_pair[0].reshape(local_rows, head_count, head_dim)
        forward_value_heads = forward_pair[1].reshape(local_rows, head_count, head_dim)
        forward_scores = (
            jnp.einsum(
                "ihd,jhd->hij", query_heads, forward_key_heads, preferred_element_type=jnp.float32
            )
            * scale
            + bias_terms
        )
        forward_weights = jnp.where(visible[None], jax.nn.silu(forward_scores), 0.0).astype(
            jnp.bfloat16
        )
        attended_part = jnp.einsum(
            "hij,jhd->ihd", forward_weights, forward_value_heads, preferred_element_type=jnp.float32
        )
        attended = attended + attended_part
        tiles.append((visible, forward_scores, forward_weights, key_bucket_indicator))
    attended = attended.reshape(local_rows, width)
    centered = attended - jnp.mean(attended, axis=1, keepdims=True)
    inverse = lax.rsqrt(jnp.mean(centered * centered, axis=1, keepdims=True) + NORM_EPSILON)
    normed = centered * inverse
    dz_rows = lax.dot_general(
        grad_rows, w_out, (((1,), (1,)), ((), ())), preferred_element_type=jnp.float32
    )
    gate_float = gate_rows.astype(jnp.float32)
    gate_grad = (dz_rows * normed).astype(jnp.bfloat16)
    mixed = (normed * gate_float).astype(jnp.bfloat16)
    lifted = dz_rows * gate_float
    attended_grad = (
        (
            lifted
            - jnp.mean(lifted, axis=1, keepdims=True)
            - normed * jnp.mean(lifted * normed, axis=1, keepdims=True)
        )
        * inverse
    ).astype(jnp.bfloat16)
    grad_heads = attended_grad.reshape(local_rows, head_count, head_dim)
    indicator_float = query_bucket_indicator.astype(jnp.float32)
    dp_size = lax.axis_size("dp")
    weight_term = lax.dot_general(
        mixed, grad_rows, (((0,), (0,)), ((), ())), preferred_element_type=jnp.float32
    )
    weight_plan = [("split", "dp", mask) for mask in axis_bits("dp")]
    weight_plan.append(("exchange", "ctx", 0))
    weight_plan += [("skip", "ctx", 0), ("skip", "ctx", 0), ("tie", "ctx", 0)]
    weight_state = [weight_term.reshape(dp_size, -1), 0]

    def slot(anchor):
        blocks, done = weight_state
        if done < len(weight_plan):
            kind, axis, mask = weight_plan[done]
            if kind != "skip":
                blocks, anchor = lax.optimization_barrier((blocks, anchor))
            if kind in ("skip", "tie"):
                weight_state[0] = blocks
            elif kind == "exchange":
                weight_state[0] = summed_by_exchange(blocks.reshape(-1), (axis,))
            else:
                weight_state[0] = plan_step(blocks, kind, axis, mask)
            weight_state[1] = done + 1
        return anchor

    query_sum = jnp.zeros((local_rows, width), jnp.float32)
    share_sum = None
    key_terms = [None, None, None]
    sent = [None, None, None]
    for distance in (2, 1, 0):
        visible, scores, weights, key_bucket_indicator = tiles[distance]
        pair = slot(window[distance])
        if distance == 0:
            sent[2], pair = lax.optimization_barrier((sent[2], pair))
        key_heads = pair[0].reshape(local_rows, head_count, head_dim)
        value_heads = pair[1].reshape(local_rows, head_count, head_dim)
        weight_grad = jnp.einsum(
            "ihd,jhd->hij", grad_heads, value_heads, preferred_element_type=jnp.float32
        )
        value_part = jnp.einsum(
            "hij,ihd->jhd", weights, grad_heads, preferred_element_type=jnp.float32
        ).reshape(local_rows, width)
        score_gradient = jnp.where(visible[None], weight_grad * silu_slope(scores), 0.0).astype(
            jnp.bfloat16
        )
        score_gradient = slot(score_gradient)
        query_part = jnp.einsum(
            "hij,jhd->ihd", score_gradient, key_heads, preferred_element_type=jnp.float32
        ).reshape(local_rows, width)
        key_part = (
            jnp.einsum(
                "hij,ihd->jhd", score_gradient, query_heads, preferred_element_type=jnp.float32
            ).reshape(local_rows, width)
            * scale
        )
        bucket_share_piece = jnp.einsum(
            "rmw,wx->rmx", score_gradient, key_bucket_indicator, preferred_element_type=jnp.float32
        )
        share_sum = bucket_share_piece if share_sum is None else share_sum + bucket_share_piece
        query_sum = query_sum + query_part
        key_terms[distance] = jnp.stack([key_part, value_part])
        if distance > 0:
            sent[distance] = passed_along(
                key_terms[distance].astype(jnp.bfloat16), "ctx", -distance
            )
    table_local = jnp.einsum(
        "qp,cqk->cpk", indicator_float, share_sum, precision=lax.Precision.HIGHEST
    )
    gathered = key_terms[0] + sent[1].astype(jnp.float32) + sent[2].astype(jnp.float32)
    query_grad = (query_sum * scale).astype(jnp.bfloat16)
    key_grad = gathered[0].astype(jnp.bfloat16)
    value_grad = gathered[1].astype(jnp.bfloat16)
    projection_grad = weight_state[0].reshape(width // dp_size, width)
    table_grad = summed_by_exchange(table_local.reshape(-1), ("ctx", "dp")).reshape(
        table_local.shape
    )
    return (
        query_grad[None],
        key_grad[None],
        value_grad[None],
        gate_grad[None],
        projection_grad,
        table_grad,
    )


def solution(mesh):
    return jax.shard_map(
        shards,
        mesh=mesh,
        in_specs=(
            P("dp", "ctx", None),
            P("dp", "ctx", None),
            P("dp", "ctx", None),
            P("dp", "ctx", None),
            P("dp", "ctx", None),
            P("dp", None),
            P("dp", None),
            P("dp", None, None),
            P(),
            P(),
        ),
        out_specs=(
            P("dp", "ctx", None),
            P("dp", "ctx", None),
            P("dp", "ctx", None),
            P("dp", "ctx", None),
            P("dp", None),
            P(),
        ),
        check_vma=False,
    )
```

```python
import jax
import jax.numpy as jnp
from jax import lax
from jax.sharding import PartitionSpec as P

BLK = 128


NORM_EPSILON = 1e-05


def passed_along(value, axis, by):
    length = lax.axis_size(axis)
    pairs = [(i, i + by) for i in range(length) if 0 <= i + by < length]
    return lax.ppermute(value, axis, pairs)


def exchanged(value, axis, mask):
    length = lax.axis_size(axis)
    pairs = [(i, i ^ mask) for i in range(length)]
    return lax.ppermute(value, axis, pairs)


def axis_bits(axis):
    length = lax.axis_size(axis)
    bits = []
    mask = 1
    while mask < length:
        bits.append(mask)
        mask *= 2
    return bits


def scatter_blocks(blocks, axis):
    index = lax.axis_index(axis)
    for mask in axis_bits(axis):
        bit = (index // mask) % 2
        pairs = blocks.reshape(blocks.shape[0] // 2, 2, blocks.shape[1])
        keep = lax.dynamic_index_in_dim(pairs, bit, axis=1, keepdims=False)
        send = lax.dynamic_index_in_dim(pairs, 1 - bit, axis=1, keepdims=False)
        blocks = keep + exchanged(send, axis, mask)
    return blocks[0]


def gather_blocks(chunk, axis):
    index = lax.axis_index(axis)
    held = chunk[None]
    for mask in reversed(axis_bits(axis)):
        bit = (index // mask) % 2
        other = exchanged(held, axis, mask)
        low = jnp.where(bit == 0, held, other)
        high = jnp.where(bit == 0, other, held)
        held = jnp.stack([low, high], axis=1).reshape(held.shape[0] * 2, held.shape[1])
    return held


def summed_over(flat, axis):
    size = lax.axis_size(axis)
    part = scatter_blocks(flat.reshape(size, flat.shape[0] // size), axis)
    return gather_blocks(part, axis).reshape(flat.shape)


def plan_step(blocks, kind, axis, mask):
    bit = (lax.axis_index(axis) // mask) % 2
    if kind == "split":
        if blocks.shape[0] == 1:
            blocks = blocks.reshape(2, -1)
        pairs = blocks.reshape(blocks.shape[0] // 2, 2, blocks.shape[1])
        keep = lax.dynamic_index_in_dim(pairs, bit, axis=1, keepdims=False)
        send = lax.dynamic_index_in_dim(pairs, 1 - bit, axis=1, keepdims=False)
        return keep + exchanged(send, axis, mask)
    other = exchanged(blocks, axis, mask)
    low = jnp.where(bit == 0, blocks, other)
    high = jnp.where(bit == 0, other, blocks)
    return jnp.concatenate([low, high], axis=1)


def summed_by_exchange(flat, axes):
    size = 1
    for axis in axes:
        size *= lax.axis_size(axis)
    pieces = lax.all_to_all(flat.reshape(size, -1), axes, 0, 0, tiled=True)
    total = jnp.sum(pieces, axis=0, keepdims=True)
    spread = jnp.broadcast_to(total, pieces.shape)
    return lax.all_to_all(spread, axes, 0, 0, tiled=True).reshape(flat.shape)


def silu_slope(scores):
    sigmoid = jax.nn.sigmoid(scores)
    return sigmoid * (1.0 + scores * (1.0 - sigmoid))


def expand_blocks(block_rows, block_size):
    return jnp.repeat(jnp.repeat(block_rows, block_size, axis=0), block_size, axis=1)


def shards(
    queries,
    keys,
    values,
    gates,
    out_grad,
    time_bucket,
    lengths,
    block_map,
    bucket_bias_matrix,
    w_out,
):
    query_rows = queries[0]
    key_rows = keys[0]
    value_rows = values[0]
    gate_rows = gates[0]
    grad_rows = out_grad[0]
    local_rows, width = query_rows.shape
    head_count = bucket_bias_matrix.shape[0]
    bucket_count = bucket_bias_matrix.shape[1]
    head_dim = width // head_count
    scale = head_dim ** (-0.5)
    blocks_here = local_rows // BLK
    cycle_index = lax.axis_index("ctx")
    row_start = cycle_index * local_rows
    offsets = jnp.cumsum(lengths[0], dtype=jnp.int32) - lengths[0]

    def segment_of(positions):
        return jnp.sum(
            (positions[:, None] >= offsets[None, 1:]).astype(jnp.int32), axis=1, dtype=jnp.int32
        )

    bucket_ids = jnp.arange(bucket_count, dtype=jnp.int32)
    query_pos = row_start + jnp.arange(local_rows, dtype=jnp.int32)
    query_seg = segment_of(query_pos)
    query_bucket = lax.dynamic_slice_in_dim(time_bucket[0], row_start, local_rows, 0)
    query_bucket_indicator = (query_bucket[:, None] == bucket_ids[None, :]).astype(jnp.bfloat16)
    bias_matrix_rows = jnp.einsum(
        "lf,sfq->slq",
        query_bucket_indicator,
        bucket_bias_matrix,
        preferred_element_type=jnp.float32,
    ).astype(jnp.bfloat16)
    map_rows = lax.dynamic_slice_in_dim(block_map[0], cycle_index * blocks_here, blocks_here, 0)
    query_heads = query_rows.reshape(local_rows, head_count, head_dim)
    stacked = jnp.stack([key_rows, value_rows])
    window = [stacked, passed_along(stacked, "ctx", 1), passed_along(stacked, "ctx", 2)]
    tiles = []
    attended = jnp.zeros((local_rows, head_count, head_dim), jnp.float32)
    for distance in range(3):
        key_first = row_start - distance * local_rows
        key_pos = key_first + jnp.arange(local_rows, dtype=jnp.int32)
        safe_first = jnp.maximum(key_first, 0)
        key_bucket = lax.dynamic_slice_in_dim(time_bucket[0], safe_first, local_rows, 0)
        key_bucket_indicator = (key_bucket[:, None] == bucket_ids[None, :]).astype(jnp.bfloat16)
        map_cols = lax.dynamic_slice_in_dim(map_rows, safe_first // BLK, blocks_here, 1)
        same_block = query_pos[:, None] // BLK == key_pos[None, :] // BLK
        key_visible = (
            (query_seg[:, None] == segment_of(key_pos)[None, :])
            & (key_pos[None, :] <= query_pos[:, None])
            & (key_pos[None, :] >= 0)
            & ((expand_blocks(map_cols, BLK) == 1) | same_block)
        )
        key_bias_terms = jnp.einsum(
            "vqx,px->vqp",
            bias_matrix_rows,
            key_bucket_indicator,
            preferred_element_type=jnp.float32,
        )
        visible, bias_terms, key_bucket_indicator = (
            key_visible,
            key_bias_terms,
            key_bucket_indicator,
        )
        forward_pair = window[distance]
        forward_key_heads = forward_pair[0].reshape(local_rows, head_count, head_dim)
        forward_value_heads = forward_pair[1].reshape(local_rows, head_count, head_dim)
        forward_scores = (
            jnp.einsum(
                "ihd,jhd->hij", query_heads, forward_key_heads, preferred_element_type=jnp.float32
            )
            * scale
            + bias_terms
        )
        forward_weights = jnp.where(visible[None], jax.nn.silu(forward_scores), 0.0).astype(
            jnp.bfloat16
        )
        attended_part = jnp.einsum(
            "hij,jhd->ihd", forward_weights, forward_value_heads, preferred_element_type=jnp.float32
        )
        attended = attended + attended_part
        tiles.append((visible, forward_scores, forward_weights, key_bucket_indicator))
    attended = attended.reshape(local_rows, width)
    centered = attended - jnp.mean(attended, axis=1, keepdims=True)
    inverse = lax.rsqrt(jnp.mean(centered * centered, axis=1, keepdims=True) + NORM_EPSILON)
    normed = centered * inverse
    dz_rows = lax.dot_general(
        grad_rows, w_out, (((1,), (1,)), ((), ())), preferred_element_type=jnp.float32
    )
    gate_float = gate_rows.astype(jnp.float32)
    gate_grad = (dz_rows * normed).astype(jnp.bfloat16)
    mixed = (normed * gate_float).astype(jnp.bfloat16)
    lifted = dz_rows * gate_float
    attended_grad = (
        (
            lifted
            - jnp.mean(lifted, axis=1, keepdims=True)
            - normed * jnp.mean(lifted * normed, axis=1, keepdims=True)
        )
        * inverse
    ).astype(jnp.bfloat16)
    grad_heads = attended_grad.reshape(local_rows, head_count, head_dim)
    indicator_float = query_bucket_indicator.astype(jnp.float32)
    dp_size = lax.axis_size("dp")
    weight_term = lax.dot_general(
        mixed, grad_rows, (((0,), (0,)), ((), ())), preferred_element_type=jnp.float32
    )
    weight_plan = [("split", "dp", mask) for mask in axis_bits("dp")]
    weight_plan.append(("exchange", "ctx", 0))
    weight_state = [weight_term.reshape(dp_size, -1), 0]

    def slot(anchor):
        blocks, done = weight_state
        if done < len(weight_plan):
            blocks, anchor = lax.optimization_barrier((blocks, anchor))
            kind, axis, mask = weight_plan[done]
            if kind == "exchange":
                weight_state[0] = lax.psum(blocks.reshape(-1), axis)
            else:
                weight_state[0] = plan_step(blocks, kind, axis, mask)
            weight_state[1] = done + 1
        return anchor

    query_sum = jnp.zeros((local_rows, width), jnp.float32)
    share_sum = None
    key_terms = [None, None, None]
    sent = [None, None, None]
    for distance in (2, 1, 0):
        visible, scores, weights, key_bucket_indicator = tiles[distance]
        pair = slot(window[distance])
        if distance == 0:
            sent[2], pair = lax.optimization_barrier((sent[2], pair))
        key_heads = pair[0].reshape(local_rows, head_count, head_dim)
        value_heads = pair[1].reshape(local_rows, head_count, head_dim)
        weight_grad = jnp.einsum(
            "ihd,jhd->hij", grad_heads, value_heads, preferred_element_type=jnp.float32
        )
        value_part = jnp.einsum(
            "hij,ihd->jhd", weights, grad_heads, preferred_element_type=jnp.float32
        ).reshape(local_rows, width)
        score_gradient = jnp.where(visible[None], weight_grad * silu_slope(scores), 0.0).astype(
            jnp.bfloat16
        )
        score_gradient = slot(score_gradient)
        query_part = jnp.einsum(
            "hij,jhd->ihd", score_gradient, key_heads, preferred_element_type=jnp.float32
        ).reshape(local_rows, width)
        key_part = (
            jnp.einsum(
                "hij,ihd->jhd", score_gradient, query_heads, preferred_element_type=jnp.float32
            ).reshape(local_rows, width)
            * scale
        )
        bucket_share_piece = jnp.einsum(
            "rmw,wx->rmx", score_gradient, key_bucket_indicator, preferred_element_type=jnp.float32
        )
        share_sum = bucket_share_piece if share_sum is None else share_sum + bucket_share_piece
        query_sum = query_sum + query_part
        key_terms[distance] = jnp.stack([key_part, value_part])
        if distance > 0:
            sent[distance] = passed_along(
                key_terms[distance].astype(jnp.bfloat16), "ctx", -distance
            )
    table_local = jnp.einsum(
        "qp,cqk->cpk", indicator_float, share_sum, precision=lax.Precision.HIGHEST
    )
    gathered = key_terms[0] + sent[1].astype(jnp.float32) + sent[2].astype(jnp.float32)
    query_grad = (query_sum * scale).astype(jnp.bfloat16)
    key_grad = gathered[0].astype(jnp.bfloat16)
    value_grad = gathered[1].astype(jnp.bfloat16)
    projection_grad = weight_state[0].reshape(width // dp_size, width)
    table_grad = summed_by_exchange(table_local.reshape(-1), ("ctx", "dp")).reshape(
        table_local.shape
    )
    return (
        query_grad[None],
        key_grad[None],
        value_grad[None],
        gate_grad[None],
        projection_grad,
        table_grad,
    )


def solution(mesh):
    return jax.shard_map(
        shards,
        mesh=mesh,
        in_specs=(
            P("dp", "ctx", None),
            P("dp", "ctx", None),
            P("dp", "ctx", None),
            P("dp", "ctx", None),
            P("dp", "ctx", None),
            P("dp", None),
            P("dp", None),
            P("dp", None, None),
            P(),
            P(),
        ),
        out_specs=(
            P("dp", "ctx", None),
            P("dp", "ctx", None),
            P("dp", "ctx", None),
            P("dp", "ctx", None),
            P("dp", None),
            P(),
        ),
        check_vma=False,
    )
```

```python
import jax
import jax.numpy as jnp
from jax import lax
from jax.sharding import PartitionSpec as P

BLK = 128


NORM_EPSILON = 1e-05


def passed_along(value, axis, by):
    length = lax.axis_size(axis)
    pairs = [(i, i + by) for i in range(length) if 0 <= i + by < length]
    return lax.ppermute(value, axis, pairs)


def exchanged(value, axis, mask):
    length = lax.axis_size(axis)
    pairs = [(i, i ^ mask) for i in range(length)]
    return lax.ppermute(value, axis, pairs)


def axis_bits(axis):
    length = lax.axis_size(axis)
    bits = []
    mask = 1
    while mask < length:
        bits.append(mask)
        mask *= 2
    return bits


def scatter_blocks(blocks, axis):
    index = lax.axis_index(axis)
    for mask in axis_bits(axis):
        bit = (index // mask) % 2
        pairs = blocks.reshape(blocks.shape[0] // 2, 2, blocks.shape[1])
        keep = lax.dynamic_index_in_dim(pairs, bit, axis=1, keepdims=False)
        send = lax.dynamic_index_in_dim(pairs, 1 - bit, axis=1, keepdims=False)
        blocks = keep + exchanged(send, axis, mask)
    return blocks[0]


def gather_blocks(chunk, axis):
    index = lax.axis_index(axis)
    held = chunk[None]
    for mask in reversed(axis_bits(axis)):
        bit = (index // mask) % 2
        other = exchanged(held, axis, mask)
        low = jnp.where(bit == 0, held, other)
        high = jnp.where(bit == 0, other, held)
        held = jnp.stack([low, high], axis=1).reshape(held.shape[0] * 2, held.shape[1])
    return held


def summed_over(flat, axis):
    size = lax.axis_size(axis)
    part = scatter_blocks(flat.reshape(size, flat.shape[0] // size), axis)
    return gather_blocks(part, axis).reshape(flat.shape)


def plan_step(blocks, kind, axis, mask):
    bit = (lax.axis_index(axis) // mask) % 2
    if kind == "split":
        if blocks.shape[0] == 1:
            blocks = blocks.reshape(2, -1)
        pairs = blocks.reshape(blocks.shape[0] // 2, 2, blocks.shape[1])
        keep = lax.dynamic_index_in_dim(pairs, bit, axis=1, keepdims=False)
        send = lax.dynamic_index_in_dim(pairs, 1 - bit, axis=1, keepdims=False)
        return keep + exchanged(send, axis, mask)
    other = exchanged(blocks, axis, mask)
    low = jnp.where(bit == 0, blocks, other)
    high = jnp.where(bit == 0, other, blocks)
    return jnp.concatenate([low, high], axis=1)


def summed_by_exchange(flat, axes):
    size = 1
    for axis in axes:
        size *= lax.axis_size(axis)
    pieces = lax.all_to_all(flat.reshape(size, -1), axes, 0, 0, tiled=True)
    total = jnp.sum(pieces, axis=0, keepdims=True)
    spread = jnp.broadcast_to(total, pieces.shape)
    return lax.all_to_all(spread, axes, 0, 0, tiled=True).reshape(flat.shape)


def silu_slope(scores):
    sigmoid = jax.nn.sigmoid(scores)
    return sigmoid * (1.0 + scores * (1.0 - sigmoid))


def expand_blocks(block_rows, block_size):
    return jnp.repeat(jnp.repeat(block_rows, block_size, axis=0), block_size, axis=1)


def shards(
    queries,
    keys,
    values,
    gates,
    out_grad,
    time_bucket,
    lengths,
    block_map,
    bucket_bias_matrix,
    w_out,
):
    query_rows = queries[0]
    key_rows = keys[0]
    value_rows = values[0]
    gate_rows = gates[0]
    grad_rows = out_grad[0]
    local_rows, width = query_rows.shape
    head_count = bucket_bias_matrix.shape[0]
    bucket_count = bucket_bias_matrix.shape[1]
    head_dim = width // head_count
    scale = head_dim ** (-0.5)
    blocks_here = local_rows // BLK
    cycle_index = lax.axis_index("ctx")
    row_start = cycle_index * local_rows
    offsets = jnp.cumsum(lengths[0], dtype=jnp.int32) - lengths[0]

    def segment_of(positions):
        return jnp.sum(
            (positions[:, None] >= offsets[None, 1:]).astype(jnp.int32), axis=1, dtype=jnp.int32
        )

    bucket_ids = jnp.arange(bucket_count, dtype=jnp.int32)
    query_pos = row_start + jnp.arange(local_rows, dtype=jnp.int32)
    query_seg = segment_of(query_pos)
    query_bucket = lax.dynamic_slice_in_dim(time_bucket[0], row_start, local_rows, 0)
    query_bucket_indicator = (query_bucket[:, None] == bucket_ids[None, :]).astype(jnp.bfloat16)
    bias_matrix_rows = jnp.einsum(
        "lf,sfq->slq",
        query_bucket_indicator,
        bucket_bias_matrix,
        preferred_element_type=jnp.float32,
    ).astype(jnp.bfloat16)
    map_rows = lax.dynamic_slice_in_dim(block_map[0], cycle_index * blocks_here, blocks_here, 0)
    query_heads = query_rows.reshape(local_rows, head_count, head_dim)
    stacked = jnp.stack([key_rows, value_rows])
    window = [stacked, passed_along(stacked, "ctx", 1), passed_along(stacked, "ctx", 2)]
    tiles = []
    attended = jnp.zeros((local_rows, head_count, head_dim), jnp.float32)
    for distance in range(3):
        key_first = row_start - distance * local_rows
        key_pos = key_first + jnp.arange(local_rows, dtype=jnp.int32)
        safe_first = jnp.maximum(key_first, 0)
        key_bucket = lax.dynamic_slice_in_dim(time_bucket[0], safe_first, local_rows, 0)
        key_bucket_indicator = (key_bucket[:, None] == bucket_ids[None, :]).astype(jnp.bfloat16)
        map_cols = lax.dynamic_slice_in_dim(map_rows, safe_first // BLK, blocks_here, 1)
        same_block = query_pos[:, None] // BLK == key_pos[None, :] // BLK
        key_visible = (
            (query_seg[:, None] == segment_of(key_pos)[None, :])
            & (key_pos[None, :] <= query_pos[:, None])
            & (key_pos[None, :] >= 0)
            & ((expand_blocks(map_cols, BLK) == 1) | same_block)
        )
        key_bias_terms = jnp.einsum(
            "vqx,px->vqp",
            bias_matrix_rows,
            key_bucket_indicator,
            preferred_element_type=jnp.float32,
        )
        visible, bias_terms, key_bucket_indicator = (
            key_visible,
            key_bias_terms,
            key_bucket_indicator,
        )
        forward_pair = window[distance]
        forward_key_heads = forward_pair[0].reshape(local_rows, head_count, head_dim)
        forward_value_heads = forward_pair[1].reshape(local_rows, head_count, head_dim)
        forward_scores = (
            jnp.einsum(
                "ihd,jhd->hij", query_heads, forward_key_heads, preferred_element_type=jnp.float32
            )
            * scale
            + bias_terms
        )
        forward_weights = jnp.where(visible[None], jax.nn.silu(forward_scores), 0.0).astype(
            jnp.bfloat16
        )
        attended_part = jnp.einsum(
            "hij,jhd->ihd", forward_weights, forward_value_heads, preferred_element_type=jnp.float32
        )
        attended = attended + attended_part
        tiles.append((visible, forward_scores, forward_weights, key_bucket_indicator))
    attended = attended.reshape(local_rows, width)
    centered = attended - jnp.mean(attended, axis=1, keepdims=True)
    inverse = lax.rsqrt(jnp.mean(centered * centered, axis=1, keepdims=True) + NORM_EPSILON)
    normed = centered * inverse
    dz_rows = lax.dot_general(
        grad_rows, w_out, (((1,), (1,)), ((), ())), preferred_element_type=jnp.float32
    )
    gate_float = gate_rows.astype(jnp.float32)
    gate_grad = (dz_rows * normed).astype(jnp.bfloat16)
    mixed = (normed * gate_float).astype(jnp.bfloat16)
    lifted = dz_rows * gate_float
    attended_grad = (
        (
            lifted
            - jnp.mean(lifted, axis=1, keepdims=True)
            - normed * jnp.mean(lifted * normed, axis=1, keepdims=True)
        )
        * inverse
    ).astype(jnp.bfloat16)
    grad_heads = attended_grad.reshape(local_rows, head_count, head_dim)
    indicator_float = query_bucket_indicator.astype(jnp.float32)
    dp_size = lax.axis_size("dp")
    weight_term = lax.dot_general(
        mixed, grad_rows, (((0,), (0,)), ((), ())), preferred_element_type=jnp.float32
    )
    weight_plan = [("split", "dp", mask) for mask in axis_bits("dp")]
    weight_plan += [("skip", "dp", 0), ("skip", "dp", 0), ("tie", "dp", 0)]
    weight_state = [weight_term.reshape(dp_size, -1), 0]

    def slot(anchor):
        blocks, done = weight_state
        if done < len(weight_plan):
            kind, axis, mask = weight_plan[done]
            if kind != "skip":
                blocks, anchor = lax.optimization_barrier((blocks, anchor))
            if kind in ("skip", "tie"):
                weight_state[0] = blocks
            elif kind == "exchange":
                weight_state[0] = summed_by_exchange(blocks.reshape(-1), (axis,))
            else:
                weight_state[0] = plan_step(blocks, kind, axis, mask)
            weight_state[1] = done + 1
        return anchor

    query_sum = jnp.zeros((local_rows, width), jnp.float32)
    share_sum = None
    key_terms = [None, None, None]
    sent = [None, None, None]
    for distance in (2, 1, 0):
        visible, scores, weights, key_bucket_indicator = tiles[distance]
        pair = slot(window[distance])
        if distance == 0:
            sent[2], pair = lax.optimization_barrier((sent[2], pair))
        key_heads = pair[0].reshape(local_rows, head_count, head_dim)
        value_heads = pair[1].reshape(local_rows, head_count, head_dim)
        weight_grad = jnp.einsum(
            "ihd,jhd->hij", grad_heads, value_heads, preferred_element_type=jnp.float32
        )
        value_part = jnp.einsum(
            "hij,ihd->jhd", weights, grad_heads, preferred_element_type=jnp.float32
        ).reshape(local_rows, width)
        score_gradient = jnp.where(visible[None], weight_grad * silu_slope(scores), 0.0).astype(
            jnp.bfloat16
        )
        score_gradient = slot(score_gradient)
        query_part = jnp.einsum(
            "hij,jhd->ihd", score_gradient, key_heads, preferred_element_type=jnp.float32
        ).reshape(local_rows, width)
        key_part = (
            jnp.einsum(
                "hij,ihd->jhd", score_gradient, query_heads, preferred_element_type=jnp.float32
            ).reshape(local_rows, width)
            * scale
        )
        bucket_share_piece = jnp.einsum(
            "rmw,wx->rmx", score_gradient, key_bucket_indicator, preferred_element_type=jnp.float32
        )
        share_sum = bucket_share_piece if share_sum is None else share_sum + bucket_share_piece
        query_sum = query_sum + query_part
        key_terms[distance] = jnp.stack([key_part, value_part])
        if distance > 0:
            sent[distance] = passed_along(
                key_terms[distance].astype(jnp.bfloat16), "ctx", -distance
            )
    table_local = jnp.einsum(
        "qp,cqk->cpk", indicator_float, share_sum, precision=lax.Precision.HIGHEST
    )
    table_part = scatter_blocks(table_local.reshape(dp_size, -1), "dp")
    weight_rows = weight_state[0].reshape(-1)
    combined = summed_by_exchange(jnp.concatenate([weight_rows, table_part]), ("ctx",))
    projection_grad = combined[: weight_rows.shape[0]].reshape(width // dp_size, width)
    table_grad = gather_blocks(combined[weight_rows.shape[0] :], "dp").reshape(table_local.shape)
    gathered = key_terms[0] + sent[1].astype(jnp.float32) + sent[2].astype(jnp.float32)
    query_grad = (query_sum * scale).astype(jnp.bfloat16)
    key_grad = gathered[0].astype(jnp.bfloat16)
    value_grad = gathered[1].astype(jnp.bfloat16)
    return (
        query_grad[None],
        key_grad[None],
        value_grad[None],
        gate_grad[None],
        projection_grad,
        table_grad,
    )


def solution(mesh):
    return jax.shard_map(
        shards,
        mesh=mesh,
        in_specs=(
            P("dp", "ctx", None),
            P("dp", "ctx", None),
            P("dp", "ctx", None),
            P("dp", "ctx", None),
            P("dp", "ctx", None),
            P("dp", None),
            P("dp", None),
            P("dp", None, None),
            P(),
            P(),
        ),
        out_specs=(
            P("dp", "ctx", None),
            P("dp", "ctx", None),
            P("dp", "ctx", None),
            P("dp", "ctx", None),
            P("dp", None),
            P(),
        ),
        check_vma=False,
    )
```

```python
import jax
import jax.numpy as jnp
from jax import lax
from jax.sharding import PartitionSpec as P

BLK = 128


NORM_EPSILON = 1e-05


def passed_along(value, axis, by):
    length = lax.axis_size(axis)
    pairs = [(i, i + by) for i in range(length) if 0 <= i + by < length]
    return lax.ppermute(value, axis, pairs)


def exchanged(value, axis, mask):
    length = lax.axis_size(axis)
    pairs = [(i, i ^ mask) for i in range(length)]
    return lax.ppermute(value, axis, pairs)


def axis_bits(axis):
    length = lax.axis_size(axis)
    bits = []
    mask = 1
    while mask < length:
        bits.append(mask)
        mask *= 2
    return bits


def scatter_blocks(blocks, axis):
    index = lax.axis_index(axis)
    for mask in axis_bits(axis):
        bit = (index // mask) % 2
        pairs = blocks.reshape(blocks.shape[0] // 2, 2, blocks.shape[1])
        keep = lax.dynamic_index_in_dim(pairs, bit, axis=1, keepdims=False)
        send = lax.dynamic_index_in_dim(pairs, 1 - bit, axis=1, keepdims=False)
        blocks = keep + exchanged(send, axis, mask)
    return blocks[0]


def gather_blocks(chunk, axis):
    index = lax.axis_index(axis)
    held = chunk[None]
    for mask in reversed(axis_bits(axis)):
        bit = (index // mask) % 2
        other = exchanged(held, axis, mask)
        low = jnp.where(bit == 0, held, other)
        high = jnp.where(bit == 0, other, held)
        held = jnp.stack([low, high], axis=1).reshape(held.shape[0] * 2, held.shape[1])
    return held


def summed_over(flat, axis):
    size = lax.axis_size(axis)
    part = scatter_blocks(flat.reshape(size, flat.shape[0] // size), axis)
    return gather_blocks(part, axis).reshape(flat.shape)


def plan_step(blocks, kind, axis, mask):
    bit = (lax.axis_index(axis) // mask) % 2
    if kind == "split":
        if blocks.shape[0] == 1:
            blocks = blocks.reshape(2, -1)
        pairs = blocks.reshape(blocks.shape[0] // 2, 2, blocks.shape[1])
        keep = lax.dynamic_index_in_dim(pairs, bit, axis=1, keepdims=False)
        send = lax.dynamic_index_in_dim(pairs, 1 - bit, axis=1, keepdims=False)
        return keep + exchanged(send, axis, mask)
    other = exchanged(blocks, axis, mask)
    low = jnp.where(bit == 0, blocks, other)
    high = jnp.where(bit == 0, other, blocks)
    return jnp.concatenate([low, high], axis=1)


def summed_by_exchange(flat, axes):
    size = 1
    for axis in axes:
        size *= lax.axis_size(axis)
    pieces = lax.all_to_all(flat.reshape(size, -1), axes, 0, 0, tiled=True)
    total = jnp.sum(pieces, axis=0, keepdims=True)
    spread = jnp.broadcast_to(total, pieces.shape)
    return lax.all_to_all(spread, axes, 0, 0, tiled=True).reshape(flat.shape)


def silu_slope(scores):
    sigmoid = jax.nn.sigmoid(scores)
    return sigmoid * (1.0 + scores * (1.0 - sigmoid))


def expand_blocks(block_rows, block_size):
    return jnp.repeat(jnp.repeat(block_rows, block_size, axis=0), block_size, axis=1)


def shards(
    queries,
    keys,
    values,
    gates,
    out_grad,
    time_bucket,
    lengths,
    block_map,
    bucket_bias_matrix,
    w_out,
):
    query_rows = queries[0]
    key_rows = keys[0]
    value_rows = values[0]
    gate_rows = gates[0]
    grad_rows = out_grad[0]
    local_rows, width = query_rows.shape
    head_count = bucket_bias_matrix.shape[0]
    bucket_count = bucket_bias_matrix.shape[1]
    head_dim = width // head_count
    scale = head_dim ** (-0.5)
    blocks_here = local_rows // BLK
    cycle_index = lax.axis_index("ctx")
    row_start = cycle_index * local_rows
    offsets = jnp.cumsum(lengths[0], dtype=jnp.int32) - lengths[0]

    def segment_of(positions):
        return jnp.sum(
            (positions[:, None] >= offsets[None, 1:]).astype(jnp.int32), axis=1, dtype=jnp.int32
        )

    bucket_ids = jnp.arange(bucket_count, dtype=jnp.int32)
    query_pos = row_start + jnp.arange(local_rows, dtype=jnp.int32)
    query_seg = segment_of(query_pos)
    query_bucket = lax.dynamic_slice_in_dim(time_bucket[0], row_start, local_rows, 0)
    query_bucket_indicator = (query_bucket[:, None] == bucket_ids[None, :]).astype(jnp.bfloat16)
    bias_matrix_rows = jnp.einsum(
        "lf,sfq->slq",
        query_bucket_indicator,
        bucket_bias_matrix,
        preferred_element_type=jnp.float32,
    ).astype(jnp.bfloat16)
    map_rows = lax.dynamic_slice_in_dim(block_map[0], cycle_index * blocks_here, blocks_here, 0)
    query_heads = query_rows.reshape(local_rows, head_count, head_dim)
    stacked = jnp.stack([key_rows, value_rows])
    window = [stacked, passed_along(stacked, "ctx", 1), passed_along(stacked, "ctx", 2)]
    tiles = []
    attended = jnp.zeros((local_rows, head_count, head_dim), jnp.float32)
    for distance in range(3):
        key_first = row_start - distance * local_rows
        key_pos = key_first + jnp.arange(local_rows, dtype=jnp.int32)
        safe_first = jnp.maximum(key_first, 0)
        key_bucket = lax.dynamic_slice_in_dim(time_bucket[0], safe_first, local_rows, 0)
        key_bucket_indicator = (key_bucket[:, None] == bucket_ids[None, :]).astype(jnp.bfloat16)
        map_cols = lax.dynamic_slice_in_dim(map_rows, safe_first // BLK, blocks_here, 1)
        same_block = query_pos[:, None] // BLK == key_pos[None, :] // BLK
        key_visible = (
            (query_seg[:, None] == segment_of(key_pos)[None, :])
            & (key_pos[None, :] <= query_pos[:, None])
            & (key_pos[None, :] >= 0)
            & ((expand_blocks(map_cols, BLK) == 1) | same_block)
        )
        key_bias_terms = jnp.einsum(
            "vqx,px->vqp",
            bias_matrix_rows,
            key_bucket_indicator,
            preferred_element_type=jnp.float32,
        )
        visible, bias_terms, key_bucket_indicator = (
            key_visible,
            key_bias_terms,
            key_bucket_indicator,
        )
        forward_pair = window[distance]
        forward_key_heads = forward_pair[0].reshape(local_rows, head_count, head_dim)
        forward_value_heads = forward_pair[1].reshape(local_rows, head_count, head_dim)
        forward_scores = (
            jnp.einsum(
                "ihd,jhd->hij", query_heads, forward_key_heads, preferred_element_type=jnp.float32
            )
            * scale
            + bias_terms
        )
        forward_weights = jnp.where(visible[None], jax.nn.silu(forward_scores), 0.0).astype(
            jnp.bfloat16
        )
        attended_part = jnp.einsum(
            "hij,jhd->ihd", forward_weights, forward_value_heads, preferred_element_type=jnp.float32
        )
        attended = attended + attended_part
        tiles.append((visible, forward_scores, forward_weights, key_bucket_indicator))
    attended = attended.reshape(local_rows, width)
    centered = attended - jnp.mean(attended, axis=1, keepdims=True)
    inverse = lax.rsqrt(jnp.mean(centered * centered, axis=1, keepdims=True) + NORM_EPSILON)
    normed = centered * inverse
    dz_rows = lax.dot_general(
        grad_rows, w_out, (((1,), (1,)), ((), ())), preferred_element_type=jnp.float32
    )
    gate_float = gate_rows.astype(jnp.float32)
    gate_grad = (dz_rows * normed).astype(jnp.bfloat16)
    mixed = (normed * gate_float).astype(jnp.bfloat16)
    lifted = dz_rows * gate_float
    attended_grad = (
        (
            lifted
            - jnp.mean(lifted, axis=1, keepdims=True)
            - normed * jnp.mean(lifted * normed, axis=1, keepdims=True)
        )
        * inverse
    ).astype(jnp.bfloat16)
    grad_heads = attended_grad.reshape(local_rows, head_count, head_dim)
    indicator_float = query_bucket_indicator.astype(jnp.float32)
    dp_size = lax.axis_size("dp")
    weight_term = lax.dot_general(
        mixed, grad_rows, (((0,), (0,)), ((), ())), preferred_element_type=jnp.float32
    )
    weight_plan = [("split", "dp", mask) for mask in axis_bits("dp")]
    weight_plan.append(("exchange", "ctx", 0))
    weight_plan.append(("tie", "ctx", 0))
    weight_state = [weight_term.reshape(dp_size, -1), 0]

    def slot(anchor):
        blocks, done = weight_state
        if done < len(weight_plan):
            kind, axis, mask = weight_plan[done]
            if kind != "skip":
                blocks, anchor = lax.optimization_barrier((blocks, anchor))
            if kind in ("skip", "tie"):
                weight_state[0] = blocks
            elif kind == "exchange":
                weight_state[0] = summed_by_exchange(blocks.reshape(-1), (axis,))
            else:
                weight_state[0] = plan_step(blocks, kind, axis, mask)
            weight_state[1] = done + 1
        return anchor

    query_sum = jnp.zeros((local_rows, width), jnp.float32)
    share_sum = None
    key_terms = [None, None, None]
    sent = [None, None, None]
    for distance in (2, 1, 0):
        visible, scores, weights, key_bucket_indicator = tiles[distance]
        pair = slot(window[distance])
        key_heads = pair[0].reshape(local_rows, head_count, head_dim)
        value_heads = pair[1].reshape(local_rows, head_count, head_dim)
        weight_grad = jnp.einsum(
            "ihd,jhd->hij", grad_heads, value_heads, preferred_element_type=jnp.float32
        )
        value_part = jnp.einsum(
            "hij,ihd->jhd", weights, grad_heads, preferred_element_type=jnp.float32
        ).reshape(local_rows, width)
        score_gradient = jnp.where(visible[None], weight_grad * silu_slope(scores), 0.0).astype(
            jnp.bfloat16
        )
        score_gradient = slot(score_gradient)
        if distance == 1:
            weight_state[0], held = lax.optimization_barrier((weight_state[0], held))
            sent[2] = passed_along(held, "ctx", -2)
        query_part = jnp.einsum(
            "hij,jhd->ihd", score_gradient, key_heads, preferred_element_type=jnp.float32
        ).reshape(local_rows, width)
        key_part = (
            jnp.einsum(
                "hij,ihd->jhd", score_gradient, query_heads, preferred_element_type=jnp.float32
            ).reshape(local_rows, width)
            * scale
        )
        bucket_share_piece = jnp.einsum(
            "rmw,wx->rmx", score_gradient, key_bucket_indicator, preferred_element_type=jnp.float32
        )
        share_sum = bucket_share_piece if share_sum is None else share_sum + bucket_share_piece
        query_sum = query_sum + query_part
        key_terms[distance] = jnp.stack([key_part, value_part])
        if distance == 2:
            held = key_terms[distance].astype(jnp.bfloat16)
        elif distance == 1:
            sent[distance] = passed_along(
                key_terms[distance].astype(jnp.bfloat16), "ctx", -distance
            )
    table_local = jnp.einsum(
        "qp,cqk->cpk", indicator_float, share_sum, precision=lax.Precision.HIGHEST
    )
    gathered = key_terms[0] + sent[1].astype(jnp.float32) + sent[2].astype(jnp.float32)
    query_grad = (query_sum * scale).astype(jnp.bfloat16)
    key_grad = gathered[0].astype(jnp.bfloat16)
    value_grad = gathered[1].astype(jnp.bfloat16)
    projection_grad = weight_state[0].reshape(width // dp_size, width)
    table_grad = summed_by_exchange(table_local.reshape(-1), ("ctx", "dp")).reshape(
        table_local.shape
    )
    return (
        query_grad[None],
        key_grad[None],
        value_grad[None],
        gate_grad[None],
        projection_grad,
        table_grad,
    )


def solution(mesh):
    return jax.shard_map(
        shards,
        mesh=mesh,
        in_specs=(
            P("dp", "ctx", None),
            P("dp", "ctx", None),
            P("dp", "ctx", None),
            P("dp", "ctx", None),
            P("dp", "ctx", None),
            P("dp", None),
            P("dp", None),
            P("dp", None, None),
            P(),
            P(),
        ),
        out_specs=(
            P("dp", "ctx", None),
            P("dp", "ctx", None),
            P("dp", "ctx", None),
            P("dp", "ctx", None),
            P("dp", None),
            P(),
        ),
        check_vma=False,
    )
```

```python
import jax
import jax.numpy as jnp
from jax import lax
from jax.sharding import PartitionSpec as P

BLK = 128


NORM_EPSILON = 1e-05


def passed_along(value, axis, by):
    length = lax.axis_size(axis)
    pairs = [(i, i + by) for i in range(length) if 0 <= i + by < length]
    return lax.ppermute(value, axis, pairs)


def exchanged(value, axis, mask):
    length = lax.axis_size(axis)
    pairs = [(i, i ^ mask) for i in range(length)]
    return lax.ppermute(value, axis, pairs)


def axis_bits(axis):
    length = lax.axis_size(axis)
    bits = []
    mask = 1
    while mask < length:
        bits.append(mask)
        mask *= 2
    return bits


def scatter_blocks(blocks, axis):
    index = lax.axis_index(axis)
    for mask in axis_bits(axis):
        bit = (index // mask) % 2
        pairs = blocks.reshape(blocks.shape[0] // 2, 2, blocks.shape[1])
        keep = lax.dynamic_index_in_dim(pairs, bit, axis=1, keepdims=False)
        send = lax.dynamic_index_in_dim(pairs, 1 - bit, axis=1, keepdims=False)
        blocks = keep + exchanged(send, axis, mask)
    return blocks[0]


def gather_blocks(chunk, axis):
    index = lax.axis_index(axis)
    held = chunk[None]
    for mask in reversed(axis_bits(axis)):
        bit = (index // mask) % 2
        other = exchanged(held, axis, mask)
        low = jnp.where(bit == 0, held, other)
        high = jnp.where(bit == 0, other, held)
        held = jnp.stack([low, high], axis=1).reshape(held.shape[0] * 2, held.shape[1])
    return held


def summed_over(flat, axis):
    size = lax.axis_size(axis)
    part = scatter_blocks(flat.reshape(size, flat.shape[0] // size), axis)
    return gather_blocks(part, axis).reshape(flat.shape)


def plan_step(blocks, kind, axis, mask):
    bit = (lax.axis_index(axis) // mask) % 2
    if kind == "split":
        if blocks.shape[0] == 1:
            blocks = blocks.reshape(2, -1)
        pairs = blocks.reshape(blocks.shape[0] // 2, 2, blocks.shape[1])
        keep = lax.dynamic_index_in_dim(pairs, bit, axis=1, keepdims=False)
        send = lax.dynamic_index_in_dim(pairs, 1 - bit, axis=1, keepdims=False)
        return keep + exchanged(send, axis, mask)
    other = exchanged(blocks, axis, mask)
    low = jnp.where(bit == 0, blocks, other)
    high = jnp.where(bit == 0, other, blocks)
    return jnp.concatenate([low, high], axis=1)


def summed_by_exchange(flat, axes):
    size = 1
    for axis in axes:
        size *= lax.axis_size(axis)
    pieces = lax.all_to_all(flat.reshape(size, -1), axes, 0, 0, tiled=True)
    total = jnp.sum(pieces, axis=0, keepdims=True)
    spread = jnp.broadcast_to(total, pieces.shape)
    return lax.all_to_all(spread, axes, 0, 0, tiled=True).reshape(flat.shape)


def silu_slope(scores):
    sigmoid = jax.nn.sigmoid(scores)
    return sigmoid * (1.0 + scores * (1.0 - sigmoid))


def expand_blocks(block_rows, block_size):
    return jnp.repeat(jnp.repeat(block_rows, block_size, axis=0), block_size, axis=1)


def shards(
    queries,
    keys,
    values,
    gates,
    out_grad,
    time_bucket,
    lengths,
    block_map,
    bucket_bias_matrix,
    w_out,
):
    query_rows = queries[0]
    key_rows = keys[0]
    value_rows = values[0]
    gate_rows = gates[0]
    grad_rows = out_grad[0]
    local_rows, width = query_rows.shape
    head_count = bucket_bias_matrix.shape[0]
    bucket_count = bucket_bias_matrix.shape[1]
    head_dim = width // head_count
    scale = head_dim ** (-0.5)
    blocks_here = local_rows // BLK
    cycle_index = lax.axis_index("ctx")
    row_start = cycle_index * local_rows
    offsets = jnp.cumsum(lengths[0], dtype=jnp.int32) - lengths[0]

    def segment_of(positions):
        return jnp.sum(
            (positions[:, None] >= offsets[None, 1:]).astype(jnp.int32), axis=1, dtype=jnp.int32
        )

    bucket_ids = jnp.arange(bucket_count, dtype=jnp.int32)
    query_pos = row_start + jnp.arange(local_rows, dtype=jnp.int32)
    query_seg = segment_of(query_pos)
    query_bucket = lax.dynamic_slice_in_dim(time_bucket[0], row_start, local_rows, 0)
    query_bucket_indicator = (query_bucket[:, None] == bucket_ids[None, :]).astype(jnp.bfloat16)
    bias_matrix_rows = jnp.einsum(
        "lf,sfq->slq",
        query_bucket_indicator,
        bucket_bias_matrix,
        preferred_element_type=jnp.float32,
    ).astype(jnp.bfloat16)
    map_rows = lax.dynamic_slice_in_dim(block_map[0], cycle_index * blocks_here, blocks_here, 0)
    query_heads = query_rows.reshape(local_rows, head_count, head_dim)
    stacked = jnp.stack([key_rows, value_rows])
    window = [stacked, None, None]
    tiles = []
    attended = jnp.zeros((local_rows, head_count, head_dim), jnp.float32)
    for distance in range(3):
        key_first = row_start - distance * local_rows
        key_pos = key_first + jnp.arange(local_rows, dtype=jnp.int32)
        safe_first = jnp.maximum(key_first, 0)
        key_bucket = lax.dynamic_slice_in_dim(time_bucket[0], safe_first, local_rows, 0)
        key_bucket_indicator = (key_bucket[:, None] == bucket_ids[None, :]).astype(jnp.bfloat16)
        map_cols = lax.dynamic_slice_in_dim(map_rows, safe_first // BLK, blocks_here, 1)
        same_block = query_pos[:, None] // BLK == key_pos[None, :] // BLK
        key_visible = (
            (query_seg[:, None] == segment_of(key_pos)[None, :])
            & (key_pos[None, :] <= query_pos[:, None])
            & (key_pos[None, :] >= 0)
            & ((expand_blocks(map_cols, BLK) == 1) | same_block)
        )
        key_bias_terms = jnp.einsum(
            "vqx,px->vqp",
            bias_matrix_rows,
            key_bucket_indicator,
            preferred_element_type=jnp.float32,
        )
        visible, bias_terms, key_bucket_indicator = (
            key_visible,
            key_bias_terms,
            key_bucket_indicator,
        )
        forward_pair = window[distance]
        forward_key_heads = forward_pair[0].reshape(local_rows, head_count, head_dim)
        forward_value_heads = forward_pair[1].reshape(local_rows, head_count, head_dim)
        forward_scores = (
            jnp.einsum(
                "ihd,jhd->hij", query_heads, forward_key_heads, preferred_element_type=jnp.float32
            )
            * scale
            + bias_terms
        )
        forward_weights = jnp.where(visible[None], jax.nn.silu(forward_scores), 0.0).astype(
            jnp.bfloat16
        )
        attended_part = jnp.einsum(
            "hij,jhd->ihd", forward_weights, forward_value_heads, preferred_element_type=jnp.float32
        )
        attended = attended + attended_part
        if distance == 0:
            shipped, attended = lax.optimization_barrier((stacked, attended))
            window[1] = passed_along(shipped, "ctx", 1)
            window[2] = passed_along(shipped, "ctx", 2)
        tiles.append((visible, forward_scores, forward_weights, key_bucket_indicator))
    attended = attended.reshape(local_rows, width)
    centered = attended - jnp.mean(attended, axis=1, keepdims=True)
    inverse = lax.rsqrt(jnp.mean(centered * centered, axis=1, keepdims=True) + NORM_EPSILON)
    normed = centered * inverse
    dz_rows = lax.dot_general(
        grad_rows, w_out, (((1,), (1,)), ((), ())), preferred_element_type=jnp.float32
    )
    gate_float = gate_rows.astype(jnp.float32)
    gate_grad = (dz_rows * normed).astype(jnp.bfloat16)
    mixed = (normed * gate_float).astype(jnp.bfloat16)
    lifted = dz_rows * gate_float
    attended_grad = (
        (
            lifted
            - jnp.mean(lifted, axis=1, keepdims=True)
            - normed * jnp.mean(lifted * normed, axis=1, keepdims=True)
        )
        * inverse
    ).astype(jnp.bfloat16)
    grad_heads = attended_grad.reshape(local_rows, head_count, head_dim)
    indicator_float = query_bucket_indicator.astype(jnp.float32)
    dp_size = lax.axis_size("dp")
    weight_term = lax.dot_general(
        mixed, grad_rows, (((0,), (0,)), ((), ())), preferred_element_type=jnp.float32
    )
    weight_plan = [("split", "dp", mask) for mask in axis_bits("dp")]
    weight_plan.append(("exchange", "ctx", 0))
    weight_state = [weight_term.reshape(dp_size, -1), 0]

    def slot(anchor):
        blocks, done = weight_state
        if done < len(weight_plan):
            blocks, anchor = lax.optimization_barrier((blocks, anchor))
            kind, axis, mask = weight_plan[done]
            if kind == "exchange":
                weight_state[0] = summed_by_exchange(blocks.reshape(-1), (axis,))
            else:
                weight_state[0] = plan_step(blocks, kind, axis, mask)
            weight_state[1] = done + 1
        return anchor

    query_sum = jnp.zeros((local_rows, width), jnp.float32)
    share_sum = None
    key_terms = [None, None, None]
    sent = [None, None, None]
    for distance in (2, 1, 0):
        visible, scores, weights, key_bucket_indicator = tiles[distance]
        pair = slot(window[distance])
        if distance == 0:
            sent[2], pair = lax.optimization_barrier((sent[2], pair))
        key_heads = pair[0].reshape(local_rows, head_count, head_dim)
        value_heads = pair[1].reshape(local_rows, head_count, head_dim)
        weight_grad = jnp.einsum(
            "ihd,jhd->hij", grad_heads, value_heads, preferred_element_type=jnp.float32
        )
        value_part = jnp.einsum(
            "hij,ihd->jhd", weights, grad_heads, preferred_element_type=jnp.float32
        ).reshape(local_rows, width)
        score_gradient = jnp.where(visible[None], weight_grad * silu_slope(scores), 0.0).astype(
            jnp.bfloat16
        )
        score_gradient = slot(score_gradient)
        query_part = jnp.einsum(
            "hij,jhd->ihd", score_gradient, key_heads, preferred_element_type=jnp.float32
        ).reshape(local_rows, width)
        key_part = (
            jnp.einsum(
                "hij,ihd->jhd", score_gradient, query_heads, preferred_element_type=jnp.float32
            ).reshape(local_rows, width)
            * scale
        )
        bucket_share_piece = jnp.einsum(
            "rmw,wx->rmx", score_gradient, key_bucket_indicator, preferred_element_type=jnp.float32
        )
        share_sum = bucket_share_piece if share_sum is None else share_sum + bucket_share_piece
        query_sum = query_sum + query_part
        key_terms[distance] = jnp.stack([key_part, value_part])
        if distance > 0:
            sent[distance] = passed_along(
                key_terms[distance].astype(jnp.bfloat16), "ctx", -distance
            )
    table_local = jnp.einsum(
        "qp,cqk->cpk", indicator_float, share_sum, precision=lax.Precision.HIGHEST
    )
    gathered = key_terms[0] + sent[1].astype(jnp.float32) + sent[2].astype(jnp.float32)
    query_grad = (query_sum * scale).astype(jnp.bfloat16)
    key_grad = gathered[0].astype(jnp.bfloat16)
    value_grad = gathered[1].astype(jnp.bfloat16)
    projection_grad = weight_state[0].reshape(width // dp_size, width)
    table_grad = summed_by_exchange(table_local.reshape(-1), ("ctx", "dp")).reshape(
        table_local.shape
    )
    return (
        query_grad[None],
        key_grad[None],
        value_grad[None],
        gate_grad[None],
        projection_grad,
        table_grad,
    )


def solution(mesh):
    return jax.shard_map(
        shards,
        mesh=mesh,
        in_specs=(
            P("dp", "ctx", None),
            P("dp", "ctx", None),
            P("dp", "ctx", None),
            P("dp", "ctx", None),
            P("dp", "ctx", None),
            P("dp", None),
            P("dp", None),
            P("dp", None, None),
            P(),
            P(),
        ),
        out_specs=(
            P("dp", "ctx", None),
            P("dp", "ctx", None),
            P("dp", "ctx", None),
            P("dp", "ctx", None),
            P("dp", None),
            P(),
        ),
        check_vma=False,
    )
```

```python
import jax
import jax.numpy as jnp
from jax import lax
from jax.sharding import PartitionSpec as P

BLK = 128


NORM_EPSILON = 1e-05


def passed_along(value, axis, by):
    length = lax.axis_size(axis)
    pairs = [(i, i + by) for i in range(length) if 0 <= i + by < length]
    return lax.ppermute(value, axis, pairs)


def exchanged(value, axis, mask):
    length = lax.axis_size(axis)
    pairs = [(i, i ^ mask) for i in range(length)]
    return lax.ppermute(value, axis, pairs)


def axis_bits(axis):
    length = lax.axis_size(axis)
    bits = []
    mask = 1
    while mask < length:
        bits.append(mask)
        mask *= 2
    return bits


def scatter_blocks(blocks, axis):
    index = lax.axis_index(axis)
    for mask in axis_bits(axis):
        bit = (index // mask) % 2
        pairs = blocks.reshape(blocks.shape[0] // 2, 2, blocks.shape[1])
        keep = lax.dynamic_index_in_dim(pairs, bit, axis=1, keepdims=False)
        send = lax.dynamic_index_in_dim(pairs, 1 - bit, axis=1, keepdims=False)
        blocks = keep + exchanged(send, axis, mask)
    return blocks[0]


def gather_blocks(chunk, axis):
    index = lax.axis_index(axis)
    held = chunk[None]
    for mask in reversed(axis_bits(axis)):
        bit = (index // mask) % 2
        other = exchanged(held, axis, mask)
        low = jnp.where(bit == 0, held, other)
        high = jnp.where(bit == 0, other, held)
        held = jnp.stack([low, high], axis=1).reshape(held.shape[0] * 2, held.shape[1])
    return held


def summed_over(flat, axis):
    size = lax.axis_size(axis)
    part = scatter_blocks(flat.reshape(size, flat.shape[0] // size), axis)
    return gather_blocks(part, axis).reshape(flat.shape)


def plan_step(blocks, kind, axis, mask):
    bit = (lax.axis_index(axis) // mask) % 2
    if kind == "split":
        if blocks.shape[0] == 1:
            blocks = blocks.reshape(2, -1)
        pairs = blocks.reshape(blocks.shape[0] // 2, 2, blocks.shape[1])
        keep = lax.dynamic_index_in_dim(pairs, bit, axis=1, keepdims=False)
        send = lax.dynamic_index_in_dim(pairs, 1 - bit, axis=1, keepdims=False)
        return keep + exchanged(send, axis, mask)
    other = exchanged(blocks, axis, mask)
    low = jnp.where(bit == 0, blocks, other)
    high = jnp.where(bit == 0, other, blocks)
    return jnp.concatenate([low, high], axis=1)


def summed_by_exchange(flat, axes):
    size = 1
    for axis in axes:
        size *= lax.axis_size(axis)
    pieces = lax.all_to_all(flat.reshape(size, -1), axes, 0, 0, tiled=True)
    total = jnp.sum(pieces, axis=0, keepdims=True)
    spread = jnp.broadcast_to(total.astype(jnp.bfloat16), pieces.shape)
    gathered = lax.all_to_all(spread, axes, 0, 0, tiled=True)
    return gathered.astype(flat.dtype).reshape(flat.shape)


def silu_slope(scores):
    sigmoid = jax.nn.sigmoid(scores)
    return sigmoid * (1.0 + scores * (1.0 - sigmoid))


def expand_blocks(block_rows, block_size):
    return jnp.repeat(jnp.repeat(block_rows, block_size, axis=0), block_size, axis=1)


def shards(
    queries,
    keys,
    values,
    gates,
    out_grad,
    time_bucket,
    lengths,
    block_map,
    bucket_bias_matrix,
    w_out,
):
    query_rows = queries[0]
    key_rows = keys[0]
    value_rows = values[0]
    gate_rows = gates[0]
    grad_rows = out_grad[0]
    local_rows, width = query_rows.shape
    head_count = bucket_bias_matrix.shape[0]
    bucket_count = bucket_bias_matrix.shape[1]
    head_dim = width // head_count
    scale = head_dim ** (-0.5)
    blocks_here = local_rows // BLK
    cycle_index = lax.axis_index("ctx")
    row_start = cycle_index * local_rows
    offsets = jnp.cumsum(lengths[0], dtype=jnp.int32) - lengths[0]

    def segment_of(positions):
        return jnp.sum(
            (positions[:, None] >= offsets[None, 1:]).astype(jnp.int32), axis=1, dtype=jnp.int32
        )

    bucket_ids = jnp.arange(bucket_count, dtype=jnp.int32)
    query_pos = row_start + jnp.arange(local_rows, dtype=jnp.int32)
    query_seg = segment_of(query_pos)
    query_bucket = lax.dynamic_slice_in_dim(time_bucket[0], row_start, local_rows, 0)
    query_bucket_indicator = (query_bucket[:, None] == bucket_ids[None, :]).astype(jnp.bfloat16)
    bias_matrix_rows = jnp.einsum(
        "lf,sfq->slq",
        query_bucket_indicator,
        bucket_bias_matrix,
        preferred_element_type=jnp.float32,
    ).astype(jnp.bfloat16)
    map_rows = lax.dynamic_slice_in_dim(block_map[0], cycle_index * blocks_here, blocks_here, 0)
    query_heads = query_rows.reshape(local_rows, head_count, head_dim)
    stacked = jnp.stack([key_rows, value_rows])
    window = [stacked, passed_along(stacked, "ctx", 1), passed_along(stacked, "ctx", 2)]
    tiles = []
    attended = jnp.zeros((local_rows, head_count, head_dim), jnp.float32)
    for distance in range(3):
        key_first = row_start - distance * local_rows
        key_pos = key_first + jnp.arange(local_rows, dtype=jnp.int32)
        safe_first = jnp.maximum(key_first, 0)
        key_bucket = lax.dynamic_slice_in_dim(time_bucket[0], safe_first, local_rows, 0)
        key_bucket_indicator = (key_bucket[:, None] == bucket_ids[None, :]).astype(jnp.bfloat16)
        map_cols = lax.dynamic_slice_in_dim(map_rows, safe_first // BLK, blocks_here, 1)
        same_block = query_pos[:, None] // BLK == key_pos[None, :] // BLK
        key_visible = (
            (query_seg[:, None] == segment_of(key_pos)[None, :])
            & (key_pos[None, :] <= query_pos[:, None])
            & (key_pos[None, :] >= 0)
            & ((expand_blocks(map_cols, BLK) == 1) | same_block)
        )
        key_bias_terms = jnp.einsum(
            "vqx,px->vqp",
            bias_matrix_rows,
            key_bucket_indicator,
            preferred_element_type=jnp.float32,
        )
        visible, bias_terms, key_bucket_indicator = (
            key_visible,
            key_bias_terms,
            key_bucket_indicator,
        )
        forward_pair = window[distance]
        forward_key_heads = forward_pair[0].reshape(local_rows, head_count, head_dim)
        forward_value_heads = forward_pair[1].reshape(local_rows, head_count, head_dim)
        forward_scores = (
            jnp.einsum(
                "ihd,jhd->hij", query_heads, forward_key_heads, preferred_element_type=jnp.float32
            )
            * scale
            + bias_terms
        )
        forward_weights = jnp.where(visible[None], jax.nn.silu(forward_scores), 0.0).astype(
            jnp.bfloat16
        )
        attended_part = jnp.einsum(
            "hij,jhd->ihd", forward_weights, forward_value_heads, preferred_element_type=jnp.float32
        )
        attended = attended + attended_part
        tiles.append((visible, forward_scores, forward_weights, key_bucket_indicator))
    attended = attended.reshape(local_rows, width)
    centered = attended - jnp.mean(attended, axis=1, keepdims=True)
    inverse = lax.rsqrt(jnp.mean(centered * centered, axis=1, keepdims=True) + NORM_EPSILON)
    normed = centered * inverse
    dz_rows = lax.dot_general(
        grad_rows, w_out, (((1,), (1,)), ((), ())), preferred_element_type=jnp.float32
    )
    gate_float = gate_rows.astype(jnp.float32)
    gate_grad = (dz_rows * normed).astype(jnp.bfloat16)
    mixed = (normed * gate_float).astype(jnp.bfloat16)
    lifted = dz_rows * gate_float
    attended_grad = (
        (
            lifted
            - jnp.mean(lifted, axis=1, keepdims=True)
            - normed * jnp.mean(lifted * normed, axis=1, keepdims=True)
        )
        * inverse
    ).astype(jnp.bfloat16)
    grad_heads = attended_grad.reshape(local_rows, head_count, head_dim)
    indicator_float = query_bucket_indicator.astype(jnp.float32)
    dp_size = lax.axis_size("dp")
    weight_term = lax.dot_general(
        mixed, grad_rows, (((0,), (0,)), ((), ())), preferred_element_type=jnp.float32
    )
    weight_plan = [("split", "dp", mask) for mask in axis_bits("dp")]
    weight_plan.append(("exchange", "ctx", 0))
    weight_state = [weight_term.reshape(dp_size, -1), 0]

    def slot(anchor):
        blocks, done = weight_state
        if done < len(weight_plan):
            blocks, anchor = lax.optimization_barrier((blocks, anchor))
            kind, axis, mask = weight_plan[done]
            if kind == "exchange":
                weight_state[0] = summed_by_exchange(blocks.reshape(-1), (axis,))
            else:
                weight_state[0] = plan_step(blocks, kind, axis, mask)
            weight_state[1] = done + 1
        return anchor

    query_sum = jnp.zeros((local_rows, width), jnp.float32)
    share_sum = None
    key_terms = [None, None, None]
    sent = [None, None, None]
    for distance in (2, 1, 0):
        visible, scores, weights, key_bucket_indicator = tiles[distance]
        pair = slot(window[distance])
        if distance == 0:
            sent[2], pair = lax.optimization_barrier((sent[2], pair))
        key_heads = pair[0].reshape(local_rows, head_count, head_dim)
        value_heads = pair[1].reshape(local_rows, head_count, head_dim)
        weight_grad = jnp.einsum(
            "ihd,jhd->hij", grad_heads, value_heads, preferred_element_type=jnp.float32
        )
        value_part = jnp.einsum(
            "hij,ihd->jhd", weights, grad_heads, preferred_element_type=jnp.float32
        ).reshape(local_rows, width)
        score_gradient = jnp.where(visible[None], weight_grad * silu_slope(scores), 0.0).astype(
            jnp.bfloat16
        )
        score_gradient = slot(score_gradient)
        query_part = jnp.einsum(
            "hij,jhd->ihd", score_gradient, key_heads, preferred_element_type=jnp.float32
        ).reshape(local_rows, width)
        key_part = (
            jnp.einsum(
                "hij,ihd->jhd", score_gradient, query_heads, preferred_element_type=jnp.float32
            ).reshape(local_rows, width)
            * scale
        )
        bucket_share_piece = jnp.einsum(
            "rmw,wx->rmx", score_gradient, key_bucket_indicator, preferred_element_type=jnp.float32
        )
        share_sum = bucket_share_piece if share_sum is None else share_sum + bucket_share_piece
        query_sum = query_sum + query_part
        key_terms[distance] = jnp.stack([key_part, value_part])
        if distance > 0:
            sent[distance] = passed_along(
                key_terms[distance].astype(jnp.bfloat16), "ctx", -distance
            )
    table_local = jnp.einsum(
        "qp,cqk->cpk", indicator_float, share_sum, precision=lax.Precision.HIGHEST
    )
    gathered = key_terms[0] + sent[1].astype(jnp.float32) + sent[2].astype(jnp.float32)
    query_grad = (query_sum * scale).astype(jnp.bfloat16)
    key_grad = gathered[0].astype(jnp.bfloat16)
    value_grad = gathered[1].astype(jnp.bfloat16)
    projection_grad = weight_state[0].reshape(width // dp_size, width)
    table_grad = summed_by_exchange(table_local.reshape(-1), ("ctx", "dp")).reshape(
        table_local.shape
    )
    return (
        query_grad[None],
        key_grad[None],
        value_grad[None],
        gate_grad[None],
        projection_grad,
        table_grad,
    )


def solution(mesh):
    return jax.shard_map(
        shards,
        mesh=mesh,
        in_specs=(
            P("dp", "ctx", None),
            P("dp", "ctx", None),
            P("dp", "ctx", None),
            P("dp", "ctx", None),
            P("dp", "ctx", None),
            P("dp", None),
            P("dp", None),
            P("dp", None, None),
            P(),
            P(),
        ),
        out_specs=(
            P("dp", "ctx", None),
            P("dp", "ctx", None),
            P("dp", "ctx", None),
            P("dp", "ctx", None),
            P("dp", None),
            P(),
        ),
        check_vma=False,
    )
```

```python
import jax
import jax.numpy as jnp
from jax import lax
from jax.sharding import PartitionSpec as P

BLK = 128


NORM_EPSILON = 1e-05


def passed_along(value, axis, by):
    length = lax.axis_size(axis)
    pairs = [(i, i + by) for i in range(length) if 0 <= i + by < length]
    return lax.ppermute(value, axis, pairs)


def exchanged(value, axis, mask):
    length = lax.axis_size(axis)
    pairs = [(i, i ^ mask) for i in range(length)]
    return lax.ppermute(value, axis, pairs)


def axis_bits(axis):
    length = lax.axis_size(axis)
    bits = []
    mask = 1
    while mask < length:
        bits.append(mask)
        mask *= 2
    return bits


def scatter_blocks(blocks, axis):
    index = lax.axis_index(axis)
    for mask in axis_bits(axis):
        bit = (index // mask) % 2
        pairs = blocks.reshape(blocks.shape[0] // 2, 2, blocks.shape[1])
        keep = lax.dynamic_index_in_dim(pairs, bit, axis=1, keepdims=False)
        send = lax.dynamic_index_in_dim(pairs, 1 - bit, axis=1, keepdims=False)
        blocks = keep + exchanged(send, axis, mask)
    return blocks[0]


def gather_blocks(chunk, axis):
    index = lax.axis_index(axis)
    held = chunk[None]
    for mask in reversed(axis_bits(axis)):
        bit = (index // mask) % 2
        other = exchanged(held, axis, mask)
        low = jnp.where(bit == 0, held, other)
        high = jnp.where(bit == 0, other, held)
        held = jnp.stack([low, high], axis=1).reshape(held.shape[0] * 2, held.shape[1])
    return held


def summed_over(flat, axis):
    size = lax.axis_size(axis)
    part = scatter_blocks(flat.reshape(size, flat.shape[0] // size), axis)
    return gather_blocks(part, axis).reshape(flat.shape)


def plan_step(blocks, kind, axis, mask):
    bit = (lax.axis_index(axis) // mask) % 2
    if kind == "split":
        if blocks.shape[0] == 1:
            blocks = blocks.reshape(2, -1)
        pairs = blocks.reshape(blocks.shape[0] // 2, 2, blocks.shape[1])
        keep = lax.dynamic_index_in_dim(pairs, bit, axis=1, keepdims=False)
        send = lax.dynamic_index_in_dim(pairs, 1 - bit, axis=1, keepdims=False)
        return keep + exchanged(send, axis, mask)
    other = exchanged(blocks, axis, mask)
    low = jnp.where(bit == 0, blocks, other)
    high = jnp.where(bit == 0, other, blocks)
    return jnp.concatenate([low, high], axis=1)


def summed_by_exchange(flat, axes):
    size = 1
    for axis in axes:
        size *= lax.axis_size(axis)
    pieces = lax.all_to_all(flat.reshape(size, -1), axes, 0, 0, tiled=True)
    total = jnp.sum(pieces, axis=0, keepdims=True)
    spread = jnp.broadcast_to(total.astype(jnp.bfloat16), pieces.shape)
    gathered = lax.all_to_all(spread, axes, 0, 0, tiled=True)
    return gathered.astype(flat.dtype).reshape(flat.shape)


def silu_slope(scores):
    sigmoid = jax.nn.sigmoid(scores)
    return sigmoid * (1.0 + scores * (1.0 - sigmoid))


def expand_blocks(block_rows, block_size):
    return jnp.repeat(jnp.repeat(block_rows, block_size, axis=0), block_size, axis=1)


def shards(
    queries,
    keys,
    values,
    gates,
    out_grad,
    time_bucket,
    lengths,
    block_map,
    bucket_bias_matrix,
    w_out,
):
    query_rows = queries[0]
    key_rows = keys[0]
    value_rows = values[0]
    gate_rows = gates[0]
    grad_rows = out_grad[0]
    local_rows, width = query_rows.shape
    head_count = bucket_bias_matrix.shape[0]
    bucket_count = bucket_bias_matrix.shape[1]
    head_dim = width // head_count
    scale = head_dim ** (-0.5)
    blocks_here = local_rows // BLK
    cycle_index = lax.axis_index("ctx")
    row_start = cycle_index * local_rows
    offsets = jnp.cumsum(lengths[0], dtype=jnp.int32) - lengths[0]

    def segment_of(positions):
        return jnp.sum(
            (positions[:, None] >= offsets[None, 1:]).astype(jnp.int32), axis=1, dtype=jnp.int32
        )

    bucket_ids = jnp.arange(bucket_count, dtype=jnp.int32)
    query_pos = row_start + jnp.arange(local_rows, dtype=jnp.int32)
    query_seg = segment_of(query_pos)
    query_bucket = lax.dynamic_slice_in_dim(time_bucket[0], row_start, local_rows, 0)
    query_bucket_indicator = (query_bucket[:, None] == bucket_ids[None, :]).astype(jnp.bfloat16)
    bias_matrix_rows = jnp.einsum(
        "lf,sfq->slq",
        query_bucket_indicator,
        bucket_bias_matrix,
        preferred_element_type=jnp.float32,
    ).astype(jnp.bfloat16)
    map_rows = lax.dynamic_slice_in_dim(block_map[0], cycle_index * blocks_here, blocks_here, 0)
    query_heads = query_rows.reshape(local_rows, head_count, head_dim)
    stacked = jnp.stack([key_rows, value_rows])
    window = [stacked, passed_along(stacked, "ctx", 1), passed_along(stacked, "ctx", 2)]
    tiles = []
    attended = jnp.zeros((local_rows, head_count, head_dim), jnp.float32)
    for distance in range(3):
        key_first = row_start - distance * local_rows
        key_pos = key_first + jnp.arange(local_rows, dtype=jnp.int32)
        safe_first = jnp.maximum(key_first, 0)
        key_bucket = lax.dynamic_slice_in_dim(time_bucket[0], safe_first, local_rows, 0)
        key_bucket_indicator = (key_bucket[:, None] == bucket_ids[None, :]).astype(jnp.bfloat16)
        map_cols = lax.dynamic_slice_in_dim(map_rows, safe_first // BLK, blocks_here, 1)
        same_block = query_pos[:, None] // BLK == key_pos[None, :] // BLK
        key_visible = (
            (query_seg[:, None] == segment_of(key_pos)[None, :])
            & (key_pos[None, :] <= query_pos[:, None])
            & (key_pos[None, :] >= 0)
            & ((expand_blocks(map_cols, BLK) == 1) | same_block)
        )
        key_bias_terms = jnp.einsum(
            "vqx,px->vqp",
            bias_matrix_rows,
            key_bucket_indicator,
            preferred_element_type=jnp.float32,
        )
        visible, bias_terms, key_bucket_indicator = (
            key_visible,
            key_bias_terms,
            key_bucket_indicator,
        )
        forward_pair = window[distance]
        forward_key_heads = forward_pair[0].reshape(local_rows, head_count, head_dim)
        forward_value_heads = forward_pair[1].reshape(local_rows, head_count, head_dim)
        forward_scores = (
            jnp.einsum(
                "ihd,jhd->hij", query_heads, forward_key_heads, preferred_element_type=jnp.float32
            )
            * scale
            + bias_terms
        )
        forward_weights = jnp.where(visible[None], jax.nn.silu(forward_scores), 0.0).astype(
            jnp.bfloat16
        )
        attended_part = jnp.einsum(
            "hij,jhd->ihd", forward_weights, forward_value_heads, preferred_element_type=jnp.float32
        )
        attended = attended + attended_part
        tiles.append((visible, forward_scores, forward_weights, key_bucket_indicator))
    attended = attended.reshape(local_rows, width)
    centered = attended - jnp.mean(attended, axis=1, keepdims=True)
    inverse = lax.rsqrt(jnp.mean(centered * centered, axis=1, keepdims=True) + NORM_EPSILON)
    normed = centered * inverse
    dz_rows = lax.dot_general(
        grad_rows, w_out, (((1,), (1,)), ((), ())), preferred_element_type=jnp.float32
    )
    gate_float = gate_rows.astype(jnp.float32)
    gate_grad = (dz_rows * normed).astype(jnp.bfloat16)
    mixed = (normed * gate_float).astype(jnp.bfloat16)
    lifted = dz_rows * gate_float
    attended_grad = (
        (
            lifted
            - jnp.mean(lifted, axis=1, keepdims=True)
            - normed * jnp.mean(lifted * normed, axis=1, keepdims=True)
        )
        * inverse
    ).astype(jnp.bfloat16)
    grad_heads = attended_grad.reshape(local_rows, head_count, head_dim)
    indicator_float = query_bucket_indicator.astype(jnp.float32)
    dp_size = lax.axis_size("dp")
    weight_term = lax.dot_general(
        mixed, grad_rows, (((0,), (0,)), ((), ())), preferred_element_type=jnp.float32
    )
    weight_plan = [("split", "dp", mask) for mask in axis_bits("dp")]
    weight_plan.append(("exchange", "ctx", 0))
    weight_state = [weight_term.reshape(dp_size, -1), 0]

    def slot(anchor):
        blocks, done = weight_state
        if done < len(weight_plan):
            blocks, anchor = lax.optimization_barrier((blocks, anchor))
            kind, axis, mask = weight_plan[done]
            if kind == "exchange":
                weight_state[0] = summed_by_exchange(blocks.reshape(-1), (axis,))
            else:
                weight_state[0] = plan_step(blocks, kind, axis, mask)
            weight_state[1] = done + 1
        return anchor

    grad_heads = slot(grad_heads)
    query_sum = jnp.zeros((local_rows, width), jnp.float32)
    share_sum = None
    key_terms = [None, None, None]
    sent = [None, None, None]
    for distance in (2, 1, 0):
        visible, scores, weights, key_bucket_indicator = tiles[distance]
        pair = slot(window[distance])
        if distance == 0:
            sent[2], pair = lax.optimization_barrier((sent[2], pair))
        key_heads = pair[0].reshape(local_rows, head_count, head_dim)
        value_heads = pair[1].reshape(local_rows, head_count, head_dim)
        weight_grad = jnp.einsum(
            "ihd,jhd->hij", grad_heads, value_heads, preferred_element_type=jnp.float32
        )
        value_part = jnp.einsum(
            "hij,ihd->jhd", weights, grad_heads, preferred_element_type=jnp.float32
        ).reshape(local_rows, width)
        score_gradient = jnp.where(visible[None], weight_grad * silu_slope(scores), 0.0).astype(
            jnp.bfloat16
        )
        score_gradient = slot(score_gradient)
        query_part = jnp.einsum(
            "hij,jhd->ihd", score_gradient, key_heads, preferred_element_type=jnp.float32
        ).reshape(local_rows, width)
        key_part = (
            jnp.einsum(
                "hij,ihd->jhd", score_gradient, query_heads, preferred_element_type=jnp.float32
            ).reshape(local_rows, width)
            * scale
        )
        bucket_share_piece = jnp.einsum(
            "rmw,wx->rmx", score_gradient, key_bucket_indicator, preferred_element_type=jnp.float32
        )
        share_sum = bucket_share_piece if share_sum is None else share_sum + bucket_share_piece
        query_sum = query_sum + query_part
        key_terms[distance] = jnp.stack([key_part, value_part])
        if distance > 0:
            sent[distance] = passed_along(
                key_terms[distance].astype(jnp.bfloat16), "ctx", -distance
            )
    table_local = jnp.einsum(
        "qp,cqk->cpk", indicator_float, share_sum, precision=lax.Precision.HIGHEST
    )
    gathered = key_terms[0] + sent[1].astype(jnp.float32) + sent[2].astype(jnp.float32)
    query_grad = (query_sum * scale).astype(jnp.bfloat16)
    key_grad = gathered[0].astype(jnp.bfloat16)
    value_grad = gathered[1].astype(jnp.bfloat16)
    projection_grad = weight_state[0].reshape(width // dp_size, width)
    table_grad = summed_by_exchange(table_local.reshape(-1), ("ctx", "dp")).reshape(
        table_local.shape
    )
    return (
        query_grad[None],
        key_grad[None],
        value_grad[None],
        gate_grad[None],
        projection_grad,
        table_grad,
    )


def solution(mesh):
    return jax.shard_map(
        shards,
        mesh=mesh,
        in_specs=(
            P("dp", "ctx", None),
            P("dp", "ctx", None),
            P("dp", "ctx", None),
            P("dp", "ctx", None),
            P("dp", "ctx", None),
            P("dp", None),
            P("dp", None),
            P("dp", None, None),
            P(),
            P(),
        ),
        out_specs=(
            P("dp", "ctx", None),
            P("dp", "ctx", None),
            P("dp", "ctx", None),
            P("dp", "ctx", None),
            P("dp", None),
            P(),
        ),
        check_vma=False,
    )
```

```python
import jax
import jax.numpy as jnp
from jax import lax
from jax.sharding import PartitionSpec as P

BLK = 128


NORM_EPSILON = 1e-05


def passed_along(value, axis, by):
    length = lax.axis_size(axis)
    pairs = [(i, i + by) for i in range(length) if 0 <= i + by < length]
    return lax.ppermute(value, axis, pairs)


def exchanged(value, axis, mask):
    length = lax.axis_size(axis)
    pairs = [(i, i ^ mask) for i in range(length)]
    return lax.ppermute(value, axis, pairs)


def axis_bits(axis):
    length = lax.axis_size(axis)
    bits = []
    mask = 1
    while mask < length:
        bits.append(mask)
        mask *= 2
    return bits


def scatter_blocks(blocks, axis):
    index = lax.axis_index(axis)
    for mask in axis_bits(axis):
        bit = (index // mask) % 2
        pairs = blocks.reshape(blocks.shape[0] // 2, 2, blocks.shape[1])
        keep = lax.dynamic_index_in_dim(pairs, bit, axis=1, keepdims=False)
        send = lax.dynamic_index_in_dim(pairs, 1 - bit, axis=1, keepdims=False)
        blocks = keep + exchanged(send, axis, mask)
    return blocks[0]


def gather_blocks(chunk, axis):
    index = lax.axis_index(axis)
    held = chunk[None]
    for mask in reversed(axis_bits(axis)):
        bit = (index // mask) % 2
        other = exchanged(held, axis, mask)
        low = jnp.where(bit == 0, held, other)
        high = jnp.where(bit == 0, other, held)
        held = jnp.stack([low, high], axis=1).reshape(held.shape[0] * 2, held.shape[1])
    return held


def summed_over(flat, axis):
    size = lax.axis_size(axis)
    part = scatter_blocks(flat.reshape(size, flat.shape[0] // size), axis)
    return gather_blocks(part, axis).reshape(flat.shape)


def plan_step(blocks, kind, axis, mask):
    bit = (lax.axis_index(axis) // mask) % 2
    if kind == "split":
        if blocks.shape[0] == 1:
            blocks = blocks.reshape(2, -1)
        pairs = blocks.reshape(blocks.shape[0] // 2, 2, blocks.shape[1])
        keep = lax.dynamic_index_in_dim(pairs, bit, axis=1, keepdims=False)
        send = lax.dynamic_index_in_dim(pairs, 1 - bit, axis=1, keepdims=False)
        return keep + exchanged(send, axis, mask)
    other = exchanged(blocks, axis, mask)
    low = jnp.where(bit == 0, blocks, other)
    high = jnp.where(bit == 0, other, blocks)
    return jnp.concatenate([low, high], axis=1)


def summed_by_exchange(flat, axes):
    size = 1
    for axis in axes:
        size *= lax.axis_size(axis)
    outgoing = flat.reshape(size, -1).astype(jnp.bfloat16)
    pieces = lax.all_to_all(outgoing, axes, 0, 0, tiled=True)
    total = jnp.sum(pieces.astype(flat.dtype), axis=0, keepdims=True)
    spread = jnp.broadcast_to(total.astype(jnp.bfloat16), pieces.shape)
    gathered = lax.all_to_all(spread, axes, 0, 0, tiled=True)
    return gathered.astype(flat.dtype).reshape(flat.shape)


def silu_slope(scores):
    sigmoid = jax.nn.sigmoid(scores)
    return sigmoid * (1.0 + scores * (1.0 - sigmoid))


def expand_blocks(block_rows, block_size):
    return jnp.repeat(jnp.repeat(block_rows, block_size, axis=0), block_size, axis=1)


def shards(
    queries,
    keys,
    values,
    gates,
    out_grad,
    time_bucket,
    lengths,
    block_map,
    bucket_bias_matrix,
    w_out,
):
    query_rows = queries[0]
    key_rows = keys[0]
    value_rows = values[0]
    gate_rows = gates[0]
    grad_rows = out_grad[0]
    local_rows, width = query_rows.shape
    head_count = bucket_bias_matrix.shape[0]
    bucket_count = bucket_bias_matrix.shape[1]
    head_dim = width // head_count
    scale = head_dim ** (-0.5)
    blocks_here = local_rows // BLK
    cycle_index = lax.axis_index("ctx")
    row_start = cycle_index * local_rows
    offsets = jnp.cumsum(lengths[0], dtype=jnp.int32) - lengths[0]

    def segment_of(positions):
        return jnp.sum(
            (positions[:, None] >= offsets[None, 1:]).astype(jnp.int32), axis=1, dtype=jnp.int32
        )

    bucket_ids = jnp.arange(bucket_count, dtype=jnp.int32)
    query_pos = row_start + jnp.arange(local_rows, dtype=jnp.int32)
    query_seg = segment_of(query_pos)
    query_bucket = lax.dynamic_slice_in_dim(time_bucket[0], row_start, local_rows, 0)
    query_bucket_indicator = (query_bucket[:, None] == bucket_ids[None, :]).astype(jnp.bfloat16)
    bias_matrix_rows = jnp.einsum(
        "lf,sfq->slq",
        query_bucket_indicator,
        bucket_bias_matrix,
        preferred_element_type=jnp.float32,
    ).astype(jnp.bfloat16)
    map_rows = lax.dynamic_slice_in_dim(block_map[0], cycle_index * blocks_here, blocks_here, 0)
    query_heads = query_rows.reshape(local_rows, head_count, head_dim)
    stacked = jnp.stack([key_rows, value_rows])
    window = [stacked, passed_along(stacked, "ctx", 1), passed_along(stacked, "ctx", 2)]
    tiles = []
    attended = jnp.zeros((local_rows, head_count, head_dim), jnp.float32)
    for distance in range(3):
        key_first = row_start - distance * local_rows
        key_pos = key_first + jnp.arange(local_rows, dtype=jnp.int32)
        safe_first = jnp.maximum(key_first, 0)
        key_bucket = lax.dynamic_slice_in_dim(time_bucket[0], safe_first, local_rows, 0)
        key_bucket_indicator = (key_bucket[:, None] == bucket_ids[None, :]).astype(jnp.bfloat16)
        map_cols = lax.dynamic_slice_in_dim(map_rows, safe_first // BLK, blocks_here, 1)
        same_block = query_pos[:, None] // BLK == key_pos[None, :] // BLK
        key_visible = (
            (query_seg[:, None] == segment_of(key_pos)[None, :])
            & (key_pos[None, :] <= query_pos[:, None])
            & (key_pos[None, :] >= 0)
            & ((expand_blocks(map_cols, BLK) == 1) | same_block)
        )
        key_bias_terms = jnp.einsum(
            "vqx,px->vqp",
            bias_matrix_rows,
            key_bucket_indicator,
            preferred_element_type=jnp.float32,
        )
        visible, bias_terms, key_bucket_indicator = (
            key_visible,
            key_bias_terms,
            key_bucket_indicator,
        )
        forward_pair = window[distance]
        forward_key_heads = forward_pair[0].reshape(local_rows, head_count, head_dim)
        forward_value_heads = forward_pair[1].reshape(local_rows, head_count, head_dim)
        forward_scores = (
            jnp.einsum(
                "ihd,jhd->hij", query_heads, forward_key_heads, preferred_element_type=jnp.float32
            )
            * scale
            + bias_terms
        )
        forward_weights = jnp.where(visible[None], jax.nn.silu(forward_scores), 0.0).astype(
            jnp.bfloat16
        )
        attended_part = jnp.einsum(
            "hij,jhd->ihd", forward_weights, forward_value_heads, preferred_element_type=jnp.float32
        )
        attended = attended + attended_part
        tiles.append((visible, forward_scores, forward_weights, key_bucket_indicator))
    attended = attended.reshape(local_rows, width)
    centered = attended - jnp.mean(attended, axis=1, keepdims=True)
    inverse = lax.rsqrt(jnp.mean(centered * centered, axis=1, keepdims=True) + NORM_EPSILON)
    normed = centered * inverse
    dz_rows = lax.dot_general(
        grad_rows, w_out, (((1,), (1,)), ((), ())), preferred_element_type=jnp.float32
    )
    gate_float = gate_rows.astype(jnp.float32)
    gate_grad = (dz_rows * normed).astype(jnp.bfloat16)
    mixed = (normed * gate_float).astype(jnp.bfloat16)
    lifted = dz_rows * gate_float
    attended_grad = (
        (
            lifted
            - jnp.mean(lifted, axis=1, keepdims=True)
            - normed * jnp.mean(lifted * normed, axis=1, keepdims=True)
        )
        * inverse
    ).astype(jnp.bfloat16)
    grad_heads = attended_grad.reshape(local_rows, head_count, head_dim)
    indicator_float = query_bucket_indicator.astype(jnp.float32)
    dp_size = lax.axis_size("dp")
    weight_term = lax.dot_general(
        mixed, grad_rows, (((0,), (0,)), ((), ())), preferred_element_type=jnp.float32
    )
    weight_plan = [("split", "dp", mask) for mask in axis_bits("dp")]
    weight_plan.append(("exchange", "ctx", 0))
    weight_state = [weight_term.reshape(dp_size, -1), 0]

    def slot(anchor):
        blocks, done = weight_state
        if done < len(weight_plan):
            blocks, anchor = lax.optimization_barrier((blocks, anchor))
            kind, axis, mask = weight_plan[done]
            if kind == "exchange":
                weight_state[0] = summed_by_exchange(blocks.reshape(-1), (axis,))
            else:
                weight_state[0] = plan_step(blocks, kind, axis, mask)
            weight_state[1] = done + 1
        return anchor

    query_sum = jnp.zeros((local_rows, width), jnp.float32)
    share_sum = None
    key_terms = [None, None, None]
    sent = [None, None, None]
    for distance in (2, 1, 0):
        visible, scores, weights, key_bucket_indicator = tiles[distance]
        pair = slot(window[distance])
        if distance == 0:
            sent[2], pair = lax.optimization_barrier((sent[2], pair))
        key_heads = pair[0].reshape(local_rows, head_count, head_dim)
        value_heads = pair[1].reshape(local_rows, head_count, head_dim)
        weight_grad = jnp.einsum(
            "ihd,jhd->hij", grad_heads, value_heads, preferred_element_type=jnp.float32
        )
        value_part = jnp.einsum(
            "hij,ihd->jhd", weights, grad_heads, preferred_element_type=jnp.float32
        ).reshape(local_rows, width)
        score_gradient = jnp.where(visible[None], weight_grad * silu_slope(scores), 0.0).astype(
            jnp.bfloat16
        )
        score_gradient = slot(score_gradient)
        query_part = jnp.einsum(
            "hij,jhd->ihd", score_gradient, key_heads, preferred_element_type=jnp.float32
        ).reshape(local_rows, width)
        key_part = (
            jnp.einsum(
                "hij,ihd->jhd", score_gradient, query_heads, preferred_element_type=jnp.float32
            ).reshape(local_rows, width)
            * scale
        )
        bucket_share_piece = jnp.einsum(
            "rmw,wx->rmx", score_gradient, key_bucket_indicator, preferred_element_type=jnp.float32
        )
        share_sum = bucket_share_piece if share_sum is None else share_sum + bucket_share_piece
        query_sum = query_sum + query_part
        key_terms[distance] = jnp.stack([key_part, value_part])
        if distance > 0:
            sent[distance] = passed_along(
                key_terms[distance].astype(jnp.bfloat16), "ctx", -distance
            )
    table_local = jnp.einsum(
        "qp,cqk->cpk", indicator_float, share_sum, precision=lax.Precision.HIGHEST
    )
    gathered = key_terms[0] + sent[1].astype(jnp.float32) + sent[2].astype(jnp.float32)
    query_grad = (query_sum * scale).astype(jnp.bfloat16)
    key_grad = gathered[0].astype(jnp.bfloat16)
    value_grad = gathered[1].astype(jnp.bfloat16)
    projection_grad = weight_state[0].reshape(width // dp_size, width)
    table_grad = summed_by_exchange(table_local.reshape(-1), ("ctx", "dp")).reshape(
        table_local.shape
    )
    return (
        query_grad[None],
        key_grad[None],
        value_grad[None],
        gate_grad[None],
        projection_grad,
        table_grad,
    )


def solution(mesh):
    return jax.shard_map(
        shards,
        mesh=mesh,
        in_specs=(
            P("dp", "ctx", None),
            P("dp", "ctx", None),
            P("dp", "ctx", None),
            P("dp", "ctx", None),
            P("dp", "ctx", None),
            P("dp", None),
            P("dp", None),
            P("dp", None, None),
            P(),
            P(),
        ),
        out_specs=(
            P("dp", "ctx", None),
            P("dp", "ctx", None),
            P("dp", "ctx", None),
            P("dp", "ctx", None),
            P("dp", None),
            P(),
        ),
        check_vma=False,
    )
```

```python
import jax
import jax.numpy as jnp
from jax import lax
from jax.sharding import PartitionSpec as P

BLK = 128


NORM_EPSILON = 1e-05


def passed_along(value, axis, by):
    length = lax.axis_size(axis)
    pairs = [(i, i + by) for i in range(length) if 0 <= i + by < length]
    return lax.ppermute(value, axis, pairs)


def exchanged(value, axis, mask):
    length = lax.axis_size(axis)
    pairs = [(i, i ^ mask) for i in range(length)]
    return lax.ppermute(value, axis, pairs)


def axis_bits(axis):
    length = lax.axis_size(axis)
    bits = []
    mask = 1
    while mask < length:
        bits.append(mask)
        mask *= 2
    return bits


def scatter_blocks(blocks, axis):
    index = lax.axis_index(axis)
    for mask in axis_bits(axis):
        bit = (index // mask) % 2
        pairs = blocks.reshape(blocks.shape[0] // 2, 2, blocks.shape[1])
        keep = lax.dynamic_index_in_dim(pairs, bit, axis=1, keepdims=False)
        send = lax.dynamic_index_in_dim(pairs, 1 - bit, axis=1, keepdims=False)
        blocks = keep + exchanged(send, axis, mask)
    return blocks[0]


def gather_blocks(chunk, axis):
    index = lax.axis_index(axis)
    held = chunk[None]
    for mask in reversed(axis_bits(axis)):
        bit = (index // mask) % 2
        other = exchanged(held, axis, mask)
        low = jnp.where(bit == 0, held, other)
        high = jnp.where(bit == 0, other, held)
        held = jnp.stack([low, high], axis=1).reshape(held.shape[0] * 2, held.shape[1])
    return held


def summed_over(flat, axis):
    size = lax.axis_size(axis)
    part = scatter_blocks(flat.reshape(size, flat.shape[0] // size), axis)
    return gather_blocks(part, axis).reshape(flat.shape)


def plan_step(blocks, kind, axis, mask):
    bit = (lax.axis_index(axis) // mask) % 2
    if kind == "split":
        if blocks.shape[0] == 1:
            blocks = blocks.reshape(2, -1)
        pairs = blocks.reshape(blocks.shape[0] // 2, 2, blocks.shape[1])
        keep = lax.dynamic_index_in_dim(pairs, bit, axis=1, keepdims=False)
        send = lax.dynamic_index_in_dim(pairs, 1 - bit, axis=1, keepdims=False)
        return keep + exchanged(send, axis, mask)
    other = exchanged(blocks, axis, mask)
    low = jnp.where(bit == 0, blocks, other)
    high = jnp.where(bit == 0, other, blocks)
    return jnp.concatenate([low, high], axis=1)


def summed_by_exchange(flat, axes):
    size = 1
    for axis in axes:
        size *= lax.axis_size(axis)
    pieces = lax.all_to_all(flat.reshape(size, -1), axes, 0, 0, tiled=True)
    total = jnp.sum(pieces, axis=0, keepdims=True)
    spread = jnp.broadcast_to(total.astype(jnp.bfloat16), pieces.shape)
    gathered = lax.all_to_all(spread, axes, 0, 0, tiled=True)
    return gathered.astype(flat.dtype).reshape(flat.shape)


def silu_slope(scores):
    sigmoid = jax.nn.sigmoid(scores)
    return sigmoid * (1.0 + scores * (1.0 - sigmoid))


def expand_blocks(block_rows, block_size):
    return jnp.repeat(jnp.repeat(block_rows, block_size, axis=0), block_size, axis=1)


def shards(
    queries,
    keys,
    values,
    gates,
    out_grad,
    time_bucket,
    lengths,
    block_map,
    bucket_bias_matrix,
    w_out,
):
    query_rows = queries[0]
    key_rows = keys[0]
    value_rows = values[0]
    gate_rows = gates[0]
    grad_rows = out_grad[0]
    local_rows, width = query_rows.shape
    head_count = bucket_bias_matrix.shape[0]
    bucket_count = bucket_bias_matrix.shape[1]
    head_dim = width // head_count
    scale = head_dim ** (-0.5)
    blocks_here = local_rows // BLK
    cycle_index = lax.axis_index("ctx")
    row_start = cycle_index * local_rows
    offsets = jnp.cumsum(lengths[0], dtype=jnp.int32) - lengths[0]

    def segment_of(positions):
        return jnp.sum(
            (positions[:, None] >= offsets[None, 1:]).astype(jnp.int32), axis=1, dtype=jnp.int32
        )

    bucket_ids = jnp.arange(bucket_count, dtype=jnp.int32)
    query_pos = row_start + jnp.arange(local_rows, dtype=jnp.int32)
    query_seg = segment_of(query_pos)
    query_bucket = lax.dynamic_slice_in_dim(time_bucket[0], row_start, local_rows, 0)
    query_bucket_indicator = (query_bucket[:, None] == bucket_ids[None, :]).astype(jnp.bfloat16)
    bias_matrix_rows = jnp.einsum(
        "lf,sfq->slq",
        query_bucket_indicator,
        bucket_bias_matrix,
        preferred_element_type=jnp.float32,
    ).astype(jnp.bfloat16)
    map_rows = lax.dynamic_slice_in_dim(block_map[0], cycle_index * blocks_here, blocks_here, 0)
    query_heads = query_rows.reshape(local_rows, head_count, head_dim)
    stacked = jnp.stack([key_rows, value_rows])
    window = [stacked, passed_along(stacked, "ctx", 1), passed_along(stacked, "ctx", 2)]
    tiles = []
    attended = jnp.zeros((local_rows, head_count, head_dim), jnp.float32)
    for distance in range(3):
        key_first = row_start - distance * local_rows
        key_pos = key_first + jnp.arange(local_rows, dtype=jnp.int32)
        safe_first = jnp.maximum(key_first, 0)
        key_bucket = lax.dynamic_slice_in_dim(time_bucket[0], safe_first, local_rows, 0)
        key_bucket_indicator = (key_bucket[:, None] == bucket_ids[None, :]).astype(jnp.bfloat16)
        map_cols = lax.dynamic_slice_in_dim(map_rows, safe_first // BLK, blocks_here, 1)
        same_block = query_pos[:, None] // BLK == key_pos[None, :] // BLK
        key_visible = (
            (query_seg[:, None] == segment_of(key_pos)[None, :])
            & (key_pos[None, :] <= query_pos[:, None])
            & (key_pos[None, :] >= 0)
            & ((expand_blocks(map_cols, BLK) == 1) | same_block)
        )
        key_bias_terms = jnp.einsum(
            "vqx,px->vqp",
            bias_matrix_rows,
            key_bucket_indicator,
            preferred_element_type=jnp.float32,
        )
        visible, bias_terms, key_bucket_indicator = (
            key_visible,
            key_bias_terms,
            key_bucket_indicator,
        )
        forward_pair = window[distance]
        forward_key_heads = forward_pair[0].reshape(local_rows, head_count, head_dim)
        forward_value_heads = forward_pair[1].reshape(local_rows, head_count, head_dim)
        forward_scores = (
            jnp.einsum(
                "ihd,jhd->hij", query_heads, forward_key_heads, preferred_element_type=jnp.float32
            )
            * scale
            + bias_terms
        )
        forward_weights = jnp.where(visible[None], jax.nn.silu(forward_scores), 0.0).astype(
            jnp.bfloat16
        )
        attended_part = jnp.einsum(
            "hij,jhd->ihd", forward_weights, forward_value_heads, preferred_element_type=jnp.float32
        )
        attended = attended + attended_part
        tiles.append((visible, forward_scores, forward_weights, key_bucket_indicator))
    attended = attended.reshape(local_rows, width)
    centered = attended - jnp.mean(attended, axis=1, keepdims=True)
    inverse = lax.rsqrt(jnp.mean(centered * centered, axis=1, keepdims=True) + NORM_EPSILON)
    normed = centered * inverse
    dz_rows = lax.dot_general(
        grad_rows, w_out, (((1,), (1,)), ((), ())), preferred_element_type=jnp.float32
    )
    gate_float = gate_rows.astype(jnp.float32)
    gate_grad = (dz_rows * normed).astype(jnp.bfloat16)
    mixed = (normed * gate_float).astype(jnp.bfloat16)
    lifted = dz_rows * gate_float
    attended_grad = (
        (
            lifted
            - jnp.mean(lifted, axis=1, keepdims=True)
            - normed * jnp.mean(lifted * normed, axis=1, keepdims=True)
        )
        * inverse
    ).astype(jnp.bfloat16)
    grad_heads = attended_grad.reshape(local_rows, head_count, head_dim)
    indicator_float = query_bucket_indicator.astype(jnp.float32)
    dp_size = lax.axis_size("dp")
    weight_term = lax.dot_general(
        mixed, grad_rows, (((0,), (0,)), ((), ())), preferred_element_type=jnp.float32
    )
    weight_plan = [("split", "dp", mask) for mask in axis_bits("dp")]
    weight_plan.append(("skip", "ctx", 0))
    weight_plan.append(("exchange", "ctx", 0))
    weight_state = [weight_term.reshape(dp_size, -1), 0]

    def slot(anchor):
        blocks, done = weight_state
        if done < len(weight_plan):
            kind, axis, mask = weight_plan[done]
            if kind != "skip":
                blocks, anchor = lax.optimization_barrier((blocks, anchor))
            if kind == "skip":
                weight_state[0] = blocks
            elif kind == "exchange":
                weight_state[0] = summed_by_exchange(blocks.reshape(-1), (axis,))
            else:
                weight_state[0] = plan_step(blocks, kind, axis, mask)
            weight_state[1] = done + 1
        return anchor

    query_sum = jnp.zeros((local_rows, width), jnp.float32)
    share_sum = None
    key_terms = [None, None, None]
    sent = [None, None, None]
    for distance in (2, 1, 0):
        visible, scores, weights, key_bucket_indicator = tiles[distance]
        pair = slot(window[distance])
        if distance == 0:
            sent[2], pair = lax.optimization_barrier((sent[2], pair))
        key_heads = pair[0].reshape(local_rows, head_count, head_dim)
        value_heads = pair[1].reshape(local_rows, head_count, head_dim)
        weight_grad = jnp.einsum(
            "ihd,jhd->hij", grad_heads, value_heads, preferred_element_type=jnp.float32
        )
        value_part = jnp.einsum(
            "hij,ihd->jhd", weights, grad_heads, preferred_element_type=jnp.float32
        ).reshape(local_rows, width)
        score_gradient = jnp.where(visible[None], weight_grad * silu_slope(scores), 0.0).astype(
            jnp.bfloat16
        )
        score_gradient = slot(score_gradient)
        query_part = jnp.einsum(
            "hij,jhd->ihd", score_gradient, key_heads, preferred_element_type=jnp.float32
        ).reshape(local_rows, width)
        key_part = (
            jnp.einsum(
                "hij,ihd->jhd", score_gradient, query_heads, preferred_element_type=jnp.float32
            ).reshape(local_rows, width)
            * scale
        )
        bucket_share_piece = jnp.einsum(
            "rmw,wx->rmx", score_gradient, key_bucket_indicator, preferred_element_type=jnp.float32
        )
        share_sum = bucket_share_piece if share_sum is None else share_sum + bucket_share_piece
        query_sum = query_sum + query_part
        key_terms[distance] = jnp.stack([key_part, value_part])
        if distance > 0:
            sent[distance] = passed_along(
                key_terms[distance].astype(jnp.bfloat16), "ctx", -distance
            )
    table_local = jnp.einsum(
        "qp,cqk->cpk", indicator_float, share_sum, precision=lax.Precision.HIGHEST
    )
    gathered = key_terms[0] + sent[1].astype(jnp.float32) + sent[2].astype(jnp.float32)
    query_grad = (query_sum * scale).astype(jnp.bfloat16)
    key_grad = gathered[0].astype(jnp.bfloat16)
    value_grad = gathered[1].astype(jnp.bfloat16)
    projection_grad = weight_state[0].reshape(width // dp_size, width)
    table_grad = summed_by_exchange(table_local.reshape(-1), ("ctx", "dp")).reshape(
        table_local.shape
    )
    return (
        query_grad[None],
        key_grad[None],
        value_grad[None],
        gate_grad[None],
        projection_grad,
        table_grad,
    )


def solution(mesh):
    return jax.shard_map(
        shards,
        mesh=mesh,
        in_specs=(
            P("dp", "ctx", None),
            P("dp", "ctx", None),
            P("dp", "ctx", None),
            P("dp", "ctx", None),
            P("dp", "ctx", None),
            P("dp", None),
            P("dp", None),
            P("dp", None, None),
            P(),
            P(),
        ),
        out_specs=(
            P("dp", "ctx", None),
            P("dp", "ctx", None),
            P("dp", "ctx", None),
            P("dp", "ctx", None),
            P("dp", None),
            P(),
        ),
        check_vma=False,
    )
```

```python
import jax
import jax.numpy as jnp
from jax import lax
from jax.sharding import PartitionSpec as P

BLK = 128


NORM_EPSILON = 1e-05


def passed_along(value, axis, by):
    length = lax.axis_size(axis)
    pairs = [(i, i + by) for i in range(length) if 0 <= i + by < length]
    return lax.ppermute(value, axis, pairs)


def exchanged(value, axis, mask):
    length = lax.axis_size(axis)
    pairs = [(i, i ^ mask) for i in range(length)]
    return lax.ppermute(value, axis, pairs)


def axis_bits(axis):
    length = lax.axis_size(axis)
    bits = []
    mask = 1
    while mask < length:
        bits.append(mask)
        mask *= 2
    return bits


def scatter_blocks(blocks, axis):
    index = lax.axis_index(axis)
    for mask in axis_bits(axis):
        bit = (index // mask) % 2
        pairs = blocks.reshape(blocks.shape[0] // 2, 2, blocks.shape[1])
        keep = lax.dynamic_index_in_dim(pairs, bit, axis=1, keepdims=False)
        send = lax.dynamic_index_in_dim(pairs, 1 - bit, axis=1, keepdims=False)
        blocks = keep + exchanged(send, axis, mask)
    return blocks[0]


def gather_blocks(chunk, axis):
    index = lax.axis_index(axis)
    held = chunk[None]
    for mask in reversed(axis_bits(axis)):
        bit = (index // mask) % 2
        other = exchanged(held, axis, mask)
        low = jnp.where(bit == 0, held, other)
        high = jnp.where(bit == 0, other, held)
        held = jnp.stack([low, high], axis=1).reshape(held.shape[0] * 2, held.shape[1])
    return held


def summed_over(flat, axis):
    size = lax.axis_size(axis)
    part = scatter_blocks(flat.reshape(size, flat.shape[0] // size), axis)
    return gather_blocks(part, axis).reshape(flat.shape)


def plan_step(blocks, kind, axis, mask):
    bit = (lax.axis_index(axis) // mask) % 2
    if kind == "split":
        if blocks.shape[0] == 1:
            blocks = blocks.reshape(2, -1)
        pairs = blocks.reshape(blocks.shape[0] // 2, 2, blocks.shape[1])
        keep = lax.dynamic_index_in_dim(pairs, bit, axis=1, keepdims=False)
        send = lax.dynamic_index_in_dim(pairs, 1 - bit, axis=1, keepdims=False)
        return keep + exchanged(send, axis, mask)
    other = exchanged(blocks, axis, mask)
    low = jnp.where(bit == 0, blocks, other)
    high = jnp.where(bit == 0, other, blocks)
    return jnp.concatenate([low, high], axis=1)


def summed_by_exchange(flat, axes):
    size = 1
    for axis in axes:
        size *= lax.axis_size(axis)
    pieces = lax.all_to_all(flat.reshape(size, -1), axes, 0, 0, tiled=True)
    total = jnp.sum(pieces, axis=0, keepdims=True)
    spread = jnp.broadcast_to(total.astype(jnp.bfloat16), pieces.shape)
    gathered = lax.all_to_all(spread, axes, 0, 0, tiled=True)
    return gathered.astype(flat.dtype).reshape(flat.shape)


def silu_slope(scores):
    sigmoid = jax.nn.sigmoid(scores)
    return sigmoid * (1.0 + scores * (1.0 - sigmoid))


def expand_blocks(block_rows, block_size):
    return jnp.repeat(jnp.repeat(block_rows, block_size, axis=0), block_size, axis=1)


def shards(
    queries,
    keys,
    values,
    gates,
    out_grad,
    time_bucket,
    lengths,
    block_map,
    bucket_bias_matrix,
    w_out,
):
    query_rows = queries[0]
    key_rows = keys[0]
    value_rows = values[0]
    gate_rows = gates[0]
    grad_rows = out_grad[0]
    local_rows, width = query_rows.shape
    head_count = bucket_bias_matrix.shape[0]
    bucket_count = bucket_bias_matrix.shape[1]
    head_dim = width // head_count
    scale = head_dim ** (-0.5)
    blocks_here = local_rows // BLK
    cycle_index = lax.axis_index("ctx")
    row_start = cycle_index * local_rows
    offsets = jnp.cumsum(lengths[0], dtype=jnp.int32) - lengths[0]

    def segment_of(positions):
        return jnp.sum(
            (positions[:, None] >= offsets[None, 1:]).astype(jnp.int32), axis=1, dtype=jnp.int32
        )

    bucket_ids = jnp.arange(bucket_count, dtype=jnp.int32)
    query_pos = row_start + jnp.arange(local_rows, dtype=jnp.int32)
    query_seg = segment_of(query_pos)
    query_bucket = lax.dynamic_slice_in_dim(time_bucket[0], row_start, local_rows, 0)
    query_bucket_indicator = (query_bucket[:, None] == bucket_ids[None, :]).astype(jnp.bfloat16)
    bias_matrix_rows = jnp.einsum(
        "lf,sfq->slq",
        query_bucket_indicator,
        bucket_bias_matrix,
        preferred_element_type=jnp.float32,
    ).astype(jnp.bfloat16)
    map_rows = lax.dynamic_slice_in_dim(block_map[0], cycle_index * blocks_here, blocks_here, 0)
    query_heads = query_rows.reshape(local_rows, head_count, head_dim)
    stacked = jnp.stack([key_rows, value_rows])
    window = [stacked, passed_along(stacked, "ctx", 1), passed_along(stacked, "ctx", 2)]
    tiles = []
    attended = jnp.zeros((local_rows, head_count, head_dim), jnp.float32)
    for distance in range(3):
        key_first = row_start - distance * local_rows
        key_pos = key_first + jnp.arange(local_rows, dtype=jnp.int32)
        safe_first = jnp.maximum(key_first, 0)
        key_bucket = lax.dynamic_slice_in_dim(time_bucket[0], safe_first, local_rows, 0)
        key_bucket_indicator = (key_bucket[:, None] == bucket_ids[None, :]).astype(jnp.bfloat16)
        map_cols = lax.dynamic_slice_in_dim(map_rows, safe_first // BLK, blocks_here, 1)
        same_block = query_pos[:, None] // BLK == key_pos[None, :] // BLK
        key_visible = (
            (query_seg[:, None] == segment_of(key_pos)[None, :])
            & (key_pos[None, :] <= query_pos[:, None])
            & (key_pos[None, :] >= 0)
            & ((expand_blocks(map_cols, BLK) == 1) | same_block)
        )
        key_bias_terms = jnp.einsum(
            "vqx,px->vqp",
            bias_matrix_rows,
            key_bucket_indicator,
            preferred_element_type=jnp.float32,
        )
        visible, bias_terms, key_bucket_indicator = (
            key_visible,
            key_bias_terms,
            key_bucket_indicator,
        )
        forward_pair = window[distance]
        forward_key_heads = forward_pair[0].reshape(local_rows, head_count, head_dim)
        forward_value_heads = forward_pair[1].reshape(local_rows, head_count, head_dim)
        forward_scores = (
            jnp.einsum(
                "ihd,jhd->hij", query_heads, forward_key_heads, preferred_element_type=jnp.float32
            )
            * scale
            + bias_terms
        )
        forward_weights = jnp.where(visible[None], jax.nn.silu(forward_scores), 0.0).astype(
            jnp.bfloat16
        )
        attended_part = jnp.einsum(
            "hij,jhd->ihd", forward_weights, forward_value_heads, preferred_element_type=jnp.float32
        )
        attended = attended + attended_part
        tiles.append((visible, forward_scores, forward_weights, key_bucket_indicator))
    attended = attended.reshape(local_rows, width)
    centered = attended - jnp.mean(attended, axis=1, keepdims=True)
    inverse = lax.rsqrt(jnp.mean(centered * centered, axis=1, keepdims=True) + NORM_EPSILON)
    normed = centered * inverse
    dz_rows = lax.dot_general(
        grad_rows, w_out, (((1,), (1,)), ((), ())), preferred_element_type=jnp.float32
    )
    gate_float = gate_rows.astype(jnp.float32)
    gate_grad = (dz_rows * normed).astype(jnp.bfloat16)
    mixed = (normed * gate_float).astype(jnp.bfloat16)
    lifted = dz_rows * gate_float
    attended_grad = (
        (
            lifted
            - jnp.mean(lifted, axis=1, keepdims=True)
            - normed * jnp.mean(lifted * normed, axis=1, keepdims=True)
        )
        * inverse
    ).astype(jnp.bfloat16)
    grad_heads = attended_grad.reshape(local_rows, head_count, head_dim)
    indicator_float = query_bucket_indicator.astype(jnp.float32)
    dp_size = lax.axis_size("dp")
    weight_term = lax.dot_general(
        mixed, grad_rows, (((0,), (0,)), ((), ())), preferred_element_type=jnp.float32
    )
    weight_plan = [("split", "dp", mask) for mask in axis_bits("dp")]
    weight_plan.append(("exchange", "ctx", 0))
    weight_plan += [("skip", "ctx", 0), ("tie", "ctx", 0)]
    weight_state = [weight_term.reshape(dp_size, -1), 0]

    def slot(anchor):
        blocks, done = weight_state
        if done < len(weight_plan):
            kind, axis, mask = weight_plan[done]
            if kind != "skip":
                blocks, anchor = lax.optimization_barrier((blocks, anchor))
            if kind in ("skip", "tie"):
                weight_state[0] = blocks
            elif kind == "exchange":
                weight_state[0] = summed_by_exchange(blocks.reshape(-1), (axis,))
            else:
                weight_state[0] = plan_step(blocks, kind, axis, mask)
            weight_state[1] = done + 1
        return anchor

    query_sum = jnp.zeros((local_rows, width), jnp.float32)
    share_sum = None
    key_terms = [None, None, None]
    sent = [None, None, None]
    for distance in (2, 1, 0):
        visible, scores, weights, key_bucket_indicator = tiles[distance]
        pair = slot(window[distance])
        if distance == 0:
            sent[2], pair = lax.optimization_barrier((sent[2], pair))
        key_heads = pair[0].reshape(local_rows, head_count, head_dim)
        value_heads = pair[1].reshape(local_rows, head_count, head_dim)
        weight_grad = jnp.einsum(
            "ihd,jhd->hij", grad_heads, value_heads, preferred_element_type=jnp.float32
        )
        value_part = jnp.einsum(
            "hij,ihd->jhd", weights, grad_heads, preferred_element_type=jnp.float32
        ).reshape(local_rows, width)
        score_gradient = jnp.where(visible[None], weight_grad * silu_slope(scores), 0.0).astype(
            jnp.bfloat16
        )
        score_gradient = slot(score_gradient)
        query_part = jnp.einsum(
            "hij,jhd->ihd", score_gradient, key_heads, preferred_element_type=jnp.float32
        ).reshape(local_rows, width)
        key_part = (
            jnp.einsum(
                "hij,ihd->jhd", score_gradient, query_heads, preferred_element_type=jnp.float32
            ).reshape(local_rows, width)
            * scale
        )
        bucket_share_piece = jnp.einsum(
            "rmw,wx->rmx", score_gradient, key_bucket_indicator, preferred_element_type=jnp.float32
        )
        share_sum = bucket_share_piece if share_sum is None else share_sum + bucket_share_piece
        query_sum = query_sum + query_part
        key_terms[distance] = jnp.stack([key_part, value_part])
        if distance > 0:
            sent[distance] = passed_along(
                key_terms[distance].astype(jnp.bfloat16), "ctx", -distance
            )
    table_local = jnp.einsum(
        "qp,cqk->cpk", indicator_float, share_sum, precision=lax.Precision.HIGHEST
    )
    gathered = key_terms[0] + sent[1].astype(jnp.float32) + sent[2].astype(jnp.float32)
    query_grad = (query_sum * scale).astype(jnp.bfloat16)
    key_grad = gathered[0].astype(jnp.bfloat16)
    value_grad = gathered[1].astype(jnp.bfloat16)
    projection_grad = weight_state[0].reshape(width // dp_size, width)
    table_grad = summed_by_exchange(table_local.reshape(-1), ("ctx", "dp")).reshape(
        table_local.shape
    )
    return (
        query_grad[None],
        key_grad[None],
        value_grad[None],
        gate_grad[None],
        projection_grad,
        table_grad,
    )


def solution(mesh):
    return jax.shard_map(
        shards,
        mesh=mesh,
        in_specs=(
            P("dp", "ctx", None),
            P("dp", "ctx", None),
            P("dp", "ctx", None),
            P("dp", "ctx", None),
            P("dp", "ctx", None),
            P("dp", None),
            P("dp", None),
            P("dp", None, None),
            P(),
            P(),
        ),
        out_specs=(
            P("dp", "ctx", None),
            P("dp", "ctx", None),
            P("dp", "ctx", None),
            P("dp", "ctx", None),
            P("dp", None),
            P(),
        ),
        check_vma=False,
    )
```

```python
import jax
import jax.numpy as jnp
from jax import lax
from jax.sharding import PartitionSpec as P

BLK = 128


NORM_EPSILON = 1e-05


def passed_along(value, axis, by):
    length = lax.axis_size(axis)
    pairs = [(i, i + by) for i in range(length) if 0 <= i + by < length]
    return lax.ppermute(value, axis, pairs)


def exchanged(value, axis, mask):
    length = lax.axis_size(axis)
    pairs = [(i, i ^ mask) for i in range(length)]
    return lax.ppermute(value, axis, pairs)


def axis_bits(axis):
    length = lax.axis_size(axis)
    bits = []
    mask = 1
    while mask < length:
        bits.append(mask)
        mask *= 2
    return bits


def scatter_blocks(blocks, axis):
    index = lax.axis_index(axis)
    for mask in axis_bits(axis):
        bit = (index // mask) % 2
        pairs = blocks.reshape(blocks.shape[0] // 2, 2, blocks.shape[1])
        keep = lax.dynamic_index_in_dim(pairs, bit, axis=1, keepdims=False)
        send = lax.dynamic_index_in_dim(pairs, 1 - bit, axis=1, keepdims=False)
        blocks = keep + exchanged(send, axis, mask)
    return blocks[0]


def gather_blocks(chunk, axis):
    index = lax.axis_index(axis)
    held = chunk[None]
    for mask in reversed(axis_bits(axis)):
        bit = (index // mask) % 2
        other = exchanged(held, axis, mask)
        low = jnp.where(bit == 0, held, other)
        high = jnp.where(bit == 0, other, held)
        held = jnp.stack([low, high], axis=1).reshape(held.shape[0] * 2, held.shape[1])
    return held


def summed_over(flat, axis):
    size = lax.axis_size(axis)
    part = scatter_blocks(flat.reshape(size, flat.shape[0] // size), axis)
    return gather_blocks(part, axis).reshape(flat.shape)


def plan_step(blocks, kind, axis, mask):
    bit = (lax.axis_index(axis) // mask) % 2
    if kind == "split":
        if blocks.shape[0] == 1:
            blocks = blocks.reshape(2, -1)
        pairs = blocks.reshape(blocks.shape[0] // 2, 2, blocks.shape[1])
        keep = lax.dynamic_index_in_dim(pairs, bit, axis=1, keepdims=False)
        send = lax.dynamic_index_in_dim(pairs, 1 - bit, axis=1, keepdims=False)
        return keep + exchanged(send, axis, mask)
    other = exchanged(blocks, axis, mask)
    low = jnp.where(bit == 0, blocks, other)
    high = jnp.where(bit == 0, other, blocks)
    return jnp.concatenate([low, high], axis=1)


def collected_by_exchange(chunk, axis):
    size = lax.axis_size(axis)
    depth = len(axis_bits(axis))
    spread = jnp.broadcast_to(chunk.astype(jnp.bfloat16)[None], (size, chunk.shape[0]))
    gathered = lax.all_to_all(spread, axis, 0, 0, tiled=True)
    gathered = gathered.reshape([2] * depth + [chunk.shape[0]])
    gathered = gathered.transpose(list(reversed(range(depth))) + [depth])
    return gathered.reshape(-1).astype(chunk.dtype)


def summed_by_exchange(flat, axes):
    size = 1
    for axis in axes:
        size *= lax.axis_size(axis)
    pieces = lax.all_to_all(flat.reshape(size, -1), axes, 0, 0, tiled=True)
    total = jnp.sum(pieces, axis=0, keepdims=True)
    spread = jnp.broadcast_to(total.astype(jnp.bfloat16), pieces.shape)
    gathered = lax.all_to_all(spread, axes, 0, 0, tiled=True)
    return gathered.astype(flat.dtype).reshape(flat.shape)


def silu_slope(scores):
    sigmoid = jax.nn.sigmoid(scores)
    return sigmoid * (1.0 + scores * (1.0 - sigmoid))


def expand_blocks(block_rows, block_size):
    return jnp.repeat(jnp.repeat(block_rows, block_size, axis=0), block_size, axis=1)


def shards(
    queries,
    keys,
    values,
    gates,
    out_grad,
    time_bucket,
    lengths,
    block_map,
    bucket_bias_matrix,
    w_out,
):
    query_rows = queries[0]
    key_rows = keys[0]
    value_rows = values[0]
    gate_rows = gates[0]
    grad_rows = out_grad[0]
    local_rows, width = query_rows.shape
    head_count = bucket_bias_matrix.shape[0]
    bucket_count = bucket_bias_matrix.shape[1]
    head_dim = width // head_count
    scale = head_dim ** (-0.5)
    blocks_here = local_rows // BLK
    cycle_index = lax.axis_index("ctx")
    row_start = cycle_index * local_rows
    offsets = jnp.cumsum(lengths[0], dtype=jnp.int32) - lengths[0]

    def segment_of(positions):
        return jnp.sum(
            (positions[:, None] >= offsets[None, 1:]).astype(jnp.int32), axis=1, dtype=jnp.int32
        )

    bucket_ids = jnp.arange(bucket_count, dtype=jnp.int32)
    query_pos = row_start + jnp.arange(local_rows, dtype=jnp.int32)
    query_seg = segment_of(query_pos)
    query_bucket = lax.dynamic_slice_in_dim(time_bucket[0], row_start, local_rows, 0)
    query_bucket_indicator = (query_bucket[:, None] == bucket_ids[None, :]).astype(jnp.bfloat16)
    bias_matrix_rows = jnp.einsum(
        "lf,sfq->slq",
        query_bucket_indicator,
        bucket_bias_matrix,
        preferred_element_type=jnp.float32,
    ).astype(jnp.bfloat16)
    map_rows = lax.dynamic_slice_in_dim(block_map[0], cycle_index * blocks_here, blocks_here, 0)
    query_heads = query_rows.reshape(local_rows, head_count, head_dim)
    stacked = jnp.stack([key_rows, value_rows])
    window = [stacked, passed_along(stacked, "ctx", 1), passed_along(stacked, "ctx", 2)]
    tiles = []
    attended = jnp.zeros((local_rows, head_count, head_dim), jnp.float32)
    for distance in range(3):
        key_first = row_start - distance * local_rows
        key_pos = key_first + jnp.arange(local_rows, dtype=jnp.int32)
        safe_first = jnp.maximum(key_first, 0)
        key_bucket = lax.dynamic_slice_in_dim(time_bucket[0], safe_first, local_rows, 0)
        key_bucket_indicator = (key_bucket[:, None] == bucket_ids[None, :]).astype(jnp.bfloat16)
        map_cols = lax.dynamic_slice_in_dim(map_rows, safe_first // BLK, blocks_here, 1)
        same_block = query_pos[:, None] // BLK == key_pos[None, :] // BLK
        key_visible = (
            (query_seg[:, None] == segment_of(key_pos)[None, :])
            & (key_pos[None, :] <= query_pos[:, None])
            & (key_pos[None, :] >= 0)
            & ((expand_blocks(map_cols, BLK) == 1) | same_block)
        )
        key_bias_terms = jnp.einsum(
            "vqx,px->vqp",
            bias_matrix_rows,
            key_bucket_indicator,
            preferred_element_type=jnp.float32,
        )
        visible, bias_terms, key_bucket_indicator = (
            key_visible,
            key_bias_terms,
            key_bucket_indicator,
        )
        forward_pair = window[distance]
        forward_key_heads = forward_pair[0].reshape(local_rows, head_count, head_dim)
        forward_value_heads = forward_pair[1].reshape(local_rows, head_count, head_dim)
        forward_scores = (
            jnp.einsum(
                "ihd,jhd->hij", query_heads, forward_key_heads, preferred_element_type=jnp.float32
            )
            * scale
            + bias_terms
        )
        forward_weights = jnp.where(visible[None], jax.nn.silu(forward_scores), 0.0).astype(
            jnp.bfloat16
        )
        attended_part = jnp.einsum(
            "hij,jhd->ihd", forward_weights, forward_value_heads, preferred_element_type=jnp.float32
        )
        attended = attended + attended_part
        tiles.append((visible, forward_scores, forward_weights, key_bucket_indicator))
    attended = attended.reshape(local_rows, width)
    centered = attended - jnp.mean(attended, axis=1, keepdims=True)
    inverse = lax.rsqrt(jnp.mean(centered * centered, axis=1, keepdims=True) + NORM_EPSILON)
    normed = centered * inverse
    dz_rows = lax.dot_general(
        grad_rows, w_out, (((1,), (1,)), ((), ())), preferred_element_type=jnp.float32
    )
    gate_float = gate_rows.astype(jnp.float32)
    gate_grad = (dz_rows * normed).astype(jnp.bfloat16)
    mixed = (normed * gate_float).astype(jnp.bfloat16)
    lifted = dz_rows * gate_float
    attended_grad = (
        (
            lifted
            - jnp.mean(lifted, axis=1, keepdims=True)
            - normed * jnp.mean(lifted * normed, axis=1, keepdims=True)
        )
        * inverse
    ).astype(jnp.bfloat16)
    grad_heads = attended_grad.reshape(local_rows, head_count, head_dim)
    indicator_float = query_bucket_indicator.astype(jnp.float32)
    dp_size = lax.axis_size("dp")
    weight_term = lax.dot_general(
        mixed, grad_rows, (((0,), (0,)), ((), ())), preferred_element_type=jnp.float32
    )
    weight_plan = [("split", "dp", mask) for mask in axis_bits("dp")]
    weight_plan += [("split", "ctx", mask) for mask in axis_bits("ctx")]
    weight_plan.append(("collect", "ctx", 0))
    weight_state = [weight_term.reshape(dp_size, -1), 0]

    def slot(anchor, tied=True):
        blocks, done = weight_state
        if done < len(weight_plan):
            if tied:
                blocks, anchor = lax.optimization_barrier((blocks, anchor))
            kind, axis, mask = weight_plan[done]
            if kind == "collect":
                weight_state[0] = collected_by_exchange(blocks.reshape(-1), axis)
            elif kind == "exchange":
                weight_state[0] = summed_by_exchange(blocks.reshape(-1), (axis,))
            else:
                weight_state[0] = plan_step(blocks, kind, axis, mask)
            weight_state[1] = done + 1
        return anchor

    query_sum = jnp.zeros((local_rows, width), jnp.float32)
    share_sum = None
    key_terms = [None, None, None]
    sent = [None, None, None]
    for distance in (2, 1, 0):
        visible, scores, weights, key_bucket_indicator = tiles[distance]
        pair = slot(window[distance])
        if distance == 0:
            sent[2], pair = lax.optimization_barrier((sent[2], pair))
        key_heads = pair[0].reshape(local_rows, head_count, head_dim)
        value_heads = pair[1].reshape(local_rows, head_count, head_dim)
        weight_grad = jnp.einsum(
            "ihd,jhd->hij", grad_heads, value_heads, preferred_element_type=jnp.float32
        )
        value_part = jnp.einsum(
            "hij,ihd->jhd", weights, grad_heads, preferred_element_type=jnp.float32
        ).reshape(local_rows, width)
        score_gradient = jnp.where(visible[None], weight_grad * silu_slope(scores), 0.0).astype(
            jnp.bfloat16
        )
        score_gradient = slot(score_gradient)
        query_part = jnp.einsum(
            "hij,jhd->ihd", score_gradient, key_heads, preferred_element_type=jnp.float32
        ).reshape(local_rows, width)
        key_part = (
            jnp.einsum(
                "hij,ihd->jhd", score_gradient, query_heads, preferred_element_type=jnp.float32
            ).reshape(local_rows, width)
            * scale
        )
        bucket_share_piece = jnp.einsum(
            "rmw,wx->rmx", score_gradient, key_bucket_indicator, preferred_element_type=jnp.float32
        )
        share_sum = bucket_share_piece if share_sum is None else share_sum + bucket_share_piece
        query_sum = query_sum + query_part
        key_terms[distance] = jnp.stack([key_part, value_part])
        if distance > 0:
            sent[distance] = passed_along(
                key_terms[distance].astype(jnp.bfloat16), "ctx", -distance
            )
    table_local = jnp.einsum(
        "qp,cqk->cpk", indicator_float, share_sum, precision=lax.Precision.HIGHEST
    )
    while weight_state[1] < len(weight_plan):
        slot(None, tied=False)
    gathered = key_terms[0] + sent[1].astype(jnp.float32) + sent[2].astype(jnp.float32)
    query_grad = (query_sum * scale).astype(jnp.bfloat16)
    key_grad = gathered[0].astype(jnp.bfloat16)
    value_grad = gathered[1].astype(jnp.bfloat16)
    projection_grad = weight_state[0].reshape(width // dp_size, width)
    table_grad = summed_by_exchange(table_local.reshape(-1), ("ctx", "dp")).reshape(
        table_local.shape
    )
    return (
        query_grad[None],
        key_grad[None],
        value_grad[None],
        gate_grad[None],
        projection_grad,
        table_grad,
    )


def solution(mesh):
    return jax.shard_map(
        shards,
        mesh=mesh,
        in_specs=(
            P("dp", "ctx", None),
            P("dp", "ctx", None),
            P("dp", "ctx", None),
            P("dp", "ctx", None),
            P("dp", "ctx", None),
            P("dp", None),
            P("dp", None),
            P("dp", None, None),
            P(),
            P(),
        ),
        out_specs=(
            P("dp", "ctx", None),
            P("dp", "ctx", None),
            P("dp", "ctx", None),
            P("dp", "ctx", None),
            P("dp", None),
            P(),
        ),
        check_vma=False,
    )
```

```python
import jax
import jax.numpy as jnp
from jax import lax
from jax.sharding import PartitionSpec as P

BLK = 128


NORM_EPSILON = 1e-05


def passed_along(value, axis, by):
    length = lax.axis_size(axis)
    pairs = [(i, i + by) for i in range(length) if 0 <= i + by < length]
    return lax.ppermute(value, axis, pairs)


def exchanged(value, axis, mask):
    length = lax.axis_size(axis)
    pairs = [(i, i ^ mask) for i in range(length)]
    return lax.ppermute(value, axis, pairs)


def axis_bits(axis):
    length = lax.axis_size(axis)
    bits = []
    mask = 1
    while mask < length:
        bits.append(mask)
        mask *= 2
    return bits


def scatter_blocks(blocks, axis):
    index = lax.axis_index(axis)
    for mask in axis_bits(axis):
        bit = (index // mask) % 2
        pairs = blocks.reshape(blocks.shape[0] // 2, 2, blocks.shape[1])
        keep = lax.dynamic_index_in_dim(pairs, bit, axis=1, keepdims=False)
        send = lax.dynamic_index_in_dim(pairs, 1 - bit, axis=1, keepdims=False)
        blocks = keep + exchanged(send, axis, mask)
    return blocks[0]


def gather_blocks(chunk, axis):
    index = lax.axis_index(axis)
    held = chunk[None]
    for mask in reversed(axis_bits(axis)):
        bit = (index // mask) % 2
        other = exchanged(held, axis, mask)
        low = jnp.where(bit == 0, held, other)
        high = jnp.where(bit == 0, other, held)
        held = jnp.stack([low, high], axis=1).reshape(held.shape[0] * 2, held.shape[1])
    return held


def summed_over(flat, axis):
    size = lax.axis_size(axis)
    part = scatter_blocks(flat.reshape(size, flat.shape[0] // size), axis)
    return gather_blocks(part, axis).reshape(flat.shape)


def plan_step(blocks, kind, axis, mask):
    bit = (lax.axis_index(axis) // mask) % 2
    if kind == "split":
        if blocks.shape[0] == 1:
            blocks = blocks.reshape(2, -1)
        pairs = blocks.reshape(blocks.shape[0] // 2, 2, blocks.shape[1])
        keep = lax.dynamic_index_in_dim(pairs, bit, axis=1, keepdims=False)
        send = lax.dynamic_index_in_dim(pairs, 1 - bit, axis=1, keepdims=False)
        return keep + exchanged(send, axis, mask)
    other = exchanged(blocks, axis, mask)
    low = jnp.where(bit == 0, blocks, other)
    high = jnp.where(bit == 0, other, blocks)
    return jnp.concatenate([low, high], axis=1)


def summed_by_exchange(flat, axes):
    size = 1
    for axis in axes:
        size *= lax.axis_size(axis)
    pieces = lax.all_to_all(flat.reshape(size, -1), axes, 0, 0, tiled=True)
    total = jnp.sum(pieces, axis=0, keepdims=True)
    spread = jnp.broadcast_to(total.astype(jnp.bfloat16), pieces.shape)
    gathered = lax.all_to_all(spread, axes, 0, 0, tiled=True)
    return gathered.astype(flat.dtype).reshape(flat.shape)


def silu_slope(scores):
    sigmoid = jax.nn.sigmoid(scores)
    return sigmoid * (1.0 + scores * (1.0 - sigmoid))


def expand_blocks(block_rows, block_size):
    return jnp.repeat(jnp.repeat(block_rows, block_size, axis=0), block_size, axis=1)


def shards(
    queries,
    keys,
    values,
    gates,
    out_grad,
    time_bucket,
    lengths,
    block_map,
    bucket_bias_matrix,
    w_out,
):
    query_rows = queries[0]
    key_rows = keys[0]
    value_rows = values[0]
    gate_rows = gates[0]
    grad_rows = out_grad[0]
    local_rows, width = query_rows.shape
    head_count = bucket_bias_matrix.shape[0]
    bucket_count = bucket_bias_matrix.shape[1]
    head_dim = width // head_count
    scale = head_dim ** (-0.5)
    blocks_here = local_rows // BLK
    cycle_index = lax.axis_index("ctx")
    row_start = cycle_index * local_rows
    offsets = jnp.cumsum(lengths[0], dtype=jnp.int32) - lengths[0]

    def segment_of(positions):
        return jnp.sum(
            (positions[:, None] >= offsets[None, 1:]).astype(jnp.int32), axis=1, dtype=jnp.int32
        )

    bucket_ids = jnp.arange(bucket_count, dtype=jnp.int32)
    query_pos = row_start + jnp.arange(local_rows, dtype=jnp.int32)
    query_seg = segment_of(query_pos)
    query_bucket = lax.dynamic_slice_in_dim(time_bucket[0], row_start, local_rows, 0)
    query_bucket_indicator = (query_bucket[:, None] == bucket_ids[None, :]).astype(jnp.bfloat16)
    bias_matrix_rows = jnp.einsum(
        "lf,sfq->slq",
        query_bucket_indicator,
        bucket_bias_matrix,
        preferred_element_type=jnp.float32,
    ).astype(jnp.bfloat16)
    map_rows = lax.dynamic_slice_in_dim(block_map[0], cycle_index * blocks_here, blocks_here, 0)
    query_heads = query_rows.reshape(local_rows, head_count, head_dim)
    stacked = jnp.stack([key_rows, value_rows])
    window = [stacked, passed_along(stacked, "ctx", 1), passed_along(stacked, "ctx", 2)]
    tiles = []
    attended = jnp.zeros((local_rows, head_count, head_dim), jnp.float32)
    for distance in range(3):
        key_first = row_start - distance * local_rows
        key_pos = key_first + jnp.arange(local_rows, dtype=jnp.int32)
        safe_first = jnp.maximum(key_first, 0)
        key_bucket = lax.dynamic_slice_in_dim(time_bucket[0], safe_first, local_rows, 0)
        key_bucket_indicator = (key_bucket[:, None] == bucket_ids[None, :]).astype(jnp.bfloat16)
        map_cols = lax.dynamic_slice_in_dim(map_rows, safe_first // BLK, blocks_here, 1)
        same_block = query_pos[:, None] // BLK == key_pos[None, :] // BLK
        key_visible = (
            (query_seg[:, None] == segment_of(key_pos)[None, :])
            & (key_pos[None, :] <= query_pos[:, None])
            & (key_pos[None, :] >= 0)
            & ((expand_blocks(map_cols, BLK) == 1) | same_block)
        )
        key_bias_terms = jnp.einsum(
            "vqx,px->vqp",
            bias_matrix_rows,
            key_bucket_indicator,
            preferred_element_type=jnp.float32,
        )
        visible, bias_terms, key_bucket_indicator = (
            key_visible,
            key_bias_terms,
            key_bucket_indicator,
        )
        forward_pair = window[distance]
        forward_key_heads = forward_pair[0].reshape(local_rows, head_count, head_dim)
        forward_value_heads = forward_pair[1].reshape(local_rows, head_count, head_dim)
        forward_scores = (
            jnp.einsum(
                "ihd,jhd->hij", query_heads, forward_key_heads, preferred_element_type=jnp.float32
            )
            * scale
            + bias_terms
        )
        forward_weights = jnp.where(visible[None], jax.nn.silu(forward_scores), 0.0).astype(
            jnp.bfloat16
        )
        attended_part = jnp.einsum(
            "hij,jhd->ihd", forward_weights, forward_value_heads, preferred_element_type=jnp.float32
        )
        attended = attended + attended_part
        tiles.append((visible, forward_scores, forward_weights, key_bucket_indicator))
    attended = attended.reshape(local_rows, width)
    centered = attended - jnp.mean(attended, axis=1, keepdims=True)
    inverse = lax.rsqrt(jnp.mean(centered * centered, axis=1, keepdims=True) + NORM_EPSILON)
    normed = centered * inverse
    dz_rows = lax.dot_general(
        grad_rows, w_out, (((1,), (1,)), ((), ())), preferred_element_type=jnp.float32
    )
    gate_float = gate_rows.astype(jnp.float32)
    gate_grad = (dz_rows * normed).astype(jnp.bfloat16)
    mixed = (normed * gate_float).astype(jnp.bfloat16)
    lifted = dz_rows * gate_float
    attended_grad = (
        (
            lifted
            - jnp.mean(lifted, axis=1, keepdims=True)
            - normed * jnp.mean(lifted * normed, axis=1, keepdims=True)
        )
        * inverse
    ).astype(jnp.bfloat16)
    grad_heads = attended_grad.reshape(local_rows, head_count, head_dim)
    indicator_float = query_bucket_indicator.astype(jnp.float32)
    dp_size = lax.axis_size("dp")
    weight_term = lax.dot_general(
        mixed, grad_rows, (((0,), (0,)), ((), ())), preferred_element_type=jnp.float32
    )
    weight_plan = [("split", "dp", mask) for mask in axis_bits("dp")]
    weight_plan.append(("exchange", "ctx", 0))
    weight_state = [weight_term.reshape(dp_size, -1), 0]

    def slot(anchor):
        blocks, done = weight_state
        if done < len(weight_plan):
            blocks, anchor = lax.optimization_barrier((blocks, anchor))
            kind, axis, mask = weight_plan[done]
            if kind == "exchange":
                weight_state[0] = summed_by_exchange(blocks.reshape(-1), (axis,))
            else:
                weight_state[0] = plan_step(blocks, kind, axis, mask)
            weight_state[1] = done + 1
        return anchor

    query_sum = jnp.zeros((local_rows, width), jnp.float32)
    share_sum = None
    key_terms = [None, None, None]
    sent = [None, None, None]
    for distance in (2, 1, 0):
        visible, scores, weights, key_bucket_indicator = tiles[distance]
        pair = slot(window[distance])
        if distance == 0:
            sent[2], pair = lax.optimization_barrier((sent[2], pair))
        key_heads = pair[0].reshape(local_rows, head_count, head_dim)
        value_heads = pair[1].reshape(local_rows, head_count, head_dim)
        weight_grad = jnp.einsum(
            "ihd,jhd->hij", grad_heads, value_heads, preferred_element_type=jnp.float32
        )
        value_part = jnp.einsum(
            "hij,ihd->jhd", weights, grad_heads, preferred_element_type=jnp.float32
        ).reshape(local_rows, width)
        score_gradient = jnp.where(visible[None], weight_grad * silu_slope(scores), 0.0).astype(
            jnp.bfloat16
        )
        score_gradient = slot(score_gradient)
        query_part = jnp.einsum(
            "hij,jhd->ihd", score_gradient, key_heads, preferred_element_type=jnp.float32
        ).reshape(local_rows, width)
        key_part = (
            jnp.einsum(
                "hij,ihd->jhd", score_gradient, query_heads, preferred_element_type=jnp.float32
            ).reshape(local_rows, width)
            * scale
        )
        bucket_share_piece = jnp.einsum(
            "rmw,wx->rmx", score_gradient, key_bucket_indicator, preferred_element_type=jnp.float32
        )
        share_sum = bucket_share_piece if share_sum is None else share_sum + bucket_share_piece
        query_sum = query_sum + query_part
        key_terms[distance] = jnp.stack([key_part, value_part])
        if distance > 0:
            sent[distance] = passed_along(
                key_terms[distance].astype(jnp.bfloat16), "ctx", -distance
            )
    indicator_heads = jnp.broadcast_to(indicator_float[None], (head_count,) + indicator_float.shape)
    table_local = jnp.einsum(
        "cqp,cqk->cpk", indicator_heads, share_sum, precision=lax.Precision.HIGHEST
    )
    gathered = key_terms[0] + sent[1].astype(jnp.float32) + sent[2].astype(jnp.float32)
    query_grad = (query_sum * scale).astype(jnp.bfloat16)
    key_grad = gathered[0].astype(jnp.bfloat16)
    value_grad = gathered[1].astype(jnp.bfloat16)
    projection_grad = weight_state[0].reshape(width // dp_size, width)
    table_grad = summed_by_exchange(table_local.reshape(-1), ("ctx", "dp")).reshape(
        table_local.shape
    )
    return (
        query_grad[None],
        key_grad[None],
        value_grad[None],
        gate_grad[None],
        projection_grad,
        table_grad,
    )


def solution(mesh):
    return jax.shard_map(
        shards,
        mesh=mesh,
        in_specs=(
            P("dp", "ctx", None),
            P("dp", "ctx", None),
            P("dp", "ctx", None),
            P("dp", "ctx", None),
            P("dp", "ctx", None),
            P("dp", None),
            P("dp", None),
            P("dp", None, None),
            P(),
            P(),
        ),
        out_specs=(
            P("dp", "ctx", None),
            P("dp", "ctx", None),
            P("dp", "ctx", None),
            P("dp", "ctx", None),
            P("dp", None),
            P(),
        ),
        check_vma=False,
    )
```

```python
import jax
import jax.numpy as jnp
from jax import lax
from jax.sharding import PartitionSpec as P

BLK = 128


NORM_EPSILON = 1e-05


def passed_along(value, axis, by):
    length = lax.axis_size(axis)
    pairs = [(i, i + by) for i in range(length) if 0 <= i + by < length]
    return lax.ppermute(value, axis, pairs)


def exchanged(value, axis, mask):
    length = lax.axis_size(axis)
    pairs = [(i, i ^ mask) for i in range(length)]
    return lax.ppermute(value, axis, pairs)


def axis_bits(axis):
    length = lax.axis_size(axis)
    bits = []
    mask = 1
    while mask < length:
        bits.append(mask)
        mask *= 2
    return bits


def scatter_blocks(blocks, axis):
    index = lax.axis_index(axis)
    for mask in axis_bits(axis):
        bit = (index // mask) % 2
        pairs = blocks.reshape(blocks.shape[0] // 2, 2, blocks.shape[1])
        keep = lax.dynamic_index_in_dim(pairs, bit, axis=1, keepdims=False)
        send = lax.dynamic_index_in_dim(pairs, 1 - bit, axis=1, keepdims=False)
        blocks = keep + exchanged(send, axis, mask)
    return blocks[0]


def gather_blocks(chunk, axis):
    index = lax.axis_index(axis)
    held = chunk[None]
    for mask in reversed(axis_bits(axis)):
        bit = (index // mask) % 2
        other = exchanged(held, axis, mask)
        low = jnp.where(bit == 0, held, other)
        high = jnp.where(bit == 0, other, held)
        held = jnp.stack([low, high], axis=1).reshape(held.shape[0] * 2, held.shape[1])
    return held


def summed_over(flat, axis):
    size = lax.axis_size(axis)
    part = scatter_blocks(flat.reshape(size, flat.shape[0] // size), axis)
    return gather_blocks(part, axis).reshape(flat.shape)


def plan_step(blocks, kind, axis, mask):
    bit = (lax.axis_index(axis) // mask) % 2
    if kind == "split":
        if blocks.shape[0] == 1:
            blocks = blocks.reshape(2, -1)
        pairs = blocks.reshape(blocks.shape[0] // 2, 2, blocks.shape[1])
        keep = lax.dynamic_index_in_dim(pairs, bit, axis=1, keepdims=False)
        send = lax.dynamic_index_in_dim(pairs, 1 - bit, axis=1, keepdims=False)
        return keep + exchanged(send, axis, mask)
    other = exchanged(blocks, axis, mask)
    low = jnp.where(bit == 0, blocks, other)
    high = jnp.where(bit == 0, other, blocks)
    return jnp.concatenate([low, high], axis=1)


def summed_by_exchange(flat, axes):
    size = 1
    for axis in axes:
        size *= lax.axis_size(axis)
    pieces = lax.all_to_all(flat.reshape(size, -1), axes, 0, 0, tiled=True)
    total = jnp.sum(pieces, axis=0, keepdims=True)
    spread = jnp.broadcast_to(total.astype(jnp.bfloat16), pieces.shape)
    gathered = lax.all_to_all(spread, axes, 0, 0, tiled=True)
    return gathered.astype(flat.dtype).reshape(flat.shape)


def silu_slope(scores):
    sigmoid = jax.nn.sigmoid(scores)
    return sigmoid * (1.0 + scores * (1.0 - sigmoid))


def expand_blocks(block_rows, block_size):
    return jnp.repeat(jnp.repeat(block_rows, block_size, axis=0), block_size, axis=1)


def shards(
    queries,
    keys,
    values,
    gates,
    out_grad,
    time_bucket,
    lengths,
    block_map,
    bucket_bias_matrix,
    w_out,
):
    query_rows = queries[0]
    key_rows = keys[0]
    value_rows = values[0]
    gate_rows = gates[0]
    grad_rows = out_grad[0]
    local_rows, width = query_rows.shape
    head_count = bucket_bias_matrix.shape[0]
    bucket_count = bucket_bias_matrix.shape[1]
    head_dim = width // head_count
    scale = head_dim ** (-0.5)
    blocks_here = local_rows // BLK
    cycle_index = lax.axis_index("ctx")
    row_start = cycle_index * local_rows
    offsets = jnp.cumsum(lengths[0], dtype=jnp.int32) - lengths[0]

    def segment_of(positions):
        return jnp.sum(
            (positions[:, None] >= offsets[None, 1:]).astype(jnp.int32), axis=1, dtype=jnp.int32
        )

    bucket_ids = jnp.arange(bucket_count, dtype=jnp.int32)
    query_pos = row_start + jnp.arange(local_rows, dtype=jnp.int32)
    query_seg = segment_of(query_pos)
    query_bucket = lax.dynamic_slice_in_dim(time_bucket[0], row_start, local_rows, 0)
    query_bucket_indicator = (query_bucket[:, None] == bucket_ids[None, :]).astype(jnp.bfloat16)
    bias_matrix_rows = jnp.einsum(
        "lf,sfq->slq",
        query_bucket_indicator,
        bucket_bias_matrix,
        preferred_element_type=jnp.float32,
    ).astype(jnp.bfloat16)
    map_rows = lax.dynamic_slice_in_dim(block_map[0], cycle_index * blocks_here, blocks_here, 0)
    query_heads = query_rows.reshape(local_rows, head_count, head_dim)
    stacked = jnp.concatenate([key_rows, value_rows], axis=0)
    window = [stacked, passed_along(stacked, "ctx", 1), passed_along(stacked, "ctx", 2)]
    tiles = []
    attended = jnp.zeros((local_rows, head_count, head_dim), jnp.float32)
    for distance in range(3):
        key_first = row_start - distance * local_rows
        key_pos = key_first + jnp.arange(local_rows, dtype=jnp.int32)
        safe_first = jnp.maximum(key_first, 0)
        key_bucket = lax.dynamic_slice_in_dim(time_bucket[0], safe_first, local_rows, 0)
        key_bucket_indicator = (key_bucket[:, None] == bucket_ids[None, :]).astype(jnp.bfloat16)
        map_cols = lax.dynamic_slice_in_dim(map_rows, safe_first // BLK, blocks_here, 1)
        same_block = query_pos[:, None] // BLK == key_pos[None, :] // BLK
        key_visible = (
            (query_seg[:, None] == segment_of(key_pos)[None, :])
            & (key_pos[None, :] <= query_pos[:, None])
            & (key_pos[None, :] >= 0)
            & ((expand_blocks(map_cols, BLK) == 1) | same_block)
        )
        key_bias_terms = jnp.einsum(
            "vqx,px->vqp",
            bias_matrix_rows,
            key_bucket_indicator,
            preferred_element_type=jnp.float32,
        )
        visible, bias_terms, key_bucket_indicator = (
            key_visible,
            key_bias_terms,
            key_bucket_indicator,
        )
        forward_pair = window[distance]
        forward_key_heads = forward_pair[:local_rows].reshape(local_rows, head_count, head_dim)
        forward_value_heads = forward_pair[local_rows:].reshape(local_rows, head_count, head_dim)
        forward_scores = (
            jnp.einsum(
                "ihd,jhd->hij", query_heads, forward_key_heads, preferred_element_type=jnp.float32
            )
            * scale
            + bias_terms
        )
        forward_weights = jnp.where(visible[None], jax.nn.silu(forward_scores), 0.0).astype(
            jnp.bfloat16
        )
        attended_part = jnp.einsum(
            "hij,jhd->ihd", forward_weights, forward_value_heads, preferred_element_type=jnp.float32
        )
        attended = attended + attended_part
        tiles.append((visible, forward_scores, forward_weights, key_bucket_indicator))
    attended = attended.reshape(local_rows, width)
    centered = attended - jnp.mean(attended, axis=1, keepdims=True)
    inverse = lax.rsqrt(jnp.mean(centered * centered, axis=1, keepdims=True) + NORM_EPSILON)
    normed = centered * inverse
    dz_rows = lax.dot_general(
        grad_rows, w_out, (((1,), (1,)), ((), ())), preferred_element_type=jnp.float32
    )
    gate_float = gate_rows.astype(jnp.float32)
    gate_grad = (dz_rows * normed).astype(jnp.bfloat16)
    mixed = (normed * gate_float).astype(jnp.bfloat16)
    lifted = dz_rows * gate_float
    attended_grad = (
        (
            lifted
            - jnp.mean(lifted, axis=1, keepdims=True)
            - normed * jnp.mean(lifted * normed, axis=1, keepdims=True)
        )
        * inverse
    ).astype(jnp.bfloat16)
    grad_heads = attended_grad.reshape(local_rows, head_count, head_dim)
    indicator_float = query_bucket_indicator.astype(jnp.float32)
    dp_size = lax.axis_size("dp")
    weight_term = lax.dot_general(
        mixed, grad_rows, (((0,), (0,)), ((), ())), preferred_element_type=jnp.float32
    )
    weight_plan = [("split", "dp", mask) for mask in axis_bits("dp")]
    weight_plan.append(("exchange", "ctx", 0))
    weight_state = [weight_term.reshape(dp_size, -1), 0]

    def slot(anchor):
        blocks, done = weight_state
        if done < len(weight_plan):
            blocks, anchor = lax.optimization_barrier((blocks, anchor))
            kind, axis, mask = weight_plan[done]
            if kind == "exchange":
                weight_state[0] = summed_by_exchange(blocks.reshape(-1), (axis,))
            else:
                weight_state[0] = plan_step(blocks, kind, axis, mask)
            weight_state[1] = done + 1
        return anchor

    query_sum = jnp.zeros((local_rows, width), jnp.float32)
    share_sum = None
    key_terms = [None, None, None]
    sent = [None, None, None]
    for distance in (2, 1, 0):
        visible, scores, weights, key_bucket_indicator = tiles[distance]
        pair = slot(window[distance])
        if distance == 0:
            sent[2], pair = lax.optimization_barrier((sent[2], pair))
        key_heads = pair[:local_rows].reshape(local_rows, head_count, head_dim)
        value_heads = pair[local_rows:].reshape(local_rows, head_count, head_dim)
        weight_grad = jnp.einsum(
            "ihd,jhd->hij", grad_heads, value_heads, preferred_element_type=jnp.float32
        )
        value_part = jnp.einsum(
            "hij,ihd->jhd", weights, grad_heads, preferred_element_type=jnp.float32
        ).reshape(local_rows, width)
        score_gradient = jnp.where(visible[None], weight_grad * silu_slope(scores), 0.0).astype(
            jnp.bfloat16
        )
        score_gradient = slot(score_gradient)
        query_part = jnp.einsum(
            "hij,jhd->ihd", score_gradient, key_heads, preferred_element_type=jnp.float32
        ).reshape(local_rows, width)
        key_part = (
            jnp.einsum(
                "hij,ihd->jhd", score_gradient, query_heads, preferred_element_type=jnp.float32
            ).reshape(local_rows, width)
            * scale
        )
        bucket_share_piece = jnp.einsum(
            "rmw,wx->rmx", score_gradient, key_bucket_indicator, preferred_element_type=jnp.float32
        )
        share_sum = bucket_share_piece if share_sum is None else share_sum + bucket_share_piece
        query_sum = query_sum + query_part
        key_terms[distance] = jnp.concatenate([key_part, value_part], axis=0)
        if distance > 0:
            sent[distance] = passed_along(
                key_terms[distance].astype(jnp.bfloat16), "ctx", -distance
            )
    indicator_heads = jnp.broadcast_to(indicator_float[None], (head_count,) + indicator_float.shape)
    table_local = jnp.einsum(
        "cqp,cqk->cpk", indicator_heads, share_sum, precision=lax.Precision.HIGHEST
    )
    gathered = key_terms[0] + sent[1].astype(jnp.float32) + sent[2].astype(jnp.float32)
    query_grad = (query_sum * scale).astype(jnp.bfloat16)
    key_grad = gathered[:local_rows].astype(jnp.bfloat16)
    value_grad = gathered[local_rows:].astype(jnp.bfloat16)
    projection_grad = weight_state[0].reshape(width // dp_size, width)
    table_grad = summed_by_exchange(table_local.reshape(-1), ("ctx", "dp")).reshape(
        table_local.shape
    )
    return (
        query_grad[None],
        key_grad[None],
        value_grad[None],
        gate_grad[None],
        projection_grad,
        table_grad,
    )


def solution(mesh):
    return jax.shard_map(
        shards,
        mesh=mesh,
        in_specs=(
            P("dp", "ctx", None),
            P("dp", "ctx", None),
            P("dp", "ctx", None),
            P("dp", "ctx", None),
            P("dp", "ctx", None),
            P("dp", None),
            P("dp", None),
            P("dp", None, None),
            P(),
            P(),
        ),
        out_specs=(
            P("dp", "ctx", None),
            P("dp", "ctx", None),
            P("dp", "ctx", None),
            P("dp", "ctx", None),
            P("dp", None),
            P(),
        ),
        check_vma=False,
    )
```

```python
import jax
import jax.numpy as jnp
from jax import lax
from jax.sharding import PartitionSpec as P

BLK = 128


NORM_EPSILON = 1e-05


def passed_along(value, axis, by):
    length = lax.axis_size(axis)
    pairs = [(i, i + by) for i in range(length) if 0 <= i + by < length]
    return lax.ppermute(value, axis, pairs)


def exchanged(value, axis, mask):
    length = lax.axis_size(axis)
    pairs = [(i, i ^ mask) for i in range(length)]
    return lax.ppermute(value, axis, pairs)


def axis_bits(axis):
    length = lax.axis_size(axis)
    bits = []
    mask = 1
    while mask < length:
        bits.append(mask)
        mask *= 2
    return bits


def scatter_blocks(blocks, axis):
    index = lax.axis_index(axis)
    for mask in axis_bits(axis):
        bit = (index // mask) % 2
        pairs = blocks.reshape(blocks.shape[0] // 2, 2, blocks.shape[1])
        keep = lax.dynamic_index_in_dim(pairs, bit, axis=1, keepdims=False)
        send = lax.dynamic_index_in_dim(pairs, 1 - bit, axis=1, keepdims=False)
        blocks = keep + exchanged(send, axis, mask)
    return blocks[0]


def gather_blocks(chunk, axis):
    index = lax.axis_index(axis)
    held = chunk[None]
    for mask in reversed(axis_bits(axis)):
        bit = (index // mask) % 2
        other = exchanged(held, axis, mask)
        low = jnp.where(bit == 0, held, other)
        high = jnp.where(bit == 0, other, held)
        held = jnp.stack([low, high], axis=1).reshape(held.shape[0] * 2, held.shape[1])
    return held


def summed_over(flat, axis):
    size = lax.axis_size(axis)
    part = scatter_blocks(flat.reshape(size, flat.shape[0] // size), axis)
    return gather_blocks(part, axis).reshape(flat.shape)


def plan_step(blocks, kind, axis, mask):
    bit = (lax.axis_index(axis) // mask) % 2
    if kind == "split":
        if blocks.shape[0] == 1:
            blocks = blocks.reshape(2, -1)
        pairs = blocks.reshape(blocks.shape[0] // 2, 2, blocks.shape[1])
        keep = lax.dynamic_index_in_dim(pairs, bit, axis=1, keepdims=False)
        send = lax.dynamic_index_in_dim(pairs, 1 - bit, axis=1, keepdims=False)
        return keep + exchanged(send, axis, mask)
    other = exchanged(blocks, axis, mask)
    low = jnp.where(bit == 0, blocks, other)
    high = jnp.where(bit == 0, other, blocks)
    return jnp.concatenate([low, high], axis=1)


def summed_by_exchange(flat, axes):
    size = 1
    for axis in axes:
        size *= lax.axis_size(axis)
    pieces = lax.all_to_all(flat.reshape(size, -1), axes, 0, 0, tiled=True)
    total = jnp.sum(pieces, axis=0, keepdims=True)
    spread = jnp.broadcast_to(total.astype(jnp.bfloat16), pieces.shape)
    gathered = lax.all_to_all(spread, axes, 0, 0, tiled=True)
    return gathered.astype(flat.dtype).reshape(flat.shape)


def silu_slope(scores):
    sigmoid = jax.nn.sigmoid(scores)
    return sigmoid * (1.0 + scores * (1.0 - sigmoid))


def expand_blocks(block_rows, block_size):
    return jnp.repeat(jnp.repeat(block_rows, block_size, axis=0), block_size, axis=1)


def shards(
    queries,
    keys,
    values,
    gates,
    out_grad,
    time_bucket,
    lengths,
    block_map,
    bucket_bias_matrix,
    w_out,
):
    query_rows = queries[0]
    key_rows = keys[0]
    value_rows = values[0]
    gate_rows = gates[0]
    grad_rows = out_grad[0]
    local_rows, width = query_rows.shape
    head_count = bucket_bias_matrix.shape[0]
    bucket_count = bucket_bias_matrix.shape[1]
    head_dim = width // head_count
    scale = head_dim ** (-0.5)
    blocks_here = local_rows // BLK
    cycle_index = lax.axis_index("ctx")
    row_start = cycle_index * local_rows
    offsets = jnp.cumsum(lengths[0], dtype=jnp.int32) - lengths[0]

    def segment_of(positions):
        return jnp.sum(
            (positions[:, None] >= offsets[None, 1:]).astype(jnp.int32), axis=1, dtype=jnp.int32
        )

    bucket_ids = jnp.arange(bucket_count, dtype=jnp.int32)
    query_pos = row_start + jnp.arange(local_rows, dtype=jnp.int32)
    query_seg = segment_of(query_pos)
    query_bucket = lax.dynamic_slice_in_dim(time_bucket[0], row_start, local_rows, 0)
    query_bucket_indicator = (query_bucket[:, None] == bucket_ids[None, :]).astype(jnp.bfloat16)
    bias_matrix_rows = jnp.einsum(
        "lf,sfq->slq",
        query_bucket_indicator,
        bucket_bias_matrix,
        preferred_element_type=jnp.float32,
    ).astype(jnp.bfloat16)
    map_rows = lax.dynamic_slice_in_dim(block_map[0], cycle_index * blocks_here, blocks_here, 0)
    query_heads = query_rows.reshape(local_rows, head_count, head_dim)
    stacked = jnp.concatenate([key_rows, value_rows], axis=0)
    window = [stacked, passed_along(stacked, "ctx", 1), passed_along(stacked, "ctx", 2)]
    tiles = []
    attended = jnp.zeros((local_rows, head_count, head_dim), jnp.float32)
    for distance in range(3):
        key_first = row_start - distance * local_rows
        key_pos = key_first + jnp.arange(local_rows, dtype=jnp.int32)
        safe_first = jnp.maximum(key_first, 0)
        key_bucket = lax.dynamic_slice_in_dim(time_bucket[0], safe_first, local_rows, 0)
        key_bucket_indicator = (key_bucket[:, None] == bucket_ids[None, :]).astype(jnp.bfloat16)
        map_cols = lax.dynamic_slice_in_dim(map_rows, safe_first // BLK, blocks_here, 1)
        same_block = query_pos[:, None] // BLK == key_pos[None, :] // BLK
        key_visible = (
            (query_seg[:, None] == segment_of(key_pos)[None, :])
            & (key_pos[None, :] <= query_pos[:, None])
            & (key_pos[None, :] >= 0)
            & ((expand_blocks(map_cols, BLK) == 1) | same_block)
        )
        key_bias_terms = jnp.einsum(
            "vqx,px->vqp",
            bias_matrix_rows,
            key_bucket_indicator,
            preferred_element_type=jnp.float32,
        )
        visible, bias_terms, key_bucket_indicator = (
            key_visible,
            key_bias_terms,
            key_bucket_indicator,
        )
        forward_pair = window[distance]
        forward_key_heads = forward_pair[:local_rows].reshape(local_rows, head_count, head_dim)
        forward_value_heads = forward_pair[local_rows:].reshape(local_rows, head_count, head_dim)
        forward_scores = (
            jnp.einsum(
                "ihd,jhd->hij", query_heads, forward_key_heads, preferred_element_type=jnp.float32
            )
            * scale
            + bias_terms
        )
        forward_weights = jnp.where(visible[None], jax.nn.silu(forward_scores), 0.0).astype(
            jnp.bfloat16
        )
        attended_part = jnp.einsum(
            "hij,jhd->ihd", forward_weights, forward_value_heads, preferred_element_type=jnp.float32
        )
        attended = attended + attended_part
        tiles.append((visible, forward_scores, forward_weights, key_bucket_indicator))
    attended = attended.reshape(local_rows, width)
    centered = attended - jnp.mean(attended, axis=1, keepdims=True)
    inverse = lax.rsqrt(jnp.mean(centered * centered, axis=1, keepdims=True) + NORM_EPSILON)
    normed = centered * inverse
    dz_rows = lax.dot_general(
        grad_rows, w_out, (((1,), (1,)), ((), ())), preferred_element_type=jnp.float32
    )
    gate_float = gate_rows.astype(jnp.float32)
    gate_grad = (dz_rows * normed).astype(jnp.bfloat16)
    mixed = (normed * gate_float).astype(jnp.bfloat16)
    lifted = dz_rows * gate_float
    attended_grad = (
        (
            lifted
            - jnp.mean(lifted, axis=1, keepdims=True)
            - normed * jnp.mean(lifted * normed, axis=1, keepdims=True)
        )
        * inverse
    ).astype(jnp.bfloat16)
    grad_heads = attended_grad.reshape(local_rows, head_count, head_dim)
    indicator_float = query_bucket_indicator.astype(jnp.float32)
    dp_size = lax.axis_size("dp")
    weight_term = lax.dot_general(
        mixed, grad_rows, (((0,), (0,)), ((), ())), preferred_element_type=jnp.float32
    )
    weight_plan = [("split", "dp", mask) for mask in axis_bits("dp")]
    weight_plan.append(("exchange", "ctx", 0))
    weight_state = [weight_term.reshape(dp_size, -1), 0]

    def slot(anchor):
        blocks, done = weight_state
        if done < len(weight_plan):
            blocks, anchor = lax.optimization_barrier((blocks, anchor))
            kind, axis, mask = weight_plan[done]
            if kind == "exchange":
                weight_state[0] = summed_by_exchange(blocks.reshape(-1), (axis,))
            else:
                weight_state[0] = plan_step(blocks, kind, axis, mask)
            weight_state[1] = done + 1
        return anchor

    query_sum = jnp.zeros((local_rows, width), jnp.float32)
    share_sum = None
    key_terms = [None, None, None]
    sent = [None, None, None]
    for distance in (2, 1, 0):
        visible, scores, weights, key_bucket_indicator = tiles[distance]
        pair = slot(window[distance])
        if distance == 0:
            sent[2], pair = lax.optimization_barrier((sent[2], pair))
        key_heads = pair[:local_rows].reshape(local_rows, head_count, head_dim)
        value_heads = pair[local_rows:].reshape(local_rows, head_count, head_dim)
        weight_grad = jnp.einsum(
            "ihd,jhd->hij", grad_heads, value_heads, preferred_element_type=jnp.float32
        )
        value_part = jnp.einsum(
            "hij,ihd->jhd", weights, grad_heads, preferred_element_type=jnp.float32
        ).reshape(local_rows, width)
        score_gradient = jnp.where(visible[None], weight_grad * silu_slope(scores), 0.0).astype(
            jnp.bfloat16
        )
        score_gradient = slot(score_gradient)
        query_part = jnp.einsum(
            "hij,jhd->ihd", score_gradient, key_heads, preferred_element_type=jnp.float32
        ).reshape(local_rows, width)
        key_part = (
            jnp.einsum(
                "hij,ihd->jhd", score_gradient, query_heads, preferred_element_type=jnp.float32
            ).reshape(local_rows, width)
            * scale
        )
        bucket_share_piece = jnp.einsum(
            "rmw,wx->rmx", score_gradient, key_bucket_indicator, preferred_element_type=jnp.float32
        )
        share_sum = bucket_share_piece if share_sum is None else share_sum + bucket_share_piece
        query_sum = query_sum + query_part
        key_terms[distance] = jnp.concatenate([key_part, value_part], axis=0)
        if distance > 0:
            sent[distance] = passed_along(
                key_terms[distance].astype(jnp.bfloat16), "ctx", -distance
            )
    indicator_heads = jnp.broadcast_to(
        query_bucket_indicator[None], (head_count,) + query_bucket_indicator.shape
    )
    share_high = share_sum.astype(jnp.bfloat16)
    share_rest = share_sum - share_high.astype(jnp.float32)
    share_mid = share_rest.astype(jnp.bfloat16)
    share_low = (share_rest - share_mid.astype(jnp.float32)).astype(jnp.bfloat16)
    table_local = None
    for share_part in (share_low, share_mid, share_high):
        term = jnp.einsum(
            "cqp,cqk->cpk", indicator_heads, share_part, preferred_element_type=jnp.float32
        )
        table_local = term if table_local is None else table_local + term
    gathered = key_terms[0] + sent[1].astype(jnp.float32) + sent[2].astype(jnp.float32)
    query_grad = (query_sum * scale).astype(jnp.bfloat16)
    key_grad = gathered[:local_rows].astype(jnp.bfloat16)
    value_grad = gathered[local_rows:].astype(jnp.bfloat16)
    projection_grad = weight_state[0].reshape(width // dp_size, width)
    table_grad = summed_by_exchange(table_local.reshape(-1), ("ctx", "dp")).reshape(
        table_local.shape
    )
    return (
        query_grad[None],
        key_grad[None],
        value_grad[None],
        gate_grad[None],
        projection_grad,
        table_grad,
    )


def solution(mesh):
    return jax.shard_map(
        shards,
        mesh=mesh,
        in_specs=(
            P("dp", "ctx", None),
            P("dp", "ctx", None),
            P("dp", "ctx", None),
            P("dp", "ctx", None),
            P("dp", "ctx", None),
            P("dp", None),
            P("dp", None),
            P("dp", None, None),
            P(),
            P(),
        ),
        out_specs=(
            P("dp", "ctx", None),
            P("dp", "ctx", None),
            P("dp", "ctx", None),
            P("dp", "ctx", None),
            P("dp", None),
            P(),
        ),
        check_vma=False,
    )
```

```python
import jax
import jax.numpy as jnp
from jax import lax
from jax.sharding import PartitionSpec as P

BLK = 128


NORM_EPSILON = 1e-05


def passed_along(value, axis, by):
    length = lax.axis_size(axis)
    pairs = [(i, i + by) for i in range(length) if 0 <= i + by < length]
    return lax.ppermute(value, axis, pairs)


def exchanged(value, axis, mask):
    length = lax.axis_size(axis)
    pairs = [(i, i ^ mask) for i in range(length)]
    return lax.ppermute(value, axis, pairs)


def axis_bits(axis):
    length = lax.axis_size(axis)
    bits = []
    mask = 1
    while mask < length:
        bits.append(mask)
        mask *= 2
    return bits


def scatter_blocks(blocks, axis):
    index = lax.axis_index(axis)
    for mask in axis_bits(axis):
        bit = (index // mask) % 2
        pairs = blocks.reshape(blocks.shape[0] // 2, 2, blocks.shape[1])
        keep = lax.dynamic_index_in_dim(pairs, bit, axis=1, keepdims=False)
        send = lax.dynamic_index_in_dim(pairs, 1 - bit, axis=1, keepdims=False)
        blocks = keep + exchanged(send, axis, mask)
    return blocks[0]


def gather_blocks(chunk, axis):
    index = lax.axis_index(axis)
    held = chunk[None]
    for mask in reversed(axis_bits(axis)):
        bit = (index // mask) % 2
        other = exchanged(held, axis, mask)
        low = jnp.where(bit == 0, held, other)
        high = jnp.where(bit == 0, other, held)
        held = jnp.stack([low, high], axis=1).reshape(held.shape[0] * 2, held.shape[1])
    return held


def summed_over(flat, axis):
    size = lax.axis_size(axis)
    part = scatter_blocks(flat.reshape(size, flat.shape[0] // size), axis)
    return gather_blocks(part, axis).reshape(flat.shape)


def plan_step(blocks, kind, axis, mask):
    bit = (lax.axis_index(axis) // mask) % 2
    if kind == "split":
        if blocks.shape[0] == 1:
            blocks = blocks.reshape(2, -1)
        pairs = blocks.reshape(blocks.shape[0] // 2, 2, blocks.shape[1])
        keep = lax.dynamic_index_in_dim(pairs, bit, axis=1, keepdims=False)
        send = lax.dynamic_index_in_dim(pairs, 1 - bit, axis=1, keepdims=False)
        return keep + exchanged(send, axis, mask)
    other = exchanged(blocks, axis, mask)
    low = jnp.where(bit == 0, blocks, other)
    high = jnp.where(bit == 0, other, blocks)
    return jnp.concatenate([low, high], axis=1)


def summed_by_exchange(flat, axes):
    size = 1
    for axis in axes:
        size *= lax.axis_size(axis)
    pieces = lax.all_to_all(flat.reshape(size, -1), axes, 0, 0, tiled=True)
    total = jnp.sum(pieces, axis=0, keepdims=True)
    spread = jnp.broadcast_to(total.astype(jnp.bfloat16), pieces.shape)
    gathered = lax.all_to_all(spread, axes, 0, 0, tiled=True)
    return gathered.astype(flat.dtype).reshape(flat.shape)


def silu_slope(scores):
    sigmoid = jax.nn.sigmoid(scores)
    return sigmoid * (1.0 + scores * (1.0 - sigmoid))


def expand_blocks(block_rows, block_size):
    return jnp.repeat(jnp.repeat(block_rows, block_size, axis=0), block_size, axis=1)


def shards(
    queries,
    keys,
    values,
    gates,
    out_grad,
    time_bucket,
    lengths,
    block_map,
    bucket_bias_matrix,
    w_out,
):
    query_rows = queries[0]
    key_rows = keys[0]
    value_rows = values[0]
    gate_rows = gates[0]
    grad_rows = out_grad[0]
    local_rows, width = query_rows.shape
    head_count = bucket_bias_matrix.shape[0]
    bucket_count = bucket_bias_matrix.shape[1]
    head_dim = width // head_count
    scale = head_dim ** (-0.5)
    blocks_here = local_rows // BLK
    cycle_index = lax.axis_index("ctx")
    row_start = cycle_index * local_rows
    offsets = jnp.cumsum(lengths[0], dtype=jnp.int32) - lengths[0]

    def segment_of(positions):
        return jnp.sum(
            (positions[:, None] >= offsets[None, 1:]).astype(jnp.int32), axis=1, dtype=jnp.int32
        )

    bucket_ids = jnp.arange(bucket_count, dtype=jnp.int32)
    query_pos = row_start + jnp.arange(local_rows, dtype=jnp.int32)
    query_seg = segment_of(query_pos)
    query_bucket = lax.dynamic_slice_in_dim(time_bucket[0], row_start, local_rows, 0)
    query_bucket_indicator = (query_bucket[:, None] == bucket_ids[None, :]).astype(jnp.bfloat16)
    bias_matrix_rows = jnp.einsum(
        "lf,sfq->slq",
        query_bucket_indicator,
        bucket_bias_matrix,
        preferred_element_type=jnp.float32,
    ).astype(jnp.bfloat16)
    map_rows = lax.dynamic_slice_in_dim(block_map[0], cycle_index * blocks_here, blocks_here, 0)
    query_heads = query_rows.reshape(local_rows, head_count, head_dim)
    stacked = jnp.concatenate([key_rows, value_rows], axis=0)
    window = [stacked, passed_along(stacked, "ctx", 1), passed_along(stacked, "ctx", 2)]
    tiles = []
    attended = jnp.zeros((local_rows, head_count, head_dim), jnp.float32)
    for distance in range(3):
        key_first = row_start - distance * local_rows
        key_pos = key_first + jnp.arange(local_rows, dtype=jnp.int32)
        safe_first = jnp.maximum(key_first, 0)
        key_bucket = lax.dynamic_slice_in_dim(time_bucket[0], safe_first, local_rows, 0)
        key_bucket_indicator = (key_bucket[:, None] == bucket_ids[None, :]).astype(jnp.bfloat16)
        map_cols = lax.dynamic_slice_in_dim(map_rows, safe_first // BLK, blocks_here, 1)
        same_block = query_pos[:, None] // BLK == key_pos[None, :] // BLK
        key_visible = (
            (query_seg[:, None] == segment_of(key_pos)[None, :])
            & (key_pos[None, :] <= query_pos[:, None])
            & (key_pos[None, :] >= 0)
            & ((expand_blocks(map_cols, BLK) == 1) | same_block)
        )
        key_bias_terms = jnp.einsum(
            "vqx,px->vqp",
            bias_matrix_rows,
            key_bucket_indicator,
            preferred_element_type=jnp.float32,
        )
        visible, bias_terms, key_bucket_indicator = (
            key_visible,
            key_bias_terms,
            key_bucket_indicator,
        )
        forward_pair = window[distance]
        forward_key_heads = forward_pair[:local_rows].reshape(local_rows, head_count, head_dim)
        forward_value_heads = forward_pair[local_rows:].reshape(local_rows, head_count, head_dim)
        forward_scores = (
            jnp.einsum(
                "ihd,jhd->hij", query_heads, forward_key_heads, preferred_element_type=jnp.float32
            )
            * scale
            + bias_terms
        )
        forward_weights = jnp.where(visible[None], jax.nn.silu(forward_scores), 0.0).astype(
            jnp.bfloat16
        )
        attended_part = jnp.einsum(
            "hij,jhd->ihd", forward_weights, forward_value_heads, preferred_element_type=jnp.float32
        )
        attended = attended + attended_part
        tiles.append((visible, forward_scores, forward_weights, key_bucket_indicator))
    attended = attended.reshape(local_rows, width)
    centered = attended - jnp.mean(attended, axis=1, keepdims=True)
    inverse = lax.rsqrt(jnp.mean(centered * centered, axis=1, keepdims=True) + NORM_EPSILON)
    normed = centered * inverse
    dz_rows = lax.dot_general(
        grad_rows, w_out, (((1,), (1,)), ((), ())), preferred_element_type=jnp.float32
    )
    gate_float = gate_rows.astype(jnp.float32)
    gate_grad = (dz_rows * normed).astype(jnp.bfloat16)
    mixed = (normed * gate_float).astype(jnp.bfloat16)
    lifted = dz_rows * gate_float
    attended_grad = (
        (
            lifted
            - jnp.mean(lifted, axis=1, keepdims=True)
            - normed * jnp.mean(lifted * normed, axis=1, keepdims=True)
        )
        * inverse
    ).astype(jnp.bfloat16)
    grad_heads = attended_grad.reshape(local_rows, head_count, head_dim)
    indicator_float = query_bucket_indicator.astype(jnp.float32)
    dp_size = lax.axis_size("dp")
    weight_term = lax.dot_general(
        mixed, grad_rows, (((0,), (0,)), ((), ())), preferred_element_type=jnp.float32
    )
    weight_plan = [("split", "dp", mask) for mask in axis_bits("dp")]
    weight_plan.append(("exchange", "ctx", 0))
    weight_state = [weight_term.reshape(dp_size, -1), 0]

    def slot(anchor):
        blocks, done = weight_state
        if done < len(weight_plan):
            blocks, anchor = lax.optimization_barrier((blocks, anchor))
            kind, axis, mask = weight_plan[done]
            if kind == "exchange":
                weight_state[0] = summed_by_exchange(blocks.reshape(-1), (axis,))
            else:
                weight_state[0] = plan_step(blocks, kind, axis, mask)
            weight_state[1] = done + 1
        return anchor

    query_sum = jnp.zeros((local_rows, width), jnp.float32)
    share_sum = None
    key_terms = [None, None, None]
    sent = [None, None, None]
    for distance in (2, 1, 0):
        visible, scores, weights, key_bucket_indicator = tiles[distance]
        pair = slot(window[distance])
        key_heads = pair[:local_rows].reshape(local_rows, head_count, head_dim)
        value_heads = pair[local_rows:].reshape(local_rows, head_count, head_dim)
        weight_grad = jnp.einsum(
            "ihd,jhd->hij", grad_heads, value_heads, preferred_element_type=jnp.float32
        )
        value_part = jnp.einsum(
            "hij,ihd->jhd", weights, grad_heads, preferred_element_type=jnp.float32
        ).reshape(local_rows, width)
        score_gradient = jnp.where(visible[None], weight_grad * silu_slope(scores), 0.0).astype(
            jnp.bfloat16
        )
        score_gradient = slot(score_gradient)
        query_part = jnp.einsum(
            "hij,jhd->ihd", score_gradient, key_heads, preferred_element_type=jnp.float32
        ).reshape(local_rows, width)
        key_part = (
            jnp.einsum(
                "hij,ihd->jhd", score_gradient, query_heads, preferred_element_type=jnp.float32
            ).reshape(local_rows, width)
            * scale
        )
        bucket_share_piece = jnp.einsum(
            "rmw,wx->rmx", score_gradient, key_bucket_indicator, preferred_element_type=jnp.float32
        )
        share_sum = bucket_share_piece if share_sum is None else share_sum + bucket_share_piece
        query_sum = query_sum + query_part
        key_terms[distance] = jnp.concatenate([key_part, value_part], axis=0)
        if distance > 0:
            sent[distance] = passed_along(
                key_terms[distance].astype(jnp.bfloat16), "ctx", -distance
            )
    indicator_heads = jnp.broadcast_to(indicator_float[None], (head_count,) + indicator_float.shape)
    table_local = jnp.einsum(
        "cqp,cqk->cpk", indicator_heads, share_sum, precision=lax.Precision.HIGHEST
    )
    gathered = key_terms[0] + sent[1].astype(jnp.float32) + sent[2].astype(jnp.float32)
    query_grad = (query_sum * scale).astype(jnp.bfloat16)
    key_grad = gathered[:local_rows].astype(jnp.bfloat16)
    value_grad = gathered[local_rows:].astype(jnp.bfloat16)
    projection_grad = weight_state[0].reshape(width // dp_size, width)
    table_grad = summed_by_exchange(table_local.reshape(-1), ("ctx", "dp")).reshape(
        table_local.shape
    )
    return (
        query_grad[None],
        key_grad[None],
        value_grad[None],
        gate_grad[None],
        projection_grad,
        table_grad,
    )


def solution(mesh):
    return jax.shard_map(
        shards,
        mesh=mesh,
        in_specs=(
            P("dp", "ctx", None),
            P("dp", "ctx", None),
            P("dp", "ctx", None),
            P("dp", "ctx", None),
            P("dp", "ctx", None),
            P("dp", None),
            P("dp", None),
            P("dp", None, None),
            P(),
            P(),
        ),
        out_specs=(
            P("dp", "ctx", None),
            P("dp", "ctx", None),
            P("dp", "ctx", None),
            P("dp", "ctx", None),
            P("dp", None),
            P(),
        ),
        check_vma=False,
    )
```

```python
import jax
import jax.numpy as jnp
from jax import lax
from jax.sharding import PartitionSpec as P

BLK = 128


NORM_EPSILON = 1e-05


def passed_along(value, axis, by):
    length = lax.axis_size(axis)
    pairs = [(i, i + by) for i in range(length) if 0 <= i + by < length]
    return lax.ppermute(value, axis, pairs)


def exchanged(value, axis, mask):
    length = lax.axis_size(axis)
    pairs = [(i, i ^ mask) for i in range(length)]
    return lax.ppermute(value, axis, pairs)


def axis_bits(axis):
    length = lax.axis_size(axis)
    bits = []
    mask = 1
    while mask < length:
        bits.append(mask)
        mask *= 2
    return bits


def scatter_blocks(blocks, axis):
    index = lax.axis_index(axis)
    for mask in axis_bits(axis):
        bit = (index // mask) % 2
        pairs = blocks.reshape(blocks.shape[0] // 2, 2, blocks.shape[1])
        keep = lax.dynamic_index_in_dim(pairs, bit, axis=1, keepdims=False)
        send = lax.dynamic_index_in_dim(pairs, 1 - bit, axis=1, keepdims=False)
        blocks = keep + exchanged(send, axis, mask)
    return blocks[0]


def gather_blocks(chunk, axis):
    index = lax.axis_index(axis)
    held = chunk[None]
    for mask in reversed(axis_bits(axis)):
        bit = (index // mask) % 2
        other = exchanged(held, axis, mask)
        low = jnp.where(bit == 0, held, other)
        high = jnp.where(bit == 0, other, held)
        held = jnp.stack([low, high], axis=1).reshape(held.shape[0] * 2, held.shape[1])
    return held


def summed_over(flat, axis):
    size = lax.axis_size(axis)
    part = scatter_blocks(flat.reshape(size, flat.shape[0] // size), axis)
    return gather_blocks(part, axis).reshape(flat.shape)


def plan_step(blocks, kind, axis, mask):
    bit = (lax.axis_index(axis) // mask) % 2
    if kind == "split":
        if blocks.shape[0] == 1:
            blocks = blocks.reshape(2, -1)
        pairs = blocks.reshape(blocks.shape[0] // 2, 2, blocks.shape[1])
        keep = lax.dynamic_index_in_dim(pairs, bit, axis=1, keepdims=False)
        send = lax.dynamic_index_in_dim(pairs, 1 - bit, axis=1, keepdims=False)
        return keep + exchanged(send, axis, mask)
    other = exchanged(blocks, axis, mask)
    low = jnp.where(bit == 0, blocks, other)
    high = jnp.where(bit == 0, other, blocks)
    return jnp.concatenate([low, high], axis=1)


def summed_by_exchange(flat, axes):
    size = 1
    for axis in axes:
        size *= lax.axis_size(axis)
    pieces = lax.all_to_all(flat.reshape(size, -1), axes, 0, 0, tiled=True)
    total = jnp.sum(pieces, axis=0, keepdims=True)
    spread = jnp.broadcast_to(total.astype(jnp.bfloat16), pieces.shape)
    gathered = lax.all_to_all(spread, axes, 0, 0, tiled=True)
    return gathered.astype(flat.dtype).reshape(flat.shape)


def silu_slope(scores):
    sigmoid = jax.nn.sigmoid(scores)
    return sigmoid * (1.0 + scores * (1.0 - sigmoid))


def expand_blocks(block_rows, block_size):
    return jnp.repeat(jnp.repeat(block_rows, block_size, axis=0), block_size, axis=1)


def shards(
    queries,
    keys,
    values,
    gates,
    out_grad,
    time_bucket,
    lengths,
    block_map,
    bucket_bias_matrix,
    w_out,
):
    query_rows = queries[0]
    key_rows = keys[0]
    value_rows = values[0]
    gate_rows = gates[0]
    grad_rows = out_grad[0]
    local_rows, width = query_rows.shape
    head_count = bucket_bias_matrix.shape[0]
    bucket_count = bucket_bias_matrix.shape[1]
    head_dim = width // head_count
    scale = head_dim ** (-0.5)
    blocks_here = local_rows // BLK
    cycle_index = lax.axis_index("ctx")
    row_start = cycle_index * local_rows
    offsets = jnp.cumsum(lengths[0], dtype=jnp.int32) - lengths[0]

    def segment_of(positions):
        return jnp.sum(
            (positions[:, None] >= offsets[None, 1:]).astype(jnp.int32), axis=1, dtype=jnp.int32
        )

    bucket_ids = jnp.arange(bucket_count, dtype=jnp.int32)
    query_pos = row_start + jnp.arange(local_rows, dtype=jnp.int32)
    query_seg = segment_of(query_pos)
    query_bucket = lax.dynamic_slice_in_dim(time_bucket[0], row_start, local_rows, 0)
    query_bucket_indicator = (query_bucket[:, None] == bucket_ids[None, :]).astype(jnp.bfloat16)
    bias_matrix_rows = jnp.einsum(
        "lf,sfq->slq",
        query_bucket_indicator,
        bucket_bias_matrix,
        preferred_element_type=jnp.float32,
    ).astype(jnp.bfloat16)
    map_rows = lax.dynamic_slice_in_dim(block_map[0], cycle_index * blocks_here, blocks_here, 0)
    query_heads = query_rows.reshape(local_rows, head_count, head_dim)
    stacked = jnp.concatenate([key_rows, value_rows], axis=0)
    window = [stacked, passed_along(stacked, "ctx", 1), passed_along(stacked, "ctx", 2)]
    tiles = []
    attended = jnp.zeros((local_rows, head_count, head_dim), jnp.float32)
    for distance in range(3):
        key_first = row_start - distance * local_rows
        key_pos = key_first + jnp.arange(local_rows, dtype=jnp.int32)
        safe_first = jnp.maximum(key_first, 0)
        key_bucket = lax.dynamic_slice_in_dim(time_bucket[0], safe_first, local_rows, 0)
        key_bucket_indicator = (key_bucket[:, None] == bucket_ids[None, :]).astype(jnp.bfloat16)
        map_cols = lax.dynamic_slice_in_dim(map_rows, safe_first // BLK, blocks_here, 1)
        same_block = query_pos[:, None] // BLK == key_pos[None, :] // BLK
        key_visible = (
            (query_seg[:, None] == segment_of(key_pos)[None, :])
            & (key_pos[None, :] <= query_pos[:, None])
            & (key_pos[None, :] >= 0)
            & ((expand_blocks(map_cols, BLK) == 1) | same_block)
        )
        key_bias_terms = jnp.einsum(
            "vqx,px->vqp",
            bias_matrix_rows,
            key_bucket_indicator,
            preferred_element_type=jnp.float32,
        )
        visible, bias_terms, key_bucket_indicator = (
            key_visible,
            key_bias_terms,
            key_bucket_indicator,
        )
        forward_pair = window[distance]
        forward_key_heads = forward_pair[:local_rows].reshape(local_rows, head_count, head_dim)
        forward_value_heads = forward_pair[local_rows:].reshape(local_rows, head_count, head_dim)
        forward_scores = (
            jnp.einsum(
                "ihd,jhd->hij", query_heads, forward_key_heads, preferred_element_type=jnp.float32
            )
            * scale
            + bias_terms
        )
        forward_weights = jnp.where(visible[None], jax.nn.silu(forward_scores), 0.0).astype(
            jnp.bfloat16
        )
        attended_part = jnp.einsum(
            "hij,jhd->ihd", forward_weights, forward_value_heads, preferred_element_type=jnp.float32
        )
        attended = attended + attended_part
        tiles.append((visible, forward_scores, forward_weights, key_bucket_indicator))
    attended = attended.reshape(local_rows, width)
    centered = attended - jnp.mean(attended, axis=1, keepdims=True)
    inverse = lax.rsqrt(jnp.mean(centered * centered, axis=1, keepdims=True) + NORM_EPSILON)
    normed = centered * inverse
    dz_rows = lax.dot_general(
        grad_rows, w_out, (((1,), (1,)), ((), ())), preferred_element_type=jnp.float32
    )
    gate_float = gate_rows.astype(jnp.float32)
    gate_grad = (dz_rows * normed).astype(jnp.bfloat16)
    mixed = (normed * gate_float).astype(jnp.bfloat16)
    lifted = dz_rows * gate_float
    attended_grad = (
        (
            lifted
            - jnp.mean(lifted, axis=1, keepdims=True)
            - normed * jnp.mean(lifted * normed, axis=1, keepdims=True)
        )
        * inverse
    ).astype(jnp.bfloat16)
    grad_heads = attended_grad.reshape(local_rows, head_count, head_dim)
    indicator_float = query_bucket_indicator.astype(jnp.float32)
    dp_size = lax.axis_size("dp")
    weight_term = lax.dot_general(
        mixed, grad_rows, (((0,), (0,)), ((), ())), preferred_element_type=jnp.float32
    )
    weight_plan = [("split", "dp", mask) for mask in axis_bits("dp")]
    weight_plan.append(("exchange", "ctx", 0))
    weight_state = [weight_term.reshape(dp_size, -1), 0]

    def slot(anchor):
        blocks, done = weight_state
        if done < len(weight_plan):
            blocks, anchor = lax.optimization_barrier((blocks, anchor))
            kind, axis, mask = weight_plan[done]
            if kind == "exchange":
                weight_state[0] = summed_by_exchange(blocks.reshape(-1), (axis,))
            else:
                weight_state[0] = plan_step(blocks, kind, axis, mask)
            weight_state[1] = done + 1
        return anchor

    query_sum = jnp.zeros((local_rows, width), jnp.float32)
    share_sum = None
    key_terms = [None, None, None]
    sent = [None, None, None]
    for distance in (2, 1, 0):
        visible, scores, weights, key_bucket_indicator = tiles[distance]
        pair = slot(window[distance])
        if distance == 0:
            sent[2], pair = lax.optimization_barrier((sent[2], pair))
        key_heads = pair[:local_rows].reshape(local_rows, head_count, head_dim)
        value_heads = pair[local_rows:].reshape(local_rows, head_count, head_dim)
        weight_grad = jnp.einsum(
            "ihd,jhd->hij", grad_heads, value_heads, preferred_element_type=jnp.float32
        )
        value_part = jnp.einsum(
            "hij,ihd->jhd", weights, grad_heads, preferred_element_type=jnp.float32
        ).reshape(local_rows, width)
        score_gradient = jnp.where(visible[None], weight_grad * silu_slope(scores), 0.0).astype(
            jnp.bfloat16
        )
        score_gradient = slot(score_gradient)
        query_part = jnp.einsum(
            "hij,jhd->ihd", score_gradient, key_heads, preferred_element_type=jnp.float32
        ).reshape(local_rows, width)
        key_part = (
            jnp.einsum(
                "hij,ihd->jhd", score_gradient, query_heads, preferred_element_type=jnp.float32
            ).reshape(local_rows, width)
            * scale
        )
        bucket_share_piece = jnp.einsum(
            "rmw,wx->rmx", score_gradient, key_bucket_indicator, preferred_element_type=jnp.float32
        )
        share_sum = bucket_share_piece if share_sum is None else share_sum + bucket_share_piece
        query_sum = query_sum + query_part
        key_terms[distance] = jnp.concatenate([key_part, value_part], axis=0)
        if distance > 0:
            sent[distance] = passed_along(
                key_terms[distance].astype(jnp.bfloat16), "ctx", -distance
            )
    indicator_heads = jnp.broadcast_to(indicator_float[None], (head_count,) + indicator_float.shape)
    table_local = jnp.einsum(
        "cqp,cqk->cpk", indicator_heads, share_sum, precision=lax.Precision.HIGHEST
    )
    gathered = key_terms[0] + sent[1].astype(jnp.float32) + sent[2].astype(jnp.float32)
    query_grad = (query_sum * scale).astype(jnp.bfloat16)
    key_grad = gathered[:local_rows].astype(jnp.bfloat16)
    value_grad = gathered[local_rows:].astype(jnp.bfloat16)
    projection_grad = weight_state[0].reshape(width // dp_size, width)
    table_grad = summed_by_exchange(table_local.reshape(-1), ("dp", "ctx")).reshape(
        table_local.shape
    )
    return (
        query_grad[None],
        key_grad[None],
        value_grad[None],
        gate_grad[None],
        projection_grad,
        table_grad,
    )


def solution(mesh):
    return jax.shard_map(
        shards,
        mesh=mesh,
        in_specs=(
            P("dp", "ctx", None),
            P("dp", "ctx", None),
            P("dp", "ctx", None),
            P("dp", "ctx", None),
            P("dp", "ctx", None),
            P("dp", None),
            P("dp", None),
            P("dp", None, None),
            P(),
            P(),
        ),
        out_specs=(
            P("dp", "ctx", None),
            P("dp", "ctx", None),
            P("dp", "ctx", None),
            P("dp", "ctx", None),
            P("dp", None),
            P(),
        ),
        check_vma=False,
    )
```
